32 devices in a mesh: group: 16 (over z, y, core), shard: 2 (over x).
Axes of the slice: x: 2, y: 2, z: 4, core: 2. Of those that a mesh axis runs over, the one named last changes fastest.
Arguments:
- tokens: bfloat16 [32768, 768], P(('group', 'shard')), may hold values from -6 to 6
- doc_lengths: int32 [32, 5], P(('group', 'shard')), may hold values from 1 to 512, 1024 in all within a row
- first_gain: bfloat16 [768], P(('group', 'shard')), may hold values from 0.099609375 to 1.8984375
- first_shift: bfloat16 [768], P(('group', 'shard')), may hold values from -3 to 3
- qkv_weight: bfloat16 [768, 2304], P(('group', 'shard')), may hold values from -0.21875 to 0.21875
- query_bias: bfloat16 [768], P(('group', 'shard')), may hold values from -3 to 3
- value_bias: bfloat16 [768], P(('group', 'shard')), may hold values from -3 to 3
- inner_gain: bfloat16 [768], P(('group', 'shard')), may hold values from 0.099609375 to 1.8984375
- inner_shift: bfloat16 [768], P(('group', 'shard')), may hold values from -3 to 3
- proj_weight: bfloat16 [768, 768], P(('group', 'shard')), may hold values from -0.21875 to 0.21875
- proj_bias: bfloat16 [768], P(('group', 'shard')), may hold values from -3 to 3
- second_gain: bfloat16 [768], P(('group', 'shard')), may hold values from 0.099609375 to 1.8984375
- second_shift: bfloat16 [768], P(('group', 'shard')), may hold values from -3 to 3
- expand_weight: bfloat16 [768, 3072], P(('group', 'shard')), may hold values from -0.21875 to 0.21875
- expand_bias: bfloat16 [3072], P(('group', 'shard')), may hold values from -3 to 3
- hidden_gain: bfloat16 [3072], P(('group', 'shard')), may hold values from 0.099609375 to 1.8984375
- hidden_shift: bfloat16 [3072], P(('group', 'shard')), may hold values from -3 to 3
- shrink_weight: bfloat16 [3072, 768], P(('group', 'shard')), may hold values from -0.109375 to 0.109375
- shrink_bias: bfloat16 [768], P(('group', 'shard')), may hold values from -3 to 3
- out_cotangent: bfloat16 [32768, 768], P(('group', 'shard')), may hold values from -6 to 6
Outputs:
- block_output: bfloat16 [32768, 768], P(('group', 'shard'))
- input_grad: bfloat16 [32768, 768], P(('group', 'shard'))
- first_gain_grad: float32 [768], P('shard')
- first_shift_grad: float32 [768], P('shard')
- qkv_weight_grad: float32 [768, 2304], P('shard')
- query_bias_grad: float32 [768], P('shard')
- value_bias_grad: float32 [768], P('shard')
- inner_gain_grad: float32 [768], P('shard')
- inner_shift_grad: float32 [768], P('shard')
- proj_weight_grad: float32 [768, 768], P('shard')
- proj_bias_grad: float32 [768], P('shard')
- second_gain_grad: float32 [768], P('shard')
- second_shift_grad: float32 [768], P('shard')
- expand_weight_grad: float32 [768, 3072], P('shard')
- expand_bias_grad: float32 [3072], P('shard')
- hidden_gain_grad: float32 [3072], P('shard')
- hidden_shift_grad: float32 [3072], P('shard')
- shrink_weight_grad: float32 [3072, 768], P('shard')
- shrink_bias_grad: float32 [768], P('shard')
The draws below stay inside these ranges and needn't reach their ends.
Inputs may be any that keep to these rules, and one draw needn't show every extreme that they name: `doc_lengths`: the last entry of each row is the padding at the row's end; one entry of every row is exactly 512; each row sums to 1024.
All inputs are finite; a program needn't handle non-finite values.
Results may differ from the reference program's by a relative error of at most 0.02.
Values may be sent and summed in bfloat16 or wider, within the bound.
No kernel may reach another device: no remote copies, remote signals or barrier semaphores. Data moves between devices by JAX's collectives and lax.ppermute only.
A program may use at most 320 MiB of HBM per device.

```python
import math
import jax
import jax.numpy as jnp
import numpy as np
from jax import lax

D = 768
HEADS = 12
HEAD = 64
FF = 3072
ROW_LEN = 1024
NSEG = 5
ROWS = 32
TOKENS = 32768


def steps_of(key, extent, cuts, least, largest):
    level = 1.0
    for position, shards_of in cuts:
        steps = jax.random.uniform(jax.random.fold_in(jax.random.fold_in(key, 6), position), (shards_of,), jnp.float32, least / len(cuts), largest / len(cuts))
        level = level * jnp.repeat(jnp.exp(steps), extent[position] // shards_of).reshape((-1,) + (1,) * (len(extent) - 1 - position))
    return level


def length_profile(amount, total, most, skew):
    loads = [(1 << 20) // math.isqrt(rank ** skew) + 1 for rank in range(2, amount + 1)]
    rest, given = total - most - (amount - 1), [1] * (amount - 1)
    while rest > 0:
        free = [i for i in range(amount - 1) if given[i] < most]
        pool, left = sum([loads[i] for i in free]), rest
        for i in free:
            addition = min(most - given[i], max(1, left * loads[i] // pool), rest)
            given[i] = given[i] + addition
            rest = rest - addition
    return np.array([most] + given)


def ragged(own_key, amount, total, bound, lean):
    if amount == 2:
        one = jax.random.randint(own_key, (), max(1, total - bound), min(bound, total - 1) + 1)
        return jnp.stack([one, total - one])
    lengths = jnp.asarray(length_profile(amount, total, bound, lean), jnp.int32)
    couples = (amount - 1) // 2
    giver, receiver = lengths[1:1 + 2 * couples:2], lengths[2:2 + 2 * couples:2]
    slack = jnp.minimum(giver - 1, bound - receiver)
    shifted = jax.random.randint(jax.random.fold_in(own_key, 1), (couples,), 0, 1 << 20) % (slack + 1)
    lengths = lengths.at[1:1 + 2 * couples:2].set(giver - shifted).at[2:2 + 2 * couples:2].set(receiver + shifted)
    return lengths[jax.random.permutation(jax.random.fold_in(own_key, 2), amount)]


def gaussian(stream_key, shape, scale, bound, shards=(), kind=jnp.bfloat16):
    entries = scale * jax.random.normal(stream_key, shape, jnp.float32)
    if shards:
        entries = entries * steps_of(stream_key, shape, shards, -0.22, 0.18)
    return jnp.clip(entries, -bound, bound).astype(kind)


def setup_inputs(seed: int = 0) -> dict:
    keys = jax.random.split(jax.random.key(seed), 21)
    tokens = gaussian(keys[0], (TOKENS, D), 1.0, 6.0, ((0, 32),))
    doc_lengths = jax.vmap(lambda own: ragged(own, NSEG, ROW_LEN, ROW_LEN // 2, 2))(jax.random.split(keys[1], ROWS)).reshape((ROWS, NSEG)).astype(jnp.int32)
    first_gain = jnp.clip(1.0 + 0.18 * jax.random.normal(keys[2], (D,), jnp.float32), 0.099609375, 1.8984375).astype(jnp.bfloat16)
    first_shift = gaussian(keys[3], (D,), 0.5, 3.0, ((0, 32),))
    qkv_weight = gaussian(keys[4], (D, 3 * D), D ** -0.5, 0.21875, ((0, 32),))
    query_bias = gaussian(keys[5], (D,), 0.5, 3.0, ((0, 32),))
    value_bias = gaussian(keys[6], (D,), 0.5, 3.0, ((0, 32),))
    inner_gain = jnp.clip(1.0 + 0.18 * jax.random.normal(keys[7], (D,), jnp.float32), 0.099609375, 1.8984375).astype(jnp.bfloat16)
    inner_shift = gaussian(keys[8], (D,), 0.5, 3.0, ((0, 32),))
    proj_weight = gaussian(keys[9], (D, D), D ** -0.5, 0.21875, ((0, 32),))
    proj_bias = gaussian(keys[10], (D,), 0.5, 3.0, ((0, 32),))
    second_gain = jnp.clip(1.0 + 0.18 * jax.random.normal(keys[11], (D,), jnp.float32), 0.099609375, 1.8984375).astype(jnp.bfloat16)
    second_shift = gaussian(keys[12], (D,), 0.5, 3.0, ((0, 32),))
    expand_weight = gaussian(keys[13], (D, FF), D ** -0.5, 0.21875, ((0, 32),))
    expand_bias = gaussian(keys[14], (FF,), 0.5, 3.0, ((0, 32),))
    hidden_gain = jnp.clip(1.0 + 0.18 * jax.random.normal(keys[15], (FF,), jnp.float32), 0.099609375, 1.8984375).astype(jnp.bfloat16)
    hidden_shift = gaussian(keys[16], (FF,), 0.5, 3.0, ((0, 32),))
    shrink_weight = gaussian(keys[17], (FF, D), FF ** -0.5, 0.109375, ((0, 32),))
    shrink_bias = gaussian(keys[18], (D,), 0.5, 3.0, ((0, 32),))
    out_cotangent = gaussian(keys[19], (TOKENS, D), 1.0, 6.0, ((0, 32),))
    return dict(tokens=tokens, doc_lengths=doc_lengths, first_gain=first_gain, first_shift=first_shift, qkv_weight=qkv_weight, query_bias=query_bias, value_bias=value_bias, inner_gain=inner_gain, inner_shift=inner_shift, proj_weight=proj_weight, proj_bias=proj_bias, second_gain=second_gain, second_shift=second_shift, expand_weight=expand_weight, expand_bias=expand_bias, hidden_gain=hidden_gain, hidden_shift=hidden_shift, shrink_weight=shrink_weight, shrink_bias=shrink_bias, out_cotangent=out_cotangent)


@jax.custom_vjp
def low(v):
    return lax.optimization_barrier(v.astype(jnp.bfloat16)).astype(jnp.float32)

@jax.custom_vjp
def low_back(v):
    return v

def low_keep(v):
    return (low(v), None)

def low_pass(kept, grad):
    return (grad,)

def back_keep(v):
    return (v, None)

def back_low(kept, grad):
    return (low(grad),)
low.defvjp(low_keep, low_pass)
low_back.defvjp(back_keep, back_low)
HIGHEST = lax.Precision.HIGHEST
EPSILON = 1e-05
MASKED = -1000000000.0

def matmul(left, right):
    return jnp.dot(left, right, precision=HIGHEST, preferred_element_type=jnp.float32)

def layer_norm(values, gain, shift):
    average = lax.optimization_barrier(jnp.mean(values, axis=-1, keepdims=True))
    centered = values - average
    variance = lax.optimization_barrier(jnp.mean(centered * centered, axis=-1, keepdims=True))
    return centered * lax.rsqrt(variance + EPSILON) * gain + shift

def segment_ids(lengths_row):
    ends = jnp.cumsum(lengths_row).astype(jnp.int32)
    places = jnp.arange(ROW_LEN, dtype=jnp.int32)
    return lax.optimization_barrier(jnp.sum((places[:, None] >= ends[None, :]).astype(jnp.int32), axis=1)).astype(jnp.int32)

def attend_row(qkv_row, segment):
    length = qkv_row.shape[0]
    queries = qkv_row[:, :D].reshape(length, HEADS, HEAD)
    key_heads = qkv_row[:, D:2 * D].reshape(length, HEADS, HEAD)
    value_heads = qkv_row[:, 2 * D:].reshape(length, HEADS, HEAD)
    valid = segment < NSEG - 1
    places = jnp.arange(length, dtype=jnp.int32)
    allowed = (segment[:, None] == segment[None, :]) & (places[:, None] >= places[None, :]) & valid[None, :]
    scores = jnp.einsum('qhd,khd->hqk', queries, key_heads, precision=HIGHEST) * (1.0 / math.sqrt(HEAD))
    scores = low_back(scores)
    scores = jnp.where(allowed[None], scores, MASKED)
    peak = lax.optimization_barrier(jnp.max(scores, axis=-1, keepdims=True))
    expd = jnp.exp(scores - peak)
    probs = expd / lax.optimization_barrier(jnp.sum(expd, axis=-1, keepdims=True)) * valid.astype(jnp.float32)[None, :, None]
    attended = jnp.einsum('hqk,khd->qhd', low(probs), value_heads, precision=HIGHEST)
    return attended.reshape(length, D)

def forward(inputs, first_gain, first_shift, qkv_weight, query_bias, value_bias, inner_gain, inner_shift, proj_weight, proj_bias, second_gain, second_shift, expand_weight, expand_bias, hidden_gain, hidden_shift, shrink_weight, shrink_bias, segments):
    normed = low(layer_norm(inputs, first_gain, first_shift))
    bias_cat = jnp.concatenate([query_bias, jnp.zeros_like(query_bias), value_bias])
    qkv = low_back(low(matmul(normed, qkv_weight) + bias_cat))
    row_attend = jax.checkpoint(attend_row)

    def advance(carried, pieces):
        return (carried, row_attend(pieces[0], pieces[1]))
    _, attended = lax.scan(advance, jnp.zeros((), jnp.float32), (qkv.reshape(ROWS, ROW_LEN, 3 * D), segments))
    attended = low_back(attended.reshape(TOKENS, D))
    inner = low(layer_norm(attended, inner_gain, inner_shift))
    middle = inputs + low_back(matmul(inner, proj_weight) + proj_bias)
    second = low(layer_norm(middle, second_gain, second_shift))
    pre_act = low_back(matmul(second, expand_weight) + expand_bias)
    hidden = low(layer_norm(jax.nn.gelu(pre_act, approximate=False), hidden_gain, hidden_shift))
    return middle + matmul(hidden, shrink_weight) + shrink_bias

def reference(tokens, doc_lengths, first_gain, first_shift, qkv_weight, query_bias, value_bias, inner_gain, inner_shift, proj_weight, proj_bias, second_gain, second_shift, expand_weight, expand_bias, hidden_gain, hidden_shift, shrink_weight, shrink_bias, out_cotangent):
    segments = jax.vmap(segment_ids)(doc_lengths)
    params = (first_gain, first_shift, qkv_weight, query_bias, value_bias, inner_gain, inner_shift, proj_weight, proj_bias, second_gain, second_shift, expand_weight, expand_bias, hidden_gain, hidden_shift, shrink_weight, shrink_bias)
    floats = tuple((item.astype(jnp.float32) for item in params))

    def closure(inputs, *weights):
        return forward(inputs, *weights, segments)
    output, pullback = jax.vjp(closure, tokens.astype(jnp.float32), *floats)
    grads = pullback(out_cotangent.astype(jnp.float32))
    return (output.astype(jnp.bfloat16), grads[0].astype(jnp.bfloat16), grads[1], grads[2], grads[3], grads[4], grads[5], grads[6], grads[7], grads[8], grads[9], grads[10], grads[11], grads[12], grads[13], grads[14], grads[15], grads[16], grads[17])
```

```python
import functools
import math

import jax
import jax.numpy as jnp
from jax import lax
from jax.sharding import PartitionSpec as P


HEADS = 12
HEAD = 64
NSEG = 5


EPSILON = 1e-05

MASKED = -1000000000.0


def norm_apply(values, gain, shift):
    average = jnp.mean(values, axis=-1, keepdims=True)
    centered = values - average
    inv_scale = lax.rsqrt(jnp.mean(centered * centered, axis=-1, keepdims=True) + EPSILON)
    unit = centered * inv_scale
    return (unit * gain + shift, unit, inv_scale)


def norm_back(unit, inv_scale, gain, grad):
    scaled = grad * gain
    back = inv_scale * (
        scaled
        - jnp.mean(scaled, axis=-1, keepdims=True)
        - unit * jnp.mean(scaled * unit, axis=-1, keepdims=True)
    )
    return (back, jnp.sum(grad * unit, axis=0), jnp.sum(grad, axis=0))


def gelu_exact(values):
    return jax.nn.gelu(values, approximate=False)


def segment_ids(lengths_row, length):
    ends = jnp.cumsum(lengths_row)
    places = jnp.arange(length, dtype=jnp.int32)
    return jnp.sum((places[:, None] >= ends[None, :]).astype(jnp.int32), axis=1)


def split_heads(qkv_row):
    length = qkv_row.shape[0]
    width = qkv_row.shape[1] // 3
    queries = qkv_row[:, :width].reshape(length, HEADS, HEAD)
    key_heads = qkv_row[:, width : 2 * width].reshape(length, HEADS, HEAD)
    value_heads = qkv_row[:, 2 * width :].reshape(length, HEADS, HEAD)
    return (queries, key_heads, value_heads)


def masked_scores(query_part, key_heads, segment, valid, offset):
    query_count = query_part.shape[0]
    scores = jnp.einsum(
        "qhd,khd->hqk", query_part, key_heads, preferred_element_type=jnp.float32
    ) * (1.0 / math.sqrt(HEAD))
    places = jnp.arange(segment.shape[0], dtype=jnp.int32)
    query_places = places[offset : offset + query_count]
    query_segment = segment[offset : offset + query_count]
    allowed = (
        (query_segment[:, None] == segment[None, :])
        & (query_places[:, None] >= places[None, :])
        & valid[None, :]
    )
    return jnp.where(allowed[None], scores, MASKED)


def row_forward(pieces):
    qkv_row, segment = pieces
    length = qkv_row.shape[0]
    queries, key_heads, value_heads = split_heads(qkv_row)
    valid = segment < NSEG - 1
    block_rows = min(512, length)
    attended_parts = []
    totals = []
    for offset in range(0, length, block_rows):
        scores = masked_scores(
            queries[offset : offset + block_rows], key_heads, segment, valid, offset
        )
        keep_rows = valid[offset : offset + block_rows].astype(jnp.float32)[None, :, None]
        peak = jnp.max(scores, axis=-1, keepdims=True)
        expd = jnp.exp(scores - peak)
        total = jnp.sum(expd, axis=-1, keepdims=True)
        probs = (expd / total * keep_rows).astype(jnp.bfloat16)
        attended_parts.append(
            jnp.einsum(
                "hqk,khd->qhd", probs, value_heads, preferred_element_type=jnp.float32
            ).reshape(block_rows, HEADS * HEAD)
        )
        totals.append((peak + jnp.log(total))[:, :, 0])
    return (jnp.concatenate(attended_parts, axis=0), jnp.concatenate(totals, axis=1))


def row_backward(pieces):
    qkv_row, segment, log_total, grad_rows = pieces
    length = qkv_row.shape[0]
    queries, key_heads, value_heads = split_heads(qkv_row)
    valid = segment < NSEG - 1
    grad_heads = grad_rows.reshape(length, HEADS, HEAD)
    block_rows = min(512, length)
    scale_factor = 1.0 / math.sqrt(HEAD)
    query_grads = []
    key_grad = jnp.zeros((length, HEADS, HEAD), jnp.float32)
    value_grad = jnp.zeros((length, HEADS, HEAD), jnp.float32)
    for offset in range(0, length, block_rows):
        query_part = queries[offset : offset + block_rows]
        scores = masked_scores(query_part, key_heads, segment, valid, offset)
        keep_rows = valid[offset : offset + block_rows].astype(jnp.float32)[None, :, None]
        probs = jnp.exp(scores - log_total[:, offset : offset + block_rows, None]) * keep_rows
        grad_block = grad_heads[offset : offset + block_rows]
        grad_probs = jnp.einsum(
            "qhd,khd->hqk", grad_block, value_heads, preferred_element_type=jnp.float32
        )
        inner_sum = jnp.sum(probs * grad_probs, axis=-1, keepdims=True)
        grad_scores = (probs * (grad_probs - inner_sum)).astype(jnp.bfloat16)
        query_grads.append(
            jnp.einsum("hqk,khd->qhd", grad_scores, key_heads, preferred_element_type=jnp.float32)
            * scale_factor
        )
        key_grad = (
            key_grad
            + jnp.einsum(
                "hqk,qhd->khd", grad_scores, query_part, preferred_element_type=jnp.float32
            )
            * scale_factor
        )
        value_grad = value_grad + jnp.einsum(
            "hqk,qhd->khd",
            probs.astype(jnp.bfloat16),
            grad_block,
            preferred_element_type=jnp.float32,
        )
    query_grad = jnp.concatenate(query_grads, axis=0)
    return jnp.concatenate(
        [
            query_grad.reshape(length, -1),
            key_grad.reshape(length, -1),
            value_grad.reshape(length, -1),
        ],
        axis=1,
    )


def pack_columns(parts, rows):
    cols = [p.reshape(rows, -1) for p in parts]
    width = sum(c.shape[1] for c in cols)
    pad = (-width) % 128
    if pad:
        cols.append(jnp.zeros((rows, pad), cols[0].dtype))
    return jnp.concatenate(cols, axis=1)


def unpack_columns(block, widths):
    out = []
    offset = 0
    for w in widths:
        out.append(block[:, offset : offset + w].reshape(-1))
        offset += w
    return out


def grad_rows_reduce(packed, group_size, shard_size):
    rows, cols = packed.shape
    n = rows // (group_size * shard_size)
    permuted = (
        packed.reshape(shard_size, group_size, n, cols)
        .transpose(1, 0, 2, 3)
        .reshape(rows, cols)
    )
    return lax.psum_scatter(
        permuted, ("group", "shard"), scatter_dimension=0, tiled=True
    )


def per_device(
    tokens,
    doc_lengths,
    first_gain,
    first_shift,
    qkv_weight,
    query_bias,
    value_bias,
    inner_gain,
    inner_shift,
    proj_weight,
    proj_bias,
    second_gain,
    second_shift,
    expand_weight,
    expand_bias,
    hidden_gain,
    hidden_shift,
    shrink_weight,
    shrink_bias,
    out_cotangent,
):
    group_size = lax.axis_size("group")
    shard_size = lax.axis_size("shard")
    n = qkv_weight.shape[0]
    model_width = n * group_size * shard_size
    wide_width = expand_weight.shape[1]
    ratio = wide_width // model_width
    qkv_width = qkv_weight.shape[1]

    small_parts = (
        first_gain,
        first_shift,
        query_bias,
        value_bias,
        inner_gain,
        inner_shift,
        proj_bias,
        second_gain,
        second_shift,
        shrink_bias,
        expand_bias,
        hidden_gain,
        hidden_shift,
    )
    small_widths = [p.shape[0] // n for p in small_parts]
    first_pack = jnp.concatenate([qkv_weight, pack_columns(small_parts, n)], axis=1)
    first_full = lax.all_gather(first_pack, ("group", "shard"), axis=0, tiled=True)
    qkv_full = first_full[:, :qkv_width]
    (
        gain_one,
        shift_one,
        qbias_full,
        vbias_full,
        gain_inner,
        shift_inner,
        pbias_full,
        gain_three,
        shift_three,
        sbias_full,
        ebias_full,
        gain_four,
        shift_four,
    ) = unpack_columns(first_full[:, qkv_width:], small_widths)
    second_pack = jnp.concatenate(
        [proj_weight, expand_weight, shrink_weight.reshape(n, ratio * model_width)], axis=1
    )
    second_full = lax.all_gather(second_pack, ("group", "shard"), axis=0, tiled=True)
    proj_full = second_full[:, :model_width]
    expand_full = second_full[:, model_width : model_width + wide_width]
    shrink_full = second_full[:, model_width + wide_width :].reshape(wide_width, model_width)

    row_count = doc_lengths.shape[0]
    length = tokens.shape[0] // row_count
    inputs = tokens.astype(jnp.float32)
    normed, unit_one, inv_one = norm_apply(
        inputs, gain_one.astype(jnp.float32), shift_one.astype(jnp.float32)
    )
    normed_low = normed.astype(jnp.bfloat16)
    bias_cat = jnp.concatenate([qbias_full, jnp.zeros_like(qbias_full), vbias_full]).astype(
        jnp.float32
    )
    qkv_low = (jnp.dot(normed_low, qkv_full, preferred_element_type=jnp.float32) + bias_cat).astype(
        jnp.bfloat16
    )
    segments = jax.vmap(functools.partial(segment_ids, length=length))(doc_lengths)
    qkv_rows = qkv_low.reshape(row_count, length, 3 * model_width)
    attended, log_totals = lax.map(row_forward, (qkv_rows, segments))
    attended = attended.reshape(-1, model_width)
    inner, unit_two, inv_two = norm_apply(
        attended, gain_inner.astype(jnp.float32), shift_inner.astype(jnp.float32)
    )
    inner_low = inner.astype(jnp.bfloat16)
    middle = (
        inputs
        + jnp.dot(inner_low, proj_full, preferred_element_type=jnp.float32)
        + pbias_full.astype(jnp.float32)
    )
    second, unit_three, inv_three = norm_apply(
        middle, gain_three.astype(jnp.float32), shift_three.astype(jnp.float32)
    )
    second_low = second.astype(jnp.bfloat16)
    pre_act = jnp.dot(
        second_low, expand_full, preferred_element_type=jnp.float32
    ) + ebias_full.astype(jnp.float32)
    activ, gelu_pull = jax.vjp(gelu_exact, pre_act)
    hidden, unit_four, inv_four = norm_apply(
        activ, gain_four.astype(jnp.float32), shift_four.astype(jnp.float32)
    )
    hidden_low = hidden.astype(jnp.bfloat16)
    output = (
        middle
        + jnp.dot(hidden_low, shrink_full, preferred_element_type=jnp.float32)
        + sbias_full.astype(jnp.float32)
    )
    block_output = output.astype(jnp.bfloat16)
    grad_out = out_cotangent.astype(jnp.float32)
    shrink_weight_grad = jnp.einsum(
        "tf,td->fd", hidden_low, out_cotangent, preferred_element_type=jnp.float32
    )
    shrink_bias_grad = jnp.sum(grad_out, axis=0)
    grad_hidden = jnp.einsum(
        "td,fd->tf", out_cotangent, shrink_full, preferred_element_type=jnp.float32
    )
    grad_activ, hidden_gain_grad, hidden_shift_grad = norm_back(
        unit_four, inv_four, gain_four.astype(jnp.float32), grad_hidden
    )
    grad_pre = gelu_pull(grad_activ)[0].astype(jnp.bfloat16)
    expand_bias_grad = jnp.sum(grad_pre.astype(jnp.float32), axis=0)
    expand_weight_grad = jnp.einsum(
        "td,tf->df", second_low, grad_pre, preferred_element_type=jnp.float32
    )
    grad_second = jnp.einsum("tf,df->td", grad_pre, expand_full, preferred_element_type=jnp.float32)
    grad_mid_part, second_gain_grad, second_shift_grad = norm_back(
        unit_three, inv_three, gain_three.astype(jnp.float32), grad_second
    )
    grad_middle = grad_out + grad_mid_part
    ffn_small = (
        second_gain_grad,
        second_shift_grad,
        shrink_bias_grad,
        expand_bias_grad,
        hidden_gain_grad,
        hidden_shift_grad,
    )
    ffn_small_widths = [p.shape[0] // model_width for p in ffn_small]
    ffn_pack = jnp.concatenate(
        [
            expand_weight_grad,
            shrink_weight_grad.reshape(model_width, ratio * model_width),
            pack_columns(ffn_small, model_width),
        ],
        axis=1,
    ).astype(jnp.bfloat16)
    ffn_part = grad_rows_reduce(ffn_pack, group_size, shard_size)

    grad_branch = grad_middle.astype(jnp.bfloat16)
    proj_bias_grad = jnp.sum(grad_branch.astype(jnp.float32), axis=0)
    proj_weight_grad = jnp.einsum(
        "td,te->de", inner_low, grad_branch, preferred_element_type=jnp.float32
    )
    grad_inner = jnp.einsum("te,de->td", grad_branch, proj_full, preferred_element_type=jnp.float32)
    grad_attended, inner_gain_grad, inner_shift_grad = norm_back(
        unit_two, inv_two, gain_inner.astype(jnp.float32), grad_inner
    )
    grad_att_low = grad_attended.astype(jnp.bfloat16).reshape(row_count, length, model_width)
    grad_qkv = (
        lax.map(row_backward, (qkv_rows, segments, log_totals, grad_att_low))
        .reshape(-1, 3 * model_width)
        .astype(jnp.bfloat16)
    )
    grad_qkv_wide = grad_qkv.astype(jnp.float32)
    query_bias_grad = jnp.sum(grad_qkv_wide[:, :model_width], axis=0)
    value_bias_grad = jnp.sum(grad_qkv_wide[:, 2 * model_width :], axis=0)
    qkv_weight_grad = jnp.einsum(
        "td,te->de", normed_low, grad_qkv, preferred_element_type=jnp.float32
    )
    grad_normed = jnp.einsum("te,de->td", grad_qkv, qkv_full, preferred_element_type=jnp.float32)
    grad_in_part, first_gain_grad, first_shift_grad = norm_back(
        unit_one, inv_one, gain_one.astype(jnp.float32), grad_normed
    )
    input_grad = (grad_middle + grad_in_part).astype(jnp.bfloat16)
    attn_small = (
        first_gain_grad,
        first_shift_grad,
        query_bias_grad,
        value_bias_grad,
        inner_gain_grad,
        inner_shift_grad,
        proj_bias_grad,
    )
    attn_pack = jnp.concatenate(
        [qkv_weight_grad, proj_weight_grad, pack_columns(attn_small, model_width)], axis=1
    ).astype(jnp.bfloat16)
    ffn_part, attn_pack = lax.optimization_barrier((ffn_part, attn_pack))
    attn_part = grad_rows_reduce(attn_pack, group_size, shard_size)
    both = lax.all_gather(
        jnp.concatenate([ffn_part, attn_part], axis=1), "group", axis=0, tiled=True
    ).astype(jnp.float32)
    ffn_cols = ffn_pack.shape[1]
    ffn_back = both[:, :ffn_cols]
    attn_back = both[:, ffn_cols:]
    half = both.shape[0]
    expand_out = ffn_back[:, :wide_width]
    shrink_out = ffn_back[:, wide_width : 2 * wide_width].reshape(half * ratio, model_width)
    (
        second_gain_out,
        second_shift_out,
        sbias_out,
        ebias_out,
        gain_four_out,
        shift_four_out,
    ) = unpack_columns(ffn_back[:, 2 * wide_width :], ffn_small_widths)
    qkv_out = attn_back[:, :qkv_width]
    proj_out = attn_back[:, qkv_width : qkv_width + model_width]
    (
        gain_one_out,
        shift_one_out,
        qbias_out,
        vbias_out,
        gain_inner_out,
        shift_inner_out,
        pbias_out,
    ) = unpack_columns(attn_back[:, qkv_width + model_width :], [1] * 7)
    return (
        block_output,
        input_grad,
        gain_one_out,
        shift_one_out,
        qkv_out,
        qbias_out,
        vbias_out,
        gain_inner_out,
        shift_inner_out,
        proj_out,
        pbias_out,
        second_gain_out,
        second_shift_out,
        expand_out,
        ebias_out,
        gain_four_out,
        shift_four_out,
        shrink_out,
        sbias_out,
    )


def solution(mesh):
    in_specs = (
        P(("group", "shard"), None),
        P(("group", "shard"), None),
        P(("group", "shard")),
        P(("group", "shard")),
        P(("group", "shard"), None),
        P(("group", "shard")),
        P(("group", "shard")),
        P(("group", "shard")),
        P(("group", "shard")),
        P(("group", "shard"), None),
        P(("group", "shard")),
        P(("group", "shard")),
        P(("group", "shard")),
        P(("group", "shard"), None),
        P(("group", "shard")),
        P(("group", "shard")),
        P(("group", "shard")),
        P(("group", "shard"), None),
        P(("group", "shard")),
        P(("group", "shard"), None),
    )
    out_specs = (
        P(("group", "shard"), None),
        P(("group", "shard"), None),
        P("shard"),
        P("shard"),
        P("shard", None),
        P("shard"),
        P("shard"),
        P("shard"),
        P("shard"),
        P("shard", None),
        P("shard"),
        P("shard"),
        P("shard"),
        P("shard", None),
        P("shard"),
        P("shard"),
        P("shard"),
        P("shard", None),
        P("shard"),
    )

    return jax.shard_map(
        per_device, mesh=mesh, in_specs=in_specs, out_specs=out_specs, check_vma=False
    )
```

```python
import functools
import math

import jax
import jax.numpy as jnp
from jax import lax
from jax.sharding import PartitionSpec as P


HEADS = 12
HEAD = 64
NSEG = 5


EPSILON = 1e-05


MASKED = -1000000000.0


def norm_apply(values, gain, shift):
    average = jnp.mean(values, axis=-1, keepdims=True)
    centered = values - average
    inv_scale = lax.rsqrt(jnp.mean(centered * centered, axis=-1, keepdims=True) + EPSILON)
    unit = centered * inv_scale
    return (unit * gain + shift, unit, inv_scale)


def norm_back(unit, inv_scale, gain, grad):
    scaled = grad * gain
    back = inv_scale * (
        scaled
        - jnp.mean(scaled, axis=-1, keepdims=True)
        - unit * jnp.mean(scaled * unit, axis=-1, keepdims=True)
    )
    return (back, jnp.sum(grad * unit, axis=0), jnp.sum(grad, axis=0))


def gelu_exact(values):
    return jax.nn.gelu(values, approximate=False)


def segment_ids(lengths_row, length):
    ends = jnp.cumsum(lengths_row)
    places = jnp.arange(length, dtype=jnp.int32)
    return jnp.sum((places[:, None] >= ends[None, :]).astype(jnp.int32), axis=1)


def split_heads(qkv_row):
    length = qkv_row.shape[0]
    width = qkv_row.shape[1] // 3
    queries = qkv_row[:, :width].reshape(length, HEADS, HEAD)
    key_heads = qkv_row[:, width : 2 * width].reshape(length, HEADS, HEAD)
    value_heads = qkv_row[:, 2 * width :].reshape(length, HEADS, HEAD)
    return (queries, key_heads, value_heads)


def masked_scores(query_part, key_heads, segment, valid, offset):
    query_count = query_part.shape[0]
    scores = jnp.einsum(
        "qhd,khd->hqk", query_part, key_heads, preferred_element_type=jnp.float32
    ) * (1.0 / math.sqrt(HEAD))
    places = jnp.arange(segment.shape[0], dtype=jnp.int32)
    query_places = places[offset : offset + query_count]
    query_segment = segment[offset : offset + query_count]
    allowed = (
        (query_segment[:, None] == segment[None, :])
        & (query_places[:, None] >= places[None, :])
        & valid[None, :]
    )
    return jnp.where(allowed[None], scores, MASKED)


def row_forward(pieces):
    qkv_row, segment = pieces
    length = qkv_row.shape[0]
    queries, key_heads, value_heads = split_heads(qkv_row)
    valid = segment < NSEG - 1
    block_rows = min(512, length)
    attended_parts = []
    totals = []
    for offset in range(0, length, block_rows):
        scores = masked_scores(
            queries[offset : offset + block_rows], key_heads, segment, valid, offset
        )
        keep_rows = valid[offset : offset + block_rows].astype(jnp.float32)[None, :, None]
        peak = jnp.max(scores, axis=-1, keepdims=True)
        expd = jnp.exp(scores - peak)
        total = jnp.sum(expd, axis=-1, keepdims=True)
        probs = (expd / total * keep_rows).astype(jnp.bfloat16)
        attended_parts.append(
            jnp.einsum(
                "hqk,khd->qhd", probs, value_heads, preferred_element_type=jnp.float32
            ).reshape(block_rows, HEADS * HEAD)
        )
        totals.append((peak + jnp.log(total))[:, :, 0])
    return (jnp.concatenate(attended_parts, axis=0), jnp.concatenate(totals, axis=1))


def row_backward(pieces):
    qkv_row, segment, log_total, grad_rows = pieces
    length = qkv_row.shape[0]
    queries, key_heads, value_heads = split_heads(qkv_row)
    valid = segment < NSEG - 1
    grad_heads = grad_rows.reshape(length, HEADS, HEAD)
    block_rows = min(512, length)
    scale_factor = 1.0 / math.sqrt(HEAD)
    query_grads = []
    key_grad = jnp.zeros((length, HEADS, HEAD), jnp.float32)
    value_grad = jnp.zeros((length, HEADS, HEAD), jnp.float32)
    for offset in range(0, length, block_rows):
        query_part = queries[offset : offset + block_rows]
        scores = masked_scores(query_part, key_heads, segment, valid, offset)
        keep_rows = valid[offset : offset + block_rows].astype(jnp.float32)[None, :, None]
        probs = jnp.exp(scores - log_total[:, offset : offset + block_rows, None]) * keep_rows
        grad_block = grad_heads[offset : offset + block_rows]
        grad_probs = jnp.einsum(
            "qhd,khd->hqk", grad_block, value_heads, preferred_element_type=jnp.float32
        )
        inner_sum = jnp.sum(probs * grad_probs, axis=-1, keepdims=True)
        grad_scores = (probs * (grad_probs - inner_sum)).astype(jnp.bfloat16)
        query_grads.append(
            jnp.einsum("hqk,khd->qhd", grad_scores, key_heads, preferred_element_type=jnp.float32)
            * scale_factor
        )
        key_grad = (
            key_grad
            + jnp.einsum(
                "hqk,qhd->khd", grad_scores, query_part, preferred_element_type=jnp.float32
            )
            * scale_factor
        )
        value_grad = value_grad + jnp.einsum(
            "hqk,qhd->khd",
            probs.astype(jnp.bfloat16),
            grad_block,
            preferred_element_type=jnp.float32,
        )
    query_grad = jnp.concatenate(query_grads, axis=0)
    return jnp.concatenate(
        [
            query_grad.reshape(length, -1),
            key_grad.reshape(length, -1),
            value_grad.reshape(length, -1),
        ],
        axis=1,
    )


def pack_columns(parts, rows):
    cols = [p.reshape(rows, -1) for p in parts]
    width = sum(c.shape[1] for c in cols)
    pad = (-width) % 128
    if pad:
        cols.append(jnp.zeros((rows, pad), cols[0].dtype))
    return jnp.concatenate(cols, axis=1)


def unpack_columns(block, widths):
    out = []
    offset = 0
    for w in widths:
        out.append(block[:, offset : offset + w].reshape(-1))
        offset += w
    return out


def grad_rows_reduce(packed, group_size, shard_size):
    rows, cols = packed.shape
    n = rows // (group_size * shard_size)
    permuted = (
        packed.reshape(shard_size, group_size, n, cols)
        .transpose(1, 0, 2, 3)
        .reshape(rows, cols)
    )
    return lax.psum_scatter(
        permuted, ("group", "shard"), scatter_dimension=0, tiled=True
    )


def hypercube_orders(group_size, shard_size):
    gbits = [("group", b) for b in range(group_size.bit_length() - 1)]
    sbits = [("shard", b) for b in range(shard_size.bit_length() - 1)]
    first = gbits[:-1] + sbits + gbits[-1:]
    second = list(first)
    if len(gbits) >= 3:
        second[1], second[2] = first[2], first[1]
    return first, second


def hypercube_reduce_scatter(x, order, group_size, shard_size):
    total = group_size * shard_size
    levels = total.bit_length() - 1
    rows, cols = x.shape
    n = rows // total
    sbits = shard_size.bit_length() - 1

    def k_bit(axis, b):
        return b if axis == "shard" else sbits + b

    axes = [levels - 1 - k_bit(axis, b) for axis, b in order]
    cur = (
        x.reshape([2] * levels + [n, cols])
        .transpose(axes + [levels, levels + 1])
        .reshape(rows, cols)
    )
    for axis, b in order:
        size = group_size if axis == "group" else shard_size
        half = cur.shape[0] // 2
        mine = (lax.axis_index(axis) >> b) & 1
        low, high = cur[:half], cur[half:]
        keep = jnp.where(mine == 1, high, low)
        send = jnp.where(mine == 1, low, high).astype(jnp.bfloat16)
        got = lax.ppermute(send, axis, [(j, j ^ (1 << b)) for j in range(size)])
        cur = keep + got.astype(jnp.float32)
    return cur


def per_device(
    tokens,
    doc_lengths,
    first_gain,
    first_shift,
    qkv_weight,
    query_bias,
    value_bias,
    inner_gain,
    inner_shift,
    proj_weight,
    proj_bias,
    second_gain,
    second_shift,
    expand_weight,
    expand_bias,
    hidden_gain,
    hidden_shift,
    shrink_weight,
    shrink_bias,
    out_cotangent,
):
    group_size = lax.axis_size("group")
    shard_size = lax.axis_size("shard")
    n = qkv_weight.shape[0]
    model_width = n * group_size * shard_size
    wide_width = expand_weight.shape[1]
    ratio = wide_width // model_width
    qkv_width = qkv_weight.shape[1]

    small_parts = (
        first_gain,
        first_shift,
        query_bias,
        value_bias,
        inner_gain,
        inner_shift,
        proj_bias,
        second_gain,
        second_shift,
        shrink_bias,
        expand_bias,
        hidden_gain,
        hidden_shift,
    )
    small_widths = [p.shape[0] // n for p in small_parts]
    first_pack = jnp.concatenate([qkv_weight, pack_columns(small_parts, n)], axis=1)
    first_full = lax.all_gather(first_pack, ("group", "shard"), axis=0, tiled=True)
    qkv_full = first_full[:, :qkv_width]
    (
        gain_one,
        shift_one,
        qbias_full,
        vbias_full,
        gain_inner,
        shift_inner,
        pbias_full,
        gain_three,
        shift_three,
        sbias_full,
        ebias_full,
        gain_four,
        shift_four,
    ) = unpack_columns(first_full[:, qkv_width:], small_widths)
    second_pack = jnp.concatenate([proj_weight, expand_weight], axis=1)
    second_full = lax.all_gather(second_pack, ("group", "shard"), axis=0, tiled=True)
    proj_full = second_full[:, :model_width]
    expand_full = second_full[:, model_width:]
    shrink_full = lax.all_gather(shrink_weight, ("group", "shard"), axis=0, tiled=True)

    row_count = doc_lengths.shape[0]
    length = tokens.shape[0] // row_count
    inputs = tokens.astype(jnp.float32)
    normed, unit_one, inv_one = norm_apply(
        inputs, gain_one.astype(jnp.float32), shift_one.astype(jnp.float32)
    )
    normed_low = normed.astype(jnp.bfloat16)
    bias_cat = jnp.concatenate([qbias_full, jnp.zeros_like(qbias_full), vbias_full]).astype(
        jnp.float32
    )
    qkv_low = (jnp.dot(normed_low, qkv_full, preferred_element_type=jnp.float32) + bias_cat).astype(
        jnp.bfloat16
    )
    segments = jax.vmap(functools.partial(segment_ids, length=length))(doc_lengths)
    qkv_rows = qkv_low.reshape(row_count, length, 3 * model_width)
    attended, log_totals = lax.map(row_forward, (qkv_rows, segments))
    attended = attended.reshape(-1, model_width)
    inner, unit_two, inv_two = norm_apply(
        attended, gain_inner.astype(jnp.float32), shift_inner.astype(jnp.float32)
    )
    inner_low = inner.astype(jnp.bfloat16)
    middle = (
        inputs
        + jnp.dot(inner_low, proj_full, preferred_element_type=jnp.float32)
        + pbias_full.astype(jnp.float32)
    )
    second, unit_three, inv_three = norm_apply(
        middle, gain_three.astype(jnp.float32), shift_three.astype(jnp.float32)
    )
    second_low = second.astype(jnp.bfloat16)
    pre_act = jnp.dot(
        second_low, expand_full, preferred_element_type=jnp.float32
    ) + ebias_full.astype(jnp.float32)
    activ, gelu_pull = jax.vjp(gelu_exact, pre_act)
    hidden, unit_four, inv_four = norm_apply(
        activ, gain_four.astype(jnp.float32), shift_four.astype(jnp.float32)
    )
    hidden_low = hidden.astype(jnp.bfloat16)
    output = (
        middle
        + jnp.dot(hidden_low, shrink_full, preferred_element_type=jnp.float32)
        + sbias_full.astype(jnp.float32)
    )
    block_output = output.astype(jnp.bfloat16)
    grad_out = out_cotangent.astype(jnp.float32)
    shrink_weight_grad = jnp.einsum(
        "tf,td->fd", hidden_low, out_cotangent, preferred_element_type=jnp.float32
    )
    shrink_bias_grad = jnp.sum(grad_out, axis=0)
    grad_hidden = jnp.einsum(
        "td,fd->tf", out_cotangent, shrink_full, preferred_element_type=jnp.float32
    )
    grad_activ, hidden_gain_grad, hidden_shift_grad = norm_back(
        unit_four, inv_four, gain_four.astype(jnp.float32), grad_hidden
    )
    grad_pre = gelu_pull(grad_activ)[0].astype(jnp.bfloat16)
    expand_bias_grad = jnp.sum(grad_pre.astype(jnp.float32), axis=0)
    expand_weight_grad = jnp.einsum(
        "td,tf->df", second_low, grad_pre, preferred_element_type=jnp.float32
    )
    grad_second = jnp.einsum("tf,df->td", grad_pre, expand_full, preferred_element_type=jnp.float32)
    grad_mid_part, second_gain_grad, second_shift_grad = norm_back(
        unit_three, inv_three, gain_three.astype(jnp.float32), grad_second
    )
    grad_middle = grad_out + grad_mid_part
    order_a, order_b = hypercube_orders(group_size, shard_size)
    shrink_in = (
        shrink_weight_grad.reshape(shard_size, group_size, -1, model_width)
        .transpose(1, 0, 2, 3)
        .reshape(wide_width, model_width)
    )
    grad_branch = grad_middle.astype(jnp.bfloat16)
    proj_bias_grad = jnp.sum(grad_branch.astype(jnp.float32), axis=0)
    proj_weight_grad = jnp.einsum(
        "td,te->de", inner_low, grad_branch, preferred_element_type=jnp.float32
    )
    grad_inner = jnp.einsum("te,de->td", grad_branch, proj_full, preferred_element_type=jnp.float32)
    grad_attended, inner_gain_grad, inner_shift_grad = norm_back(
        unit_two, inv_two, gain_inner.astype(jnp.float32), grad_inner
    )
    ffn_small = (
        second_gain_grad,
        second_shift_grad,
        shrink_bias_grad,
        expand_bias_grad,
        hidden_gain_grad,
        hidden_shift_grad,
        inner_gain_grad,
        inner_shift_grad,
        proj_bias_grad,
    )
    ffn_small_widths = [p.shape[0] // model_width for p in ffn_small]
    ffn_pack = jnp.concatenate(
        [
            expand_weight_grad,
            proj_weight_grad,
            pack_columns(ffn_small, model_width),
        ],
        axis=1,
    ).astype(jnp.bfloat16)
    grad_att_low = grad_attended.astype(jnp.bfloat16).reshape(row_count, length, model_width)
    ffn_pack, shrink_in, grad_att_low = lax.optimization_barrier(
        (ffn_pack, shrink_in, grad_att_low)
    )
    ffn_part = grad_rows_reduce(ffn_pack, group_size, shard_size)
    shrink_part = hypercube_reduce_scatter(shrink_in, order_a, group_size, shard_size)
    grad_qkv = (
        lax.map(row_backward, (qkv_rows, segments, log_totals, grad_att_low))
        .reshape(-1, 3 * model_width)
        .astype(jnp.bfloat16)
    )
    grad_qkv_wide = grad_qkv.astype(jnp.float32)
    query_bias_grad = jnp.sum(grad_qkv_wide[:, :model_width], axis=0)
    value_bias_grad = jnp.sum(grad_qkv_wide[:, 2 * model_width :], axis=0)
    qkv_weight_grad = jnp.einsum(
        "td,te->de", normed_low, grad_qkv, preferred_element_type=jnp.float32
    )
    grad_normed = jnp.einsum("te,de->td", grad_qkv, qkv_full, preferred_element_type=jnp.float32)
    grad_in_part, first_gain_grad, first_shift_grad = norm_back(
        unit_one, inv_one, gain_one.astype(jnp.float32), grad_normed
    )
    input_grad = (grad_middle + grad_in_part).astype(jnp.bfloat16)
    attn_small = (
        first_gain_grad,
        first_shift_grad,
        query_bias_grad,
        value_bias_grad,
    )
    attn_pack = jnp.concatenate(
        [qkv_weight_grad, pack_columns(attn_small, model_width)], axis=1
    )
    attn_pack = (
        attn_pack.reshape(shard_size, group_size, n, -1)
        .transpose(1, 0, 2, 3)
        .reshape(model_width, -1)
    )
    ffn_part, shrink_part, attn_pack = lax.optimization_barrier(
        (ffn_part, shrink_part, attn_pack)
    )
    split = (attn_pack.shape[1] // 256) * 128
    attn_left = hypercube_reduce_scatter(
        attn_pack[:, :split], order_a, group_size, shard_size
    )
    attn_right = hypercube_reduce_scatter(
        attn_pack[:, split:], order_b, group_size, shard_size
    )
    both = lax.all_gather(
        jnp.concatenate(
            [
                ffn_part,
                shrink_part.astype(jnp.bfloat16).reshape(n, ratio * model_width),
                attn_left.astype(jnp.bfloat16),
                attn_right.astype(jnp.bfloat16),
            ],
            axis=1,
        ),
        "group",
        axis=0,
        tiled=True,
    ).astype(jnp.float32)
    ffn_cols = ffn_pack.shape[1]
    ffn_back = both[:, :ffn_cols]
    shrink_back = both[:, ffn_cols : ffn_cols + ratio * model_width]
    attn_back = both[:, ffn_cols + ratio * model_width :]
    half = both.shape[0]
    expand_out = ffn_back[:, :wide_width]
    proj_out = ffn_back[:, wide_width : wide_width + model_width]
    shrink_out = shrink_back.reshape(half * ratio, model_width)
    (
        second_gain_out,
        second_shift_out,
        sbias_out,
        ebias_out,
        gain_four_out,
        shift_four_out,
        gain_inner_out,
        shift_inner_out,
        pbias_out,
    ) = unpack_columns(ffn_back[:, wide_width + model_width :], ffn_small_widths)
    qkv_out = attn_back[:, :qkv_width]
    (
        gain_one_out,
        shift_one_out,
        qbias_out,
        vbias_out,
    ) = unpack_columns(attn_back[:, qkv_width:], [1] * 4)
    return (
        block_output,
        input_grad,
        gain_one_out,
        shift_one_out,
        qkv_out,
        qbias_out,
        vbias_out,
        gain_inner_out,
        shift_inner_out,
        proj_out,
        pbias_out,
        second_gain_out,
        second_shift_out,
        expand_out,
        ebias_out,
        gain_four_out,
        shift_four_out,
        shrink_out,
        sbias_out,
    )


def solution(mesh):
    in_specs = (
        P(("group", "shard"), None),
        P(("group", "shard"), None),
        P(("group", "shard")),
        P(("group", "shard")),
        P(("group", "shard"), None),
        P(("group", "shard")),
        P(("group", "shard")),
        P(("group", "shard")),
        P(("group", "shard")),
        P(("group", "shard"), None),
        P(("group", "shard")),
        P(("group", "shard")),
        P(("group", "shard")),
        P(("group", "shard"), None),
        P(("group", "shard")),
        P(("group", "shard")),
        P(("group", "shard")),
        P(("group", "shard"), None),
        P(("group", "shard")),
        P(("group", "shard"), None),
    )
    out_specs = (
        P(("group", "shard"), None),
        P(("group", "shard"), None),
        P("shard"),
        P("shard"),
        P("shard", None),
        P("shard"),
        P("shard"),
        P("shard"),
        P("shard"),
        P("shard", None),
        P("shard"),
        P("shard"),
        P("shard"),
        P("shard", None),
        P("shard"),
        P("shard"),
        P("shard"),
        P("shard", None),
        P("shard"),
    )

    return jax.shard_map(
        per_device, mesh=mesh, in_specs=in_specs, out_specs=out_specs, check_vma=False
    )
```

```python
import functools

import jax
import jax.numpy as jnp
from jax import lax
from jax.experimental import pallas as pl
from jax.experimental.pallas import tpu as pltpu
from jax.sharding import PartitionSpec as P


HEADS = 12
HEAD = 64
NSEG = 5


EPSILON = 1e-05


MASKED = -1000000000.0

CHUNK = 128
QBLOCK = 256


def _scores(q, k_ref, segq, posq, segk_ref, c, scale):
    kc = k_ref[0, pl.ds(c * CHUNK, CHUNK), :]
    s = lax.dot_general(q, kc, (((1,), (1,)), ((), ())), preferred_element_type=jnp.float32) * scale
    segk = segk_ref[:, pl.ds(c * CHUNK, CHUNK)]
    posk = c * CHUNK + lax.broadcasted_iota(jnp.int32, (1, CHUNK), 1)
    allowed = (segq == segk) & (posq >= posk) & (segk < NSEG - 1)
    return jnp.where(allowed, s, MASKED)


def _softmax_rows(q, k_ref, segq, posq, segk_ref, lo, hi, s_ref, scale):
    tq = q.shape[0]

    def first(c, m):
        s = _scores(q, k_ref, segq, posq, segk_ref, c, scale)
        s_ref[:, pl.ds(c * CHUNK, CHUNK)] = s
        return jnp.maximum(m, jnp.max(s, axis=1, keepdims=True))

    m = lax.fori_loop(lo, hi, first, jnp.full((tq, 1), -jnp.inf, jnp.float32))

    def second(c, l):
        e = jnp.exp(s_ref[:, pl.ds(c * CHUNK, CHUNK)] - m)
        s_ref[:, pl.ds(c * CHUNK, CHUNK)] = e
        return l + jnp.sum(e, axis=1, keepdims=True)

    return lax.fori_loop(lo, hi, second, jnp.zeros((tq, 1), jnp.float32))


def _fwd_kernel(lo_ref, q_ref, k_ref, v_ref, segq_ref, segk_ref, o_ref, s_ref):
    i = pl.program_id(1)
    tq = q_ref.shape[1]
    q = q_ref[0]
    segq = segq_ref[...]
    posq = i * tq + lax.broadcasted_iota(jnp.int32, (tq, 1), 0)
    keep = (segq < NSEG - 1).astype(jnp.float32)
    lo = lo_ref[i]
    hi = (i + 1) * (tq // CHUNK)
    total = _softmax_rows(q, k_ref, segq, posq, segk_ref, lo, hi, s_ref, 0.125)

    def third(c, acc):
        p = (s_ref[:, pl.ds(c * CHUNK, CHUNK)] / total * keep).astype(jnp.bfloat16)
        vc = v_ref[0, pl.ds(c * CHUNK, CHUNK), :]
        return acc + jnp.dot(p, vc, preferred_element_type=jnp.float32)

    o_ref[0] = lax.fori_loop(lo, hi, third, jnp.zeros((tq, q.shape[1]), jnp.float32))


def _bwd_kernel(lo_ref, q_ref, k_ref, v_ref, do_ref, segq_ref, segk_ref, dq_ref, dk_ref, dv_ref, s_ref, dp_ref):
    i = pl.program_id(1)
    tq = q_ref.shape[1]

    @pl.when(i == 0)
    def _():
        dk_ref[...] = jnp.zeros_like(dk_ref)
        dv_ref[...] = jnp.zeros_like(dv_ref)

    q = q_ref[0]
    do = do_ref[0]
    segq = segq_ref[...]
    posq = i * tq + lax.broadcasted_iota(jnp.int32, (tq, 1), 0)
    keep = (segq < NSEG - 1).astype(jnp.float32)
    lo = lo_ref[i]
    hi = (i + 1) * (tq // CHUNK)
    total = _softmax_rows(q, k_ref, segq, posq, segk_ref, lo, hi, s_ref, 0.125)

    def third(c, inner):
        p = s_ref[:, pl.ds(c * CHUNK, CHUNK)] / total * keep
        vc = v_ref[0, pl.ds(c * CHUNK, CHUNK), :]
        dp = lax.dot_general(do, vc, (((1,), (1,)), ((), ())), preferred_element_type=jnp.float32)
        s_ref[:, pl.ds(c * CHUNK, CHUNK)] = p
        dp_ref[:, pl.ds(c * CHUNK, CHUNK)] = dp
        return inner + jnp.sum(p * dp, axis=1, keepdims=True)

    inner = lax.fori_loop(lo, hi, third, jnp.zeros((tq, 1), jnp.float32))

    def fourth(c, dq):
        p = s_ref[:, pl.ds(c * CHUNK, CHUNK)]
        ds = (p * (dp_ref[:, pl.ds(c * CHUNK, CHUNK)] - inner)).astype(jnp.bfloat16)
        kc = k_ref[0, pl.ds(c * CHUNK, CHUNK), :]
        rows = pl.ds(c * CHUNK, CHUNK)
        dk_ref[0, rows, :] += lax.dot_general(ds, q, (((0,), (0,)), ((), ())), preferred_element_type=jnp.float32) * 0.125
        dv_ref[0, rows, :] += lax.dot_general(p.astype(jnp.bfloat16), do, (((0,), (0,)), ((), ())), preferred_element_type=jnp.float32)
        return dq + jnp.dot(ds, kc, preferred_element_type=jnp.float32)

    dq = lax.fori_loop(lo, hi, fourth, jnp.zeros((tq, q.shape[1]), jnp.float32))
    dq_ref[0] = dq * 0.125


def _specs(length, head, tq):
    qspec = pl.BlockSpec((1, tq, head), lambda h, i, lo: (h, i, 0))
    kspec = pl.BlockSpec((1, length, head), lambda h, i, lo: (h, 0, 0))
    segq = pl.BlockSpec((tq, 1), lambda h, i, lo: (i, 0))
    segk = pl.BlockSpec((1, length), lambda h, i, lo: (0, 0))
    return qspec, kspec, segq, segk


def attention_forward(q, k, v, seg, lo):
    heads, length, head = q.shape
    tq = min(QBLOCK, length)
    qspec, kspec, segq, segk = _specs(length, head, tq)
    return pl.pallas_call(
        _fwd_kernel,
        out_shape=jax.ShapeDtypeStruct((heads, length, head), jnp.float32),
        grid_spec=pltpu.PrefetchScalarGridSpec(
            num_scalar_prefetch=1,
            grid=(heads, length // tq),
            in_specs=[qspec, kspec, kspec, segq, segk],
            out_specs=qspec,
            scratch_shapes=[pltpu.VMEM((tq, length), jnp.float32)],
        ),
        compiler_params=pltpu.CompilerParams(dimension_semantics=("arbitrary", "arbitrary")),
        cost_estimate=pl.CostEstimate(
            flops=2 * heads * length * length * head,
            transcendentals=heads * length * length // 2,
            bytes_accessed=4 * heads * length * head * 2,
        ),
    )(lo, q, k, v, seg[:, None], seg[None, :])


def attention_backward(q, k, v, do, seg, lo):
    heads, length, head = q.shape
    tq = min(QBLOCK, length)
    qspec, kspec, segq, segk = _specs(length, head, tq)
    out = jax.ShapeDtypeStruct((heads, length, head), jnp.float32)
    return pl.pallas_call(
        _bwd_kernel,
        out_shape=(out, out, out),
        grid_spec=pltpu.PrefetchScalarGridSpec(
            num_scalar_prefetch=1,
            grid=(heads, length // tq),
            in_specs=[qspec, kspec, kspec, qspec, segq, segk],
            out_specs=(qspec, kspec, kspec),
            scratch_shapes=[pltpu.VMEM((tq, length), jnp.float32), pltpu.VMEM((tq, length), jnp.float32)],
        ),
        compiler_params=pltpu.CompilerParams(dimension_semantics=("arbitrary", "arbitrary")),
        cost_estimate=pl.CostEstimate(
            flops=5 * heads * length * length * head,
            transcendentals=heads * length * length // 2,
            bytes_accessed=8 * heads * length * head * 2,
        ),
    )(lo, q, k, v, do, seg[:, None], seg[None, :])


def block_starts(seg, lengths, tq):
    ends = jnp.cumsum(lengths)
    starts = jnp.concatenate([jnp.zeros((1,), ends.dtype), ends[:-1]])
    first_seg = seg[::tq]
    return (starts[first_seg] // CHUNK).astype(jnp.int32)


def heads_major(block):
    return block.reshape(block.shape[0], HEADS, HEAD).transpose(1, 0, 2)


def tokens_major(block):
    return block.transpose(1, 0, 2).reshape(block.shape[1], HEADS * HEAD)


def norm_apply(values, gain, shift):
    average = jnp.mean(values, axis=-1, keepdims=True)
    centered = values - average
    inv_scale = lax.rsqrt(jnp.mean(centered * centered, axis=-1, keepdims=True) + EPSILON)
    unit = centered * inv_scale
    return (unit * gain + shift, unit, inv_scale)


def norm_back(unit, inv_scale, gain, grad):
    scaled = grad * gain
    back = inv_scale * (
        scaled
        - jnp.mean(scaled, axis=-1, keepdims=True)
        - unit * jnp.mean(scaled * unit, axis=-1, keepdims=True)
    )
    return (back, jnp.sum(grad * unit, axis=0), jnp.sum(grad, axis=0))


def gelu_exact(values):
    return jax.nn.gelu(values, approximate=False)


def segment_ids(lengths_row, length):
    ends = jnp.cumsum(lengths_row)
    places = jnp.arange(length, dtype=jnp.int32)
    return jnp.sum((places[:, None] >= ends[None, :]).astype(jnp.int32), axis=1)


def pack_columns(parts, rows):
    cols = [p.reshape(rows, -1) for p in parts]
    width = sum(c.shape[1] for c in cols)
    pad = (-width) % 128
    if pad:
        cols.append(jnp.zeros((rows, pad), cols[0].dtype))
    return jnp.concatenate(cols, axis=1)


def unpack_columns(block, widths):
    out = []
    offset = 0
    for w in widths:
        out.append(block[:, offset : offset + w].reshape(-1))
        offset += w
    return out


def grad_rows_reduce(packed, group_size, shard_size):
    rows, cols = packed.shape
    n = rows // (group_size * shard_size)
    permuted = (
        packed.reshape(shard_size, group_size, n, cols)
        .transpose(1, 0, 2, 3)
        .reshape(rows, cols)
    )
    return lax.psum_scatter(
        permuted, ("group", "shard"), scatter_dimension=0, tiled=True
    )


def hypercube_orders(group_size, shard_size):
    gbits = [("group", b) for b in range(group_size.bit_length() - 1)]
    sbits = [("shard", b) for b in range(shard_size.bit_length() - 1)]
    first = gbits[:-1] + sbits + gbits[-1:]
    second = list(first)
    if len(gbits) >= 3:
        second[1], second[2] = first[2], first[1]
    return first, second


def hypercube_reduce_scatter(x, order, group_size, shard_size):
    total = group_size * shard_size
    levels = total.bit_length() - 1
    rows, cols = x.shape
    n = rows // total
    sbits = shard_size.bit_length() - 1

    def k_bit(axis, b):
        return b if axis == "shard" else sbits + b

    axes = [levels - 1 - k_bit(axis, b) for axis, b in order]
    cur = (
        x.reshape([2] * levels + [n, cols])
        .transpose(axes + [levels, levels + 1])
        .reshape(rows, cols)
    )
    for axis, b in order:
        size = group_size if axis == "group" else shard_size
        half = cur.shape[0] // 2
        mine = (lax.axis_index(axis) >> b) & 1
        low, high = cur[:half], cur[half:]
        keep = jnp.where(mine == 1, high, low)
        send = jnp.where(mine == 1, low, high).astype(jnp.bfloat16)
        got = lax.ppermute(send, axis, [(j, j ^ (1 << b)) for j in range(size)])
        cur = keep + got.astype(jnp.float32)
    return cur


def per_device(
    tokens,
    doc_lengths,
    first_gain,
    first_shift,
    qkv_weight,
    query_bias,
    value_bias,
    inner_gain,
    inner_shift,
    proj_weight,
    proj_bias,
    second_gain,
    second_shift,
    expand_weight,
    expand_bias,
    hidden_gain,
    hidden_shift,
    shrink_weight,
    shrink_bias,
    out_cotangent,
):
    group_size = lax.axis_size("group")
    shard_size = lax.axis_size("shard")
    n = qkv_weight.shape[0]
    model_width = n * group_size * shard_size
    wide_width = expand_weight.shape[1]
    ratio = wide_width // model_width
    qkv_width = qkv_weight.shape[1]

    small_parts = (
        first_gain,
        first_shift,
        query_bias,
        value_bias,
        inner_gain,
        inner_shift,
        proj_bias,
        second_gain,
        second_shift,
        shrink_bias,
        expand_bias,
        hidden_gain,
        hidden_shift,
    )
    small_widths = [p.shape[0] // n for p in small_parts]
    first_pack = jnp.concatenate([qkv_weight, pack_columns(small_parts, n)], axis=1)
    first_full = lax.all_gather(first_pack, ("group", "shard"), axis=0, tiled=True)
    qkv_full = first_full[:, :qkv_width]
    (
        gain_one,
        shift_one,
        qbias_full,
        vbias_full,
        gain_inner,
        shift_inner,
        pbias_full,
        gain_three,
        shift_three,
        sbias_full,
        ebias_full,
        gain_four,
        shift_four,
    ) = unpack_columns(first_full[:, qkv_width:], small_widths)
    second_pack = jnp.concatenate([proj_weight, expand_weight], axis=1)
    second_full = lax.all_gather(second_pack, ("group", "shard"), axis=0, tiled=True)
    proj_full = second_full[:, :model_width]
    expand_full = second_full[:, model_width:]
    shrink_full = lax.all_gather(shrink_weight, ("group", "shard"), axis=0, tiled=True)

    row_count = doc_lengths.shape[0]
    length = tokens.shape[0] // row_count
    inputs = tokens.astype(jnp.float32)
    normed, unit_one, inv_one = norm_apply(
        inputs, gain_one.astype(jnp.float32), shift_one.astype(jnp.float32)
    )
    normed_low = normed.astype(jnp.bfloat16)
    bias_cat = jnp.concatenate([qbias_full, jnp.zeros_like(qbias_full), vbias_full]).astype(
        jnp.float32
    )
    qkv_low = (jnp.dot(normed_low, qkv_full, preferred_element_type=jnp.float32) + bias_cat).astype(
        jnp.bfloat16
    )
    segments = jax.vmap(functools.partial(segment_ids, length=length))(doc_lengths).astype(
        jnp.int32
    )
    tq = min(QBLOCK, length)
    row_heads = []
    row_starts = []
    attended_rows = []
    for r in range(row_count):
        piece = qkv_low[r * length : (r + 1) * length]
        heads = tuple(
            heads_major(piece[:, j * model_width : (j + 1) * model_width]) for j in range(3)
        )
        lo = block_starts(segments[r], doc_lengths[r], tq)
        row_heads.append(heads)
        row_starts.append(lo)
        attended_rows.append(tokens_major(attention_forward(*heads, segments[r], lo)))
    attended = jnp.concatenate(attended_rows, axis=0)
    inner, unit_two, inv_two = norm_apply(
        attended, gain_inner.astype(jnp.float32), shift_inner.astype(jnp.float32)
    )
    inner_low = inner.astype(jnp.bfloat16)
    middle = (
        inputs
        + jnp.dot(inner_low, proj_full, preferred_element_type=jnp.float32)
        + pbias_full.astype(jnp.float32)
    )
    second, unit_three, inv_three = norm_apply(
        middle, gain_three.astype(jnp.float32), shift_three.astype(jnp.float32)
    )
    second_low = second.astype(jnp.bfloat16)
    pre_act = jnp.dot(
        second_low, expand_full, preferred_element_type=jnp.float32
    ) + ebias_full.astype(jnp.float32)
    activ, gelu_pull = jax.vjp(gelu_exact, pre_act)
    hidden, unit_four, inv_four = norm_apply(
        activ, gain_four.astype(jnp.float32), shift_four.astype(jnp.float32)
    )
    hidden_low = hidden.astype(jnp.bfloat16)
    output = (
        middle
        + jnp.dot(hidden_low, shrink_full, preferred_element_type=jnp.float32)
        + sbias_full.astype(jnp.float32)
    )
    block_output = output.astype(jnp.bfloat16)
    grad_out = out_cotangent.astype(jnp.float32)
    shrink_weight_grad = jnp.einsum(
        "tf,td->fd", hidden_low, out_cotangent, preferred_element_type=jnp.float32
    )
    shrink_bias_grad = jnp.sum(grad_out, axis=0)
    grad_hidden = jnp.einsum(
        "td,fd->tf", out_cotangent, shrink_full, preferred_element_type=jnp.float32
    )
    grad_activ, hidden_gain_grad, hidden_shift_grad = norm_back(
        unit_four, inv_four, gain_four.astype(jnp.float32), grad_hidden
    )
    grad_pre = gelu_pull(grad_activ)[0].astype(jnp.bfloat16)
    expand_bias_grad = jnp.sum(grad_pre.astype(jnp.float32), axis=0)
    expand_weight_grad = jnp.einsum(
        "td,tf->df", second_low, grad_pre, preferred_element_type=jnp.float32
    )
    grad_second = jnp.einsum("tf,df->td", grad_pre, expand_full, preferred_element_type=jnp.float32)
    grad_mid_part, second_gain_grad, second_shift_grad = norm_back(
        unit_three, inv_three, gain_three.astype(jnp.float32), grad_second
    )
    grad_middle = grad_out + grad_mid_part
    order_a, order_b = hypercube_orders(group_size, shard_size)
    shrink_in = (
        shrink_weight_grad.reshape(shard_size, group_size, -1, model_width)
        .transpose(1, 0, 2, 3)
        .reshape(wide_width, model_width)
    )
    grad_branch = grad_middle.astype(jnp.bfloat16)
    proj_bias_grad = jnp.sum(grad_branch.astype(jnp.float32), axis=0)
    proj_weight_grad = jnp.einsum(
        "td,te->de", inner_low, grad_branch, preferred_element_type=jnp.float32
    )
    grad_inner = jnp.einsum("te,de->td", grad_branch, proj_full, preferred_element_type=jnp.float32)
    grad_attended, inner_gain_grad, inner_shift_grad = norm_back(
        unit_two, inv_two, gain_inner.astype(jnp.float32), grad_inner
    )
    ffn_small = (
        second_gain_grad,
        second_shift_grad,
        shrink_bias_grad,
        expand_bias_grad,
        hidden_gain_grad,
        hidden_shift_grad,
        inner_gain_grad,
        inner_shift_grad,
        proj_bias_grad,
    )
    ffn_small_widths = [p.shape[0] // model_width for p in ffn_small]
    ffn_pack = jnp.concatenate(
        [
            expand_weight_grad,
            proj_weight_grad,
            pack_columns(ffn_small, model_width),
        ],
        axis=1,
    ).astype(jnp.bfloat16)
    grad_att_low = grad_attended.astype(jnp.bfloat16)
    ffn_pack, shrink_in, grad_att_low = lax.optimization_barrier(
        (ffn_pack, shrink_in, grad_att_low)
    )
    ffn_part = grad_rows_reduce(ffn_pack, group_size, shard_size)
    shrink_part = hypercube_reduce_scatter(shrink_in, order_a, group_size, shard_size)
    grad_rows = []
    for r in range(row_count):
        parts = attention_backward(
            *row_heads[r],
            heads_major(grad_att_low[r * length : (r + 1) * length]),
            segments[r],
            row_starts[r],
        )
        grad_rows.append(jnp.concatenate([tokens_major(p) for p in parts], axis=1))
    grad_qkv = jnp.concatenate(grad_rows, axis=0).astype(jnp.bfloat16)
    grad_qkv_wide = grad_qkv.astype(jnp.float32)
    query_bias_grad = jnp.sum(grad_qkv_wide[:, :model_width], axis=0)
    value_bias_grad = jnp.sum(grad_qkv_wide[:, 2 * model_width :], axis=0)
    qkv_weight_grad = jnp.einsum(
        "td,te->de", normed_low, grad_qkv, preferred_element_type=jnp.float32
    )
    grad_normed = jnp.einsum("te,de->td", grad_qkv, qkv_full, preferred_element_type=jnp.float32)
    grad_in_part, first_gain_grad, first_shift_grad = norm_back(
        unit_one, inv_one, gain_one.astype(jnp.float32), grad_normed
    )
    input_grad = (grad_middle + grad_in_part).astype(jnp.bfloat16)
    attn_small = (
        first_gain_grad,
        first_shift_grad,
        query_bias_grad,
        value_bias_grad,
    )
    attn_pack = jnp.concatenate(
        [qkv_weight_grad, pack_columns(attn_small, model_width)], axis=1
    )
    attn_pack = (
        attn_pack.reshape(shard_size, group_size, n, -1)
        .transpose(1, 0, 2, 3)
        .reshape(model_width, -1)
    )
    ffn_part, shrink_part, attn_pack = lax.optimization_barrier(
        (ffn_part, shrink_part, attn_pack)
    )
    split = (attn_pack.shape[1] // 256) * 128
    attn_left = hypercube_reduce_scatter(
        attn_pack[:, :split], order_a, group_size, shard_size
    )
    attn_right = hypercube_reduce_scatter(
        attn_pack[:, split:], order_b, group_size, shard_size
    )
    both = lax.all_gather(
        jnp.concatenate(
            [
                ffn_part,
                shrink_part.astype(jnp.bfloat16).reshape(n, ratio * model_width),
                attn_left.astype(jnp.bfloat16),
                attn_right.astype(jnp.bfloat16),
            ],
            axis=1,
        ),
        "group",
        axis=0,
        tiled=True,
    ).astype(jnp.float32)
    ffn_cols = ffn_pack.shape[1]
    ffn_back = both[:, :ffn_cols]
    shrink_back = both[:, ffn_cols : ffn_cols + ratio * model_width]
    attn_back = both[:, ffn_cols + ratio * model_width :]
    half = both.shape[0]
    expand_out = ffn_back[:, :wide_width]
    proj_out = ffn_back[:, wide_width : wide_width + model_width]
    shrink_out = shrink_back.reshape(half * ratio, model_width)
    (
        second_gain_out,
        second_shift_out,
        sbias_out,
        ebias_out,
        gain_four_out,
        shift_four_out,
        gain_inner_out,
        shift_inner_out,
        pbias_out,
    ) = unpack_columns(ffn_back[:, wide_width + model_width :], ffn_small_widths)
    qkv_out = attn_back[:, :qkv_width]
    (
        gain_one_out,
        shift_one_out,
        qbias_out,
        vbias_out,
    ) = unpack_columns(attn_back[:, qkv_width:], [1] * 4)
    return (
        block_output,
        input_grad,
        gain_one_out,
        shift_one_out,
        qkv_out,
        qbias_out,
        vbias_out,
        gain_inner_out,
        shift_inner_out,
        proj_out,
        pbias_out,
        second_gain_out,
        second_shift_out,
        expand_out,
        ebias_out,
        gain_four_out,
        shift_four_out,
        shrink_out,
        sbias_out,
    )


def solution(mesh):
    in_specs = (
        P(("group", "shard"), None),
        P(("group", "shard"), None),
        P(("group", "shard")),
        P(("group", "shard")),
        P(("group", "shard"), None),
        P(("group", "shard")),
        P(("group", "shard")),
        P(("group", "shard")),
        P(("group", "shard")),
        P(("group", "shard"), None),
        P(("group", "shard")),
        P(("group", "shard")),
        P(("group", "shard")),
        P(("group", "shard"), None),
        P(("group", "shard")),
        P(("group", "shard")),
        P(("group", "shard")),
        P(("group", "shard"), None),
        P(("group", "shard")),
        P(("group", "shard"), None),
    )
    out_specs = (
        P(("group", "shard"), None),
        P(("group", "shard"), None),
        P("shard"),
        P("shard"),
        P("shard", None),
        P("shard"),
        P("shard"),
        P("shard"),
        P("shard"),
        P("shard", None),
        P("shard"),
        P("shard"),
        P("shard"),
        P("shard", None),
        P("shard"),
        P("shard"),
        P("shard"),
        P("shard", None),
        P("shard"),
    )

    return jax.shard_map(
        per_device, mesh=mesh, in_specs=in_specs, out_specs=out_specs, check_vma=False
    )
```

```python
import functools

import jax
import jax.numpy as jnp
from jax import lax
from jax.experimental import pallas as pl
from jax.experimental.pallas import tpu as pltpu
from jax.sharding import PartitionSpec as P


HEADS = 12
HEAD = 64
NSEG = 5


EPSILON = 1e-05


MASKED = -1000000000.0

CHUNK = 128
QBLOCK = 512


def _row_setup(segq_ref, i, tq):
    segq = segq_ref[...]
    own = jnp.broadcast_to(jnp.where(segq < NSEG - 1, segq, -1), (tq, CHUNK))
    rel = (i * tq + lax.broadcasted_iota(jnp.int32, (tq, CHUNK), 0)) - lax.broadcasted_iota(
        jnp.int32, (tq, CHUNK), 1
    )
    keep = (segq < NSEG - 1).astype(jnp.float32)
    return own, rel, keep


def _softmax_rows(q, kt_ref, own, rel, segk_ref, lo, hi, s_ref):
    tq = q.shape[0]

    def first(c, top):
        kc = kt_ref[0, :, pl.ds(c * CHUNK, CHUNK)]
        s = jnp.dot(q, kc, preferred_element_type=jnp.float32)
        allowed = (own == segk_ref[:, pl.ds(c * CHUNK, CHUNK)]) & (rel >= c * CHUNK)
        s = jnp.where(allowed, s, MASKED)
        s_ref[:, pl.ds(c * CHUNK, CHUNK)] = s
        return jnp.maximum(top, s)

    top = lax.fori_loop(lo, hi, first, jnp.full((tq, CHUNK), MASKED, jnp.float32))
    peak = jnp.broadcast_to(jnp.max(top, axis=1, keepdims=True), (tq, CHUNK))

    def second(c, acc):
        e = jnp.exp(s_ref[:, pl.ds(c * CHUNK, CHUNK)] - peak)
        s_ref[:, pl.ds(c * CHUNK, CHUNK)] = e
        return acc + e

    acc = lax.fori_loop(lo, hi, second, jnp.zeros((tq, CHUNK), jnp.float32))
    return jnp.sum(acc, axis=1, keepdims=True)


def _fwd_kernel(lo_ref, q_ref, kt_ref, v_ref, segq_ref, segk_ref, o_ref, s_ref):
    i = pl.program_id(1)
    tq = q_ref.shape[1]
    q = q_ref[0] * jnp.asarray(0.125, q_ref.dtype)
    own, rel, keep = _row_setup(segq_ref, i, tq)
    lo = lo_ref[i]
    hi = (i + 1) * (tq // CHUNK)
    total = _softmax_rows(q, kt_ref, own, rel, segk_ref, lo, hi, s_ref)
    scale = jnp.broadcast_to(keep / total, (tq, CHUNK))

    def third(c, acc):
        p = (s_ref[:, pl.ds(c * CHUNK, CHUNK)] * scale).astype(jnp.bfloat16)
        vc = v_ref[0, pl.ds(c * CHUNK, CHUNK), :]
        return acc + jnp.dot(p, vc, preferred_element_type=jnp.float32)

    o_ref[0] = lax.fori_loop(lo, hi, third, jnp.zeros((tq, q.shape[1]), jnp.float32))


def _bwd_kernel(lo_ref, q_ref, qt_ref, k_ref, kt_ref, vt_ref, do_ref, dot_ref, segq_ref, segk_ref,
                dq_ref, dkt_ref, dvt_ref, s_ref, dp_ref):
    i = pl.program_id(1)
    tq = q_ref.shape[1]

    @pl.when(i == 0)
    def _():
        dkt_ref[...] = jnp.zeros_like(dkt_ref)
        dvt_ref[...] = jnp.zeros_like(dvt_ref)

    eighth = jnp.asarray(0.125, q_ref.dtype)
    qs = q_ref[0] * eighth
    qts = qt_ref[0] * eighth
    do = do_ref[0]
    dot_ = dot_ref[0]
    own, rel, keep = _row_setup(segq_ref, i, tq)
    lo = lo_ref[i]
    hi = (i + 1) * (tq // CHUNK)
    total = _softmax_rows(qs, kt_ref, own, rel, segk_ref, lo, hi, s_ref)
    scale = jnp.broadcast_to(keep / total, (tq, CHUNK))

    def third(c, acc):
        p = s_ref[:, pl.ds(c * CHUNK, CHUNK)] * scale
        dp = jnp.dot(do, vt_ref[0, :, pl.ds(c * CHUNK, CHUNK)], preferred_element_type=jnp.float32)
        s_ref[:, pl.ds(c * CHUNK, CHUNK)] = p
        dp_ref[:, pl.ds(c * CHUNK, CHUNK)] = dp
        return acc + p * dp

    acc = lax.fori_loop(lo, hi, third, jnp.zeros((tq, CHUNK), jnp.float32))
    inner = jnp.broadcast_to(jnp.sum(acc, axis=1, keepdims=True), (tq, CHUNK))

    def fourth(c, dq):
        cols = pl.ds(c * CHUNK, CHUNK)
        p = s_ref[:, cols]
        ds = (p * (dp_ref[:, cols] - inner)).astype(jnp.bfloat16)
        dkt_ref[0, :, cols] += jnp.dot(qts, ds, preferred_element_type=jnp.float32)
        dvt_ref[0, :, cols] += jnp.dot(dot_, p.astype(jnp.bfloat16), preferred_element_type=jnp.float32)
        return dq + jnp.dot(ds, k_ref[0, cols, :], preferred_element_type=jnp.float32)

    dq = lax.fori_loop(lo, hi, fourth, jnp.zeros((tq, q_ref.shape[2]), jnp.float32))
    dq_ref[0] = dq * 0.125


def attention_forward(q, k, v, seg, lo):
    heads, length, head = q.shape
    tq = min(QBLOCK, length)
    rows = pl.BlockSpec((1, tq, head), lambda h, i, lo: (h, i, 0))
    whole = pl.BlockSpec((1, length, head), lambda h, i, lo: (h, 0, 0))
    wide = pl.BlockSpec((1, head, length), lambda h, i, lo: (h, 0, 0))
    segq = pl.BlockSpec((tq, 1), lambda h, i, lo: (i, 0))
    segk = pl.BlockSpec((1, length), lambda h, i, lo: (0, 0))
    return pl.pallas_call(
        _fwd_kernel,
        out_shape=jax.ShapeDtypeStruct((heads, length, head), jnp.float32),
        grid_spec=pltpu.PrefetchScalarGridSpec(
            num_scalar_prefetch=1,
            grid=(heads, length // tq),
            in_specs=[rows, wide, whole, segq, segk],
            out_specs=rows,
            scratch_shapes=[pltpu.VMEM((tq, length), jnp.float32)],
        ),
        compiler_params=pltpu.CompilerParams(dimension_semantics=("arbitrary", "arbitrary")),
        cost_estimate=pl.CostEstimate(
            flops=2 * heads * length * length * head,
            transcendentals=heads * length * length // 2,
            bytes_accessed=4 * heads * length * head * 2,
        ),
    )(lo, q, k.transpose(0, 2, 1), v, seg[:, None], seg[None, :])


def attention_backward(q, k, v, do, seg, lo):
    heads, length, head = q.shape
    tq = min(QBLOCK, length)
    rows = pl.BlockSpec((1, tq, head), lambda h, i, lo: (h, i, 0))
    rows_t = pl.BlockSpec((1, head, tq), lambda h, i, lo: (h, 0, i))
    whole = pl.BlockSpec((1, length, head), lambda h, i, lo: (h, 0, 0))
    wide = pl.BlockSpec((1, head, length), lambda h, i, lo: (h, 0, 0))
    segq = pl.BlockSpec((tq, 1), lambda h, i, lo: (i, 0))
    segk = pl.BlockSpec((1, length), lambda h, i, lo: (0, 0))
    dq, dkt, dvt = pl.pallas_call(
        _bwd_kernel,
        out_shape=(
            jax.ShapeDtypeStruct((heads, length, head), jnp.float32),
            jax.ShapeDtypeStruct((heads, head, length), jnp.float32),
            jax.ShapeDtypeStruct((heads, head, length), jnp.float32),
        ),
        grid_spec=pltpu.PrefetchScalarGridSpec(
            num_scalar_prefetch=1,
            grid=(heads, length // tq),
            in_specs=[rows, rows_t, whole, wide, wide, rows, rows_t, segq, segk],
            out_specs=(rows, wide, wide),
            scratch_shapes=[pltpu.VMEM((tq, length), jnp.float32), pltpu.VMEM((tq, length), jnp.float32)],
        ),
        compiler_params=pltpu.CompilerParams(dimension_semantics=("arbitrary", "arbitrary")),
        cost_estimate=pl.CostEstimate(
            flops=5 * heads * length * length * head,
            transcendentals=heads * length * length // 2,
            bytes_accessed=8 * heads * length * head * 2,
        ),
    )(lo, q, q.transpose(0, 2, 1), k, k.transpose(0, 2, 1), v.transpose(0, 2, 1), do, do.transpose(0, 2, 1), seg[:, None], seg[None, :])
    return dq, dkt.transpose(0, 2, 1), dvt.transpose(0, 2, 1)


def block_starts(seg, lengths, tq):
    ends = jnp.cumsum(lengths)
    starts = jnp.concatenate([jnp.zeros((1,), ends.dtype), ends[:-1]])
    first_seg = seg[::tq]
    return (starts[first_seg] // CHUNK).astype(jnp.int32)


def heads_major(block):
    return block.reshape(block.shape[0], HEADS, HEAD).transpose(1, 0, 2)


def tokens_major(block):
    return block.transpose(1, 0, 2).reshape(block.shape[1], HEADS * HEAD)


def norm_apply(values, gain, shift):
    average = jnp.mean(values, axis=-1, keepdims=True)
    centered = values - average
    inv_scale = lax.rsqrt(jnp.mean(centered * centered, axis=-1, keepdims=True) + EPSILON)
    unit = centered * inv_scale
    return (unit * gain + shift, unit, inv_scale)


def norm_back(unit, inv_scale, gain, grad):
    scaled = grad * gain
    back = inv_scale * (
        scaled
        - jnp.mean(scaled, axis=-1, keepdims=True)
        - unit * jnp.mean(scaled * unit, axis=-1, keepdims=True)
    )
    return (back, jnp.sum(grad * unit, axis=0), jnp.sum(grad, axis=0))


def gelu_exact(values):
    return jax.nn.gelu(values, approximate=False)


def segment_ids(lengths_row, length):
    ends = jnp.cumsum(lengths_row)
    places = jnp.arange(length, dtype=jnp.int32)
    return jnp.sum((places[:, None] >= ends[None, :]).astype(jnp.int32), axis=1)


def pack_columns(parts, rows):
    cols = [p.reshape(rows, -1) for p in parts]
    width = sum(c.shape[1] for c in cols)
    pad = (-width) % 128
    if pad:
        cols.append(jnp.zeros((rows, pad), cols[0].dtype))
    return jnp.concatenate(cols, axis=1)


def unpack_columns(block, widths):
    out = []
    offset = 0
    for w in widths:
        out.append(block[:, offset : offset + w].reshape(-1))
        offset += w
    return out


def grad_rows_reduce(packed, group_size, shard_size):
    rows, cols = packed.shape
    n = rows // (group_size * shard_size)
    permuted = (
        packed.reshape(shard_size, group_size, n, cols)
        .transpose(1, 0, 2, 3)
        .reshape(rows, cols)
    )
    return lax.psum_scatter(
        permuted, ("group", "shard"), scatter_dimension=0, tiled=True
    )


def hypercube_orders(group_size, shard_size):
    gbits = [("group", b) for b in range(group_size.bit_length() - 1)]
    sbits = [("shard", b) for b in range(shard_size.bit_length() - 1)]
    first = gbits[:-1] + sbits + gbits[-1:]
    second = list(first)
    if len(gbits) >= 3:
        second[1], second[2] = first[2], first[1]
    return first, second


def hypercube_reduce_scatter(x, order, group_size, shard_size):
    total = group_size * shard_size
    levels = total.bit_length() - 1
    rows, cols = x.shape
    n = rows // total
    sbits = shard_size.bit_length() - 1

    def k_bit(axis, b):
        return b if axis == "shard" else sbits + b

    axes = [levels - 1 - k_bit(axis, b) for axis, b in order]
    cur = (
        x.reshape([2] * levels + [n, cols])
        .transpose(axes + [levels, levels + 1])
        .reshape(rows, cols)
    )
    for axis, b in order:
        size = group_size if axis == "group" else shard_size
        half = cur.shape[0] // 2
        mine = (lax.axis_index(axis) >> b) & 1
        low, high = cur[:half], cur[half:]
        keep = jnp.where(mine == 1, high, low)
        send = jnp.where(mine == 1, low, high).astype(jnp.bfloat16)
        got = lax.ppermute(send, axis, [(j, j ^ (1 << b)) for j in range(size)])
        cur = keep + got.astype(jnp.float32)
    return cur


def per_device(
    tokens,
    doc_lengths,
    first_gain,
    first_shift,
    qkv_weight,
    query_bias,
    value_bias,
    inner_gain,
    inner_shift,
    proj_weight,
    proj_bias,
    second_gain,
    second_shift,
    expand_weight,
    expand_bias,
    hidden_gain,
    hidden_shift,
    shrink_weight,
    shrink_bias,
    out_cotangent,
):
    group_size = lax.axis_size("group")
    shard_size = lax.axis_size("shard")
    n = qkv_weight.shape[0]
    model_width = n * group_size * shard_size
    wide_width = expand_weight.shape[1]
    ratio = wide_width // model_width
    qkv_width = qkv_weight.shape[1]

    small_parts = (
        first_gain,
        first_shift,
        query_bias,
        value_bias,
        inner_gain,
        inner_shift,
        proj_bias,
        second_gain,
        second_shift,
        shrink_bias,
        expand_bias,
        hidden_gain,
        hidden_shift,
    )
    small_widths = [p.shape[0] // n for p in small_parts]
    first_pack = jnp.concatenate([qkv_weight, pack_columns(small_parts, n)], axis=1)
    first_full = lax.all_gather(first_pack, ("group", "shard"), axis=0, tiled=True)
    qkv_full = first_full[:, :qkv_width]
    (
        gain_one,
        shift_one,
        qbias_full,
        vbias_full,
        gain_inner,
        shift_inner,
        pbias_full,
        gain_three,
        shift_three,
        sbias_full,
        ebias_full,
        gain_four,
        shift_four,
    ) = unpack_columns(first_full[:, qkv_width:], small_widths)
    second_pack = jnp.concatenate([proj_weight, expand_weight], axis=1)
    second_full = lax.all_gather(second_pack, ("group", "shard"), axis=0, tiled=True)
    proj_full = second_full[:, :model_width]
    expand_full = second_full[:, model_width:]
    shrink_full = lax.all_gather(shrink_weight, ("group", "shard"), axis=0, tiled=True)

    row_count = doc_lengths.shape[0]
    length = tokens.shape[0] // row_count
    inputs = tokens.astype(jnp.float32)
    normed, unit_one, inv_one = norm_apply(
        inputs, gain_one.astype(jnp.float32), shift_one.astype(jnp.float32)
    )
    normed_low = normed.astype(jnp.bfloat16)
    bias_cat = jnp.concatenate([qbias_full, jnp.zeros_like(qbias_full), vbias_full]).astype(
        jnp.float32
    )
    qkv_low = (jnp.dot(normed_low, qkv_full, preferred_element_type=jnp.float32) + bias_cat).astype(
        jnp.bfloat16
    )
    segments = jax.vmap(functools.partial(segment_ids, length=length))(doc_lengths).astype(
        jnp.int32
    )
    tq = min(QBLOCK, length)
    row_heads = []
    row_starts = []
    attended_rows = []
    for r in range(row_count):
        piece = qkv_low[r * length : (r + 1) * length]
        heads = tuple(
            heads_major(piece[:, j * model_width : (j + 1) * model_width]) for j in range(3)
        )
        lo = block_starts(segments[r], doc_lengths[r], tq)
        row_heads.append(heads)
        row_starts.append(lo)
        attended_rows.append(tokens_major(attention_forward(*heads, segments[r], lo)))
    attended = jnp.concatenate(attended_rows, axis=0)
    inner, unit_two, inv_two = norm_apply(
        attended, gain_inner.astype(jnp.float32), shift_inner.astype(jnp.float32)
    )
    inner_low = inner.astype(jnp.bfloat16)
    middle = (
        inputs
        + jnp.dot(inner_low, proj_full, preferred_element_type=jnp.float32)
        + pbias_full.astype(jnp.float32)
    )
    second, unit_three, inv_three = norm_apply(
        middle, gain_three.astype(jnp.float32), shift_three.astype(jnp.float32)
    )
    second_low = second.astype(jnp.bfloat16)
    pre_act = jnp.dot(
        second_low, expand_full, preferred_element_type=jnp.float32
    ) + ebias_full.astype(jnp.float32)
    activ, gelu_pull = jax.vjp(gelu_exact, pre_act)
    hidden, unit_four, inv_four = norm_apply(
        activ, gain_four.astype(jnp.float32), shift_four.astype(jnp.float32)
    )
    hidden_low = hidden.astype(jnp.bfloat16)
    output = (
        middle
        + jnp.dot(hidden_low, shrink_full, preferred_element_type=jnp.float32)
        + sbias_full.astype(jnp.float32)
    )
    block_output = output.astype(jnp.bfloat16)
    grad_out = out_cotangent.astype(jnp.float32)
    shrink_weight_grad = jnp.einsum(
        "tf,td->fd", hidden_low, out_cotangent, preferred_element_type=jnp.float32
    )
    shrink_bias_grad = jnp.sum(grad_out, axis=0)
    grad_hidden = jnp.einsum(
        "td,fd->tf", out_cotangent, shrink_full, preferred_element_type=jnp.float32
    )
    grad_activ, hidden_gain_grad, hidden_shift_grad = norm_back(
        unit_four, inv_four, gain_four.astype(jnp.float32), grad_hidden
    )
    grad_pre = gelu_pull(grad_activ)[0].astype(jnp.bfloat16)
    expand_bias_grad = jnp.sum(grad_pre.astype(jnp.float32), axis=0)
    expand_weight_grad = jnp.einsum(
        "td,tf->df", second_low, grad_pre, preferred_element_type=jnp.float32
    )
    grad_second = jnp.einsum("tf,df->td", grad_pre, expand_full, preferred_element_type=jnp.float32)
    grad_mid_part, second_gain_grad, second_shift_grad = norm_back(
        unit_three, inv_three, gain_three.astype(jnp.float32), grad_second
    )
    grad_middle = grad_out + grad_mid_part
    order_a, order_b = hypercube_orders(group_size, shard_size)
    shrink_in = (
        shrink_weight_grad.reshape(shard_size, group_size, -1, model_width)
        .transpose(1, 0, 2, 3)
        .reshape(wide_width, model_width)
    )
    grad_branch = grad_middle.astype(jnp.bfloat16)
    proj_bias_grad = jnp.sum(grad_branch.astype(jnp.float32), axis=0)
    proj_weight_grad = jnp.einsum(
        "td,te->de", inner_low, grad_branch, preferred_element_type=jnp.float32
    )
    grad_inner = jnp.einsum("te,de->td", grad_branch, proj_full, preferred_element_type=jnp.float32)
    grad_attended, inner_gain_grad, inner_shift_grad = norm_back(
        unit_two, inv_two, gain_inner.astype(jnp.float32), grad_inner
    )
    ffn_small = (
        second_gain_grad,
        second_shift_grad,
        shrink_bias_grad,
        expand_bias_grad,
        hidden_gain_grad,
        hidden_shift_grad,
        inner_gain_grad,
        inner_shift_grad,
        proj_bias_grad,
    )
    ffn_small_widths = [p.shape[0] // model_width for p in ffn_small]
    ffn_pack = jnp.concatenate(
        [
            expand_weight_grad,
            proj_weight_grad,
            pack_columns(ffn_small, model_width),
        ],
        axis=1,
    ).astype(jnp.bfloat16)
    grad_att_low = grad_attended.astype(jnp.bfloat16)
    ffn_pack, shrink_in, grad_att_low = lax.optimization_barrier(
        (ffn_pack, shrink_in, grad_att_low)
    )
    ffn_part = grad_rows_reduce(ffn_pack, group_size, shard_size)
    shrink_part = hypercube_reduce_scatter(shrink_in, order_a, group_size, shard_size)
    grad_rows = []
    for r in range(row_count):
        parts = attention_backward(
            *row_heads[r],
            heads_major(grad_att_low[r * length : (r + 1) * length]),
            segments[r],
            row_starts[r],
        )
        grad_rows.append(jnp.concatenate([tokens_major(p) for p in parts], axis=1))
    grad_qkv = jnp.concatenate(grad_rows, axis=0).astype(jnp.bfloat16)
    grad_qkv_wide = grad_qkv.astype(jnp.float32)
    query_bias_grad = jnp.sum(grad_qkv_wide[:, :model_width], axis=0)
    value_bias_grad = jnp.sum(grad_qkv_wide[:, 2 * model_width :], axis=0)
    qkv_weight_grad = jnp.einsum(
        "td,te->de", normed_low, grad_qkv, preferred_element_type=jnp.float32
    )
    grad_normed = jnp.einsum("te,de->td", grad_qkv, qkv_full, preferred_element_type=jnp.float32)
    grad_in_part, first_gain_grad, first_shift_grad = norm_back(
        unit_one, inv_one, gain_one.astype(jnp.float32), grad_normed
    )
    input_grad = (grad_middle + grad_in_part).astype(jnp.bfloat16)
    attn_small = (
        first_gain_grad,
        first_shift_grad,
        query_bias_grad,
        value_bias_grad,
    )
    attn_pack = jnp.concatenate(
        [qkv_weight_grad, pack_columns(attn_small, model_width)], axis=1
    )
    attn_pack = (
        attn_pack.reshape(shard_size, group_size, n, -1)
        .transpose(1, 0, 2, 3)
        .reshape(model_width, -1)
    )
    ffn_part, shrink_part, attn_pack = lax.optimization_barrier(
        (ffn_part, shrink_part, attn_pack)
    )
    split = (attn_pack.shape[1] // 256) * 128
    attn_left = hypercube_reduce_scatter(
        attn_pack[:, :split], order_a, group_size, shard_size
    )
    attn_right = hypercube_reduce_scatter(
        attn_pack[:, split:], order_b, group_size, shard_size
    )
    both = lax.all_gather(
        jnp.concatenate(
            [
                ffn_part,
                shrink_part.astype(jnp.bfloat16).reshape(n, ratio * model_width),
                attn_left.astype(jnp.bfloat16),
                attn_right.astype(jnp.bfloat16),
            ],
            axis=1,
        ),
        "group",
        axis=0,
        tiled=True,
    ).astype(jnp.float32)
    ffn_cols = ffn_pack.shape[1]
    ffn_back = both[:, :ffn_cols]
    shrink_back = both[:, ffn_cols : ffn_cols + ratio * model_width]
    attn_back = both[:, ffn_cols + ratio * model_width :]
    half = both.shape[0]
    expand_out = ffn_back[:, :wide_width]
    proj_out = ffn_back[:, wide_width : wide_width + model_width]
    shrink_out = shrink_back.reshape(half * ratio, model_width)
    (
        second_gain_out,
        second_shift_out,
        sbias_out,
        ebias_out,
        gain_four_out,
        shift_four_out,
        gain_inner_out,
        shift_inner_out,
        pbias_out,
    ) = unpack_columns(ffn_back[:, wide_width + model_width :], ffn_small_widths)
    qkv_out = attn_back[:, :qkv_width]
    (
        gain_one_out,
        shift_one_out,
        qbias_out,
        vbias_out,
    ) = unpack_columns(attn_back[:, qkv_width:], [1] * 4)
    return (
        block_output,
        input_grad,
        gain_one_out,
        shift_one_out,
        qkv_out,
        qbias_out,
        vbias_out,
        gain_inner_out,
        shift_inner_out,
        proj_out,
        pbias_out,
        second_gain_out,
        second_shift_out,
        expand_out,
        ebias_out,
        gain_four_out,
        shift_four_out,
        shrink_out,
        sbias_out,
    )


def solution(mesh):
    in_specs = (
        P(("group", "shard"), None),
        P(("group", "shard"), None),
        P(("group", "shard")),
        P(("group", "shard")),
        P(("group", "shard"), None),
        P(("group", "shard")),
        P(("group", "shard")),
        P(("group", "shard")),
        P(("group", "shard")),
        P(("group", "shard"), None),
        P(("group", "shard")),
        P(("group", "shard")),
        P(("group", "shard")),
        P(("group", "shard"), None),
        P(("group", "shard")),
        P(("group", "shard")),
        P(("group", "shard")),
        P(("group", "shard"), None),
        P(("group", "shard")),
        P(("group", "shard"), None),
    )
    out_specs = (
        P(("group", "shard"), None),
        P(("group", "shard"), None),
        P("shard"),
        P("shard"),
        P("shard", None),
        P("shard"),
        P("shard"),
        P("shard"),
        P("shard"),
        P("shard", None),
        P("shard"),
        P("shard"),
        P("shard"),
        P("shard", None),
        P("shard"),
        P("shard"),
        P("shard"),
        P("shard", None),
        P("shard"),
    )

    return jax.shard_map(
        per_device, mesh=mesh, in_specs=in_specs, out_specs=out_specs, check_vma=False
    )
```

```python
import functools

import jax
import jax.numpy as jnp
from jax import lax
from jax.experimental import pallas as pl
from jax.experimental.pallas import tpu as pltpu
from jax.sharding import PartitionSpec as P


HEADS = 12
HEAD = 64
NSEG = 5


EPSILON = 1e-05


MASKED = -1000000000.0

CHUNK = 128
QBLOCK = 512
HEAD_GROUP = 2


def _row_setup(segq_ref, i, tq):
    segq = segq_ref[...]
    own = jnp.broadcast_to(jnp.where(segq < NSEG - 1, segq, -1), (tq, CHUNK))
    rel = (i * tq + lax.broadcasted_iota(jnp.int32, (tq, CHUNK), 0)) - lax.broadcasted_iota(
        jnp.int32, (tq, CHUNK), 1
    )
    keep = (segq < NSEG - 1).astype(jnp.float32)
    return own, rel, keep


def _softmax_rows(q, kt_ref, own, rel, segk_ref, lo, hi, s_ref):
    tq = q.shape[0]

    def first(c, top):
        kc = kt_ref[0, :, pl.ds(c * CHUNK, CHUNK)]
        s = jnp.dot(q, kc, preferred_element_type=jnp.float32)
        allowed = (own == segk_ref[:, pl.ds(c * CHUNK, CHUNK)]) & (rel >= c * CHUNK)
        s = jnp.where(allowed, s, MASKED)
        s_ref[:, pl.ds(c * CHUNK, CHUNK)] = s
        return jnp.maximum(top, s)

    top = lax.fori_loop(lo, hi, first, jnp.full((tq, CHUNK), MASKED, jnp.float32))
    peak = jnp.broadcast_to(jnp.max(top, axis=1, keepdims=True), (tq, CHUNK))

    def second(c, acc):
        e = jnp.exp(s_ref[:, pl.ds(c * CHUNK, CHUNK)] - peak)
        s_ref[:, pl.ds(c * CHUNK, CHUNK)] = e
        return acc + e

    acc = lax.fori_loop(lo, hi, second, jnp.zeros((tq, CHUNK), jnp.float32))
    return jnp.sum(acc, axis=1, keepdims=True)


def _fwd_kernel(lo_ref, q_ref, kt_ref, v_ref, segq_ref, segk_ref, o_ref, s_ref):
    i = pl.program_id(1)
    tq = q_ref.shape[1]
    q = q_ref[0] * jnp.asarray(0.125, q_ref.dtype)
    own, rel, keep = _row_setup(segq_ref, i, tq)
    lo = lo_ref[i]
    hi = (i + 1) * (tq // CHUNK)
    total = _softmax_rows(q, kt_ref, own, rel, segk_ref, lo, hi, s_ref)
    scale = jnp.broadcast_to(keep / total, (tq, CHUNK))

    def third(c, acc):
        p = (s_ref[:, pl.ds(c * CHUNK, CHUNK)] * scale).astype(jnp.bfloat16)
        vc = v_ref[0, pl.ds(c * CHUNK, CHUNK), :]
        return acc + jnp.dot(p, vc, preferred_element_type=jnp.float32)

    o_ref[0] = lax.fori_loop(lo, hi, third, jnp.zeros((tq, q.shape[1]), jnp.float32))


def _bwd_kernel(lo_ref, q_ref, qt_ref, k_ref, kt_ref, vt_ref, do_ref, dot_ref, segq_ref, segk_ref,
                dq_ref, dkt_ref, dvt_ref, s_ref, dp_ref):
    i = pl.program_id(1)
    tq = q_ref.shape[1]

    @pl.when(i == 0)
    def _():
        dkt_ref[...] = jnp.zeros_like(dkt_ref)
        dvt_ref[...] = jnp.zeros_like(dvt_ref)

    eighth = jnp.asarray(0.125, q_ref.dtype)
    qs = q_ref[0] * eighth
    qts = qt_ref[0] * eighth
    do = do_ref[0]
    dot_ = dot_ref[0]
    own, rel, keep = _row_setup(segq_ref, i, tq)
    lo = lo_ref[i]
    hi = (i + 1) * (tq // CHUNK)
    total = _softmax_rows(qs, kt_ref, own, rel, segk_ref, lo, hi, s_ref)
    scale = jnp.broadcast_to(keep / total, (tq, CHUNK))

    def third(c, acc):
        p = s_ref[:, pl.ds(c * CHUNK, CHUNK)] * scale
        dp = jnp.dot(do, vt_ref[0, :, pl.ds(c * CHUNK, CHUNK)], preferred_element_type=jnp.float32)
        s_ref[:, pl.ds(c * CHUNK, CHUNK)] = p
        dp_ref[:, pl.ds(c * CHUNK, CHUNK)] = dp
        return acc + p * dp

    acc = lax.fori_loop(lo, hi, third, jnp.zeros((tq, CHUNK), jnp.float32))
    inner = jnp.broadcast_to(jnp.sum(acc, axis=1, keepdims=True), (tq, CHUNK))

    def fourth(c, dq):
        cols = pl.ds(c * CHUNK, CHUNK)
        p = s_ref[:, cols]
        ds = (p * (dp_ref[:, cols] - inner)).astype(jnp.bfloat16)
        dkt_ref[0, :, cols] += jnp.dot(qts, ds, preferred_element_type=jnp.float32)
        dvt_ref[0, :, cols] += jnp.dot(dot_, p.astype(jnp.bfloat16), preferred_element_type=jnp.float32)
        return dq + jnp.dot(ds, k_ref[0, cols, :], preferred_element_type=jnp.float32)

    dq = lax.fori_loop(lo, hi, fourth, jnp.zeros((tq, q_ref.shape[2]), jnp.float32))
    dq_ref[0] = dq * 0.125


def attention_forward(q, k, v, seg, lo):
    heads, length, head = q.shape
    tq = min(QBLOCK, length)
    rows = pl.BlockSpec((1, tq, head), lambda h, i, lo: (h, i, 0))
    whole = pl.BlockSpec((1, length, head), lambda h, i, lo: (h, 0, 0))
    wide = pl.BlockSpec((1, head, length), lambda h, i, lo: (h, 0, 0))
    segq = pl.BlockSpec((tq, 1), lambda h, i, lo: (i, 0))
    segk = pl.BlockSpec((1, length), lambda h, i, lo: (0, 0))
    return pl.pallas_call(
        _fwd_kernel,
        out_shape=jax.ShapeDtypeStruct((heads, length, head), jnp.float32),
        grid_spec=pltpu.PrefetchScalarGridSpec(
            num_scalar_prefetch=1,
            grid=(heads, length // tq),
            in_specs=[rows, wide, whole, segq, segk],
            out_specs=rows,
            scratch_shapes=[pltpu.VMEM((tq, length), jnp.float32)],
        ),
        compiler_params=pltpu.CompilerParams(dimension_semantics=("arbitrary", "arbitrary")),
        cost_estimate=pl.CostEstimate(
            flops=2 * heads * length * length * head,
            transcendentals=heads * length * length // 2,
            bytes_accessed=4 * heads * length * head * 2,
        ),
    )(lo, q, k.transpose(0, 2, 1), v, seg[:, None], seg[None, :])


def attention_backward(q, k, v, do, seg, lo):
    heads, length, head = q.shape
    tq = min(QBLOCK, length)
    rows = pl.BlockSpec((1, tq, head), lambda h, i, lo: (h, i, 0))
    rows_t = pl.BlockSpec((1, head, tq), lambda h, i, lo: (h, 0, i))
    whole = pl.BlockSpec((1, length, head), lambda h, i, lo: (h, 0, 0))
    wide = pl.BlockSpec((1, head, length), lambda h, i, lo: (h, 0, 0))
    segq = pl.BlockSpec((tq, 1), lambda h, i, lo: (i, 0))
    segk = pl.BlockSpec((1, length), lambda h, i, lo: (0, 0))
    dq, dkt, dvt = pl.pallas_call(
        _bwd_kernel,
        out_shape=(
            jax.ShapeDtypeStruct((heads, length, head), jnp.float32),
            jax.ShapeDtypeStruct((heads, head, length), jnp.float32),
            jax.ShapeDtypeStruct((heads, head, length), jnp.float32),
        ),
        grid_spec=pltpu.PrefetchScalarGridSpec(
            num_scalar_prefetch=1,
            grid=(heads, length // tq),
            in_specs=[rows, rows_t, whole, wide, wide, rows, rows_t, segq, segk],
            out_specs=(rows, wide, wide),
            scratch_shapes=[pltpu.VMEM((tq, length), jnp.float32), pltpu.VMEM((tq, length), jnp.float32)],
        ),
        compiler_params=pltpu.CompilerParams(dimension_semantics=("arbitrary", "arbitrary")),
        cost_estimate=pl.CostEstimate(
            flops=5 * heads * length * length * head,
            transcendentals=heads * length * length // 2,
            bytes_accessed=8 * heads * length * head * 2,
        ),
    )(lo, q, q.transpose(0, 2, 1), k, k.transpose(0, 2, 1), v.transpose(0, 2, 1), do, do.transpose(0, 2, 1), seg[:, None], seg[None, :])
    return dq, dkt.transpose(0, 2, 1), dvt.transpose(0, 2, 1)


def block_starts(seg, lengths, tq):
    ends = jnp.cumsum(lengths)
    starts = jnp.concatenate([jnp.zeros((1,), ends.dtype), ends[:-1]])
    first_seg = seg[::tq]
    return (starts[first_seg] // CHUNK).astype(jnp.int32)


def heads_major(block):
    return block.reshape(block.shape[0], HEADS, HEAD).transpose(1, 0, 2)


def tokens_major(block):
    return block.transpose(1, 0, 2).reshape(block.shape[1], HEADS * HEAD)


def norm_apply(values, gain, shift):
    average = jnp.mean(values, axis=-1, keepdims=True)
    centered = values - average
    inv_scale = lax.rsqrt(jnp.mean(centered * centered, axis=-1, keepdims=True) + EPSILON)
    unit = centered * inv_scale
    return (unit * gain + shift, unit, inv_scale)


def norm_back(unit, inv_scale, gain, grad):
    scaled = grad * gain
    back = inv_scale * (
        scaled
        - jnp.mean(scaled, axis=-1, keepdims=True)
        - unit * jnp.mean(scaled * unit, axis=-1, keepdims=True)
    )
    return (back, jnp.sum(grad * unit, axis=0), jnp.sum(grad, axis=0))


def gelu_exact(values):
    return jax.nn.gelu(values, approximate=False)


def segment_ids(lengths_row, length):
    ends = jnp.cumsum(lengths_row)
    places = jnp.arange(length, dtype=jnp.int32)
    return jnp.sum((places[:, None] >= ends[None, :]).astype(jnp.int32), axis=1)


def pack_columns(parts, rows):
    cols = [p.reshape(rows, -1) for p in parts]
    width = sum(c.shape[1] for c in cols)
    pad = (-width) % 128
    if pad:
        cols.append(jnp.zeros((rows, pad), cols[0].dtype))
    return jnp.concatenate(cols, axis=1)


def unpack_columns(block, widths):
    out = []
    offset = 0
    for w in widths:
        out.append(block[:, offset : offset + w].reshape(-1))
        offset += w
    return out


def grad_rows_reduce(packed, group_size, shard_size):
    rows, cols = packed.shape
    n = rows // (group_size * shard_size)
    permuted = (
        packed.reshape(shard_size, group_size, n, cols)
        .transpose(1, 0, 2, 3)
        .reshape(rows, cols)
    )
    return lax.psum_scatter(
        permuted, ("group", "shard"), scatter_dimension=0, tiled=True
    )


def hypercube_orders(group_size, shard_size):
    gbits = [("group", b) for b in range(group_size.bit_length() - 1)]
    sbits = [("shard", b) for b in range(shard_size.bit_length() - 1)]
    first = gbits[:-1] + sbits + gbits[-1:]
    second = list(first)
    if len(gbits) >= 3:
        second[1], second[2] = first[2], first[1]
    return first, second


def hypercube_reduce_scatter(x, order, group_size, shard_size, ties=()):
    total = group_size * shard_size
    levels = total.bit_length() - 1
    rows, cols = x.shape
    n = rows // total
    sbits = shard_size.bit_length() - 1

    def k_bit(axis, b):
        return b if axis == "shard" else sbits + b

    axes = [levels - 1 - k_bit(axis, b) for axis, b in order]
    cur = (
        x.reshape([2] * levels + [n, cols])
        .transpose(axes + [levels, levels + 1])
        .reshape(rows, cols)
    )
    for step, (axis, b) in enumerate(order):
        size = group_size if axis == "group" else shard_size
        half = cur.shape[0] // 2
        mine = (lax.axis_index(axis) >> b) & 1
        low, high = cur[:half], cur[half:]
        keep = jnp.where(mine == 1, high, low)
        send = jnp.where(mine == 1, low, high).astype(jnp.bfloat16)
        got = lax.ppermute(send, axis, [(j, j ^ (1 << b)) for j in range(size)])
        cur = keep + got.astype(jnp.float32)
        if step < len(ties):
            cur, tied = lax.optimization_barrier((cur, ties[step]))
            ties = ties[:step] + (tied,) + ties[step + 1 :]
    return cur, ties


def per_device(
    tokens,
    doc_lengths,
    first_gain,
    first_shift,
    qkv_weight,
    query_bias,
    value_bias,
    inner_gain,
    inner_shift,
    proj_weight,
    proj_bias,
    second_gain,
    second_shift,
    expand_weight,
    expand_bias,
    hidden_gain,
    hidden_shift,
    shrink_weight,
    shrink_bias,
    out_cotangent,
):
    group_size = lax.axis_size("group")
    shard_size = lax.axis_size("shard")
    n = qkv_weight.shape[0]
    model_width = n * group_size * shard_size
    wide_width = expand_weight.shape[1]
    ratio = wide_width // model_width
    qkv_width = qkv_weight.shape[1]

    small_parts = (
        first_gain,
        first_shift,
        query_bias,
        value_bias,
        inner_gain,
        inner_shift,
        proj_bias,
        second_gain,
        second_shift,
        shrink_bias,
        expand_bias,
        hidden_gain,
        hidden_shift,
    )
    small_widths = [p.shape[0] // n for p in small_parts]
    first_pack = jnp.concatenate([qkv_weight, pack_columns(small_parts, n)], axis=1)
    first_full = lax.all_gather(first_pack, ("group", "shard"), axis=0, tiled=True)
    qkv_full = first_full[:, :qkv_width]
    (
        gain_one,
        shift_one,
        qbias_full,
        vbias_full,
        gain_inner,
        shift_inner,
        pbias_full,
        gain_three,
        shift_three,
        sbias_full,
        ebias_full,
        gain_four,
        shift_four,
    ) = unpack_columns(first_full[:, qkv_width:], small_widths)
    second_pack = jnp.concatenate([proj_weight, expand_weight], axis=1)
    second_full = lax.all_gather(second_pack, ("group", "shard"), axis=0, tiled=True)
    proj_full = second_full[:, :model_width]
    expand_full = second_full[:, model_width:]
    shrink_full = lax.all_gather(shrink_weight, ("group", "shard"), axis=0, tiled=True)

    row_count = doc_lengths.shape[0]
    length = tokens.shape[0] // row_count
    inputs = tokens.astype(jnp.float32)
    normed, unit_one, inv_one = norm_apply(
        inputs, gain_one.astype(jnp.float32), shift_one.astype(jnp.float32)
    )
    normed_low = normed.astype(jnp.bfloat16)
    bias_cat = jnp.concatenate([qbias_full, jnp.zeros_like(qbias_full), vbias_full]).astype(
        jnp.float32
    )
    qkv_low = (jnp.dot(normed_low, qkv_full, preferred_element_type=jnp.float32) + bias_cat).astype(
        jnp.bfloat16
    )
    segments = jax.vmap(functools.partial(segment_ids, length=length))(doc_lengths).astype(
        jnp.int32
    )
    tq = min(QBLOCK, length)
    row_heads = []
    row_starts = []
    attended_rows = []
    for r in range(row_count):
        piece = qkv_low[r * length : (r + 1) * length]
        heads = tuple(
            heads_major(piece[:, j * model_width : (j + 1) * model_width]) for j in range(3)
        )
        lo = block_starts(segments[r], doc_lengths[r], tq)
        row_heads.append(heads)
        row_starts.append(lo)
        attended_rows.append(tokens_major(attention_forward(*heads, segments[r], lo)))
    attended = jnp.concatenate(attended_rows, axis=0)
    inner, unit_two, inv_two = norm_apply(
        attended, gain_inner.astype(jnp.float32), shift_inner.astype(jnp.float32)
    )
    inner_low = inner.astype(jnp.bfloat16)
    middle = (
        inputs
        + jnp.dot(inner_low, proj_full, preferred_element_type=jnp.float32)
        + pbias_full.astype(jnp.float32)
    )
    second, unit_three, inv_three = norm_apply(
        middle, gain_three.astype(jnp.float32), shift_three.astype(jnp.float32)
    )
    second_low = second.astype(jnp.bfloat16)
    pre_act = jnp.dot(
        second_low, expand_full, preferred_element_type=jnp.float32
    ) + ebias_full.astype(jnp.float32)
    activ, gelu_pull = jax.vjp(gelu_exact, pre_act)
    hidden, unit_four, inv_four = norm_apply(
        activ, gain_four.astype(jnp.float32), shift_four.astype(jnp.float32)
    )
    hidden_low = hidden.astype(jnp.bfloat16)
    output = (
        middle
        + jnp.dot(hidden_low, shrink_full, preferred_element_type=jnp.float32)
        + sbias_full.astype(jnp.float32)
    )
    block_output = output.astype(jnp.bfloat16)
    grad_out = out_cotangent.astype(jnp.float32)
    shrink_weight_grad = jnp.einsum(
        "tf,td->fd", hidden_low, out_cotangent, preferred_element_type=jnp.float32
    )
    shrink_bias_grad = jnp.sum(grad_out, axis=0)
    grad_hidden = jnp.einsum(
        "td,fd->tf", out_cotangent, shrink_full, preferred_element_type=jnp.float32
    )
    grad_activ, hidden_gain_grad, hidden_shift_grad = norm_back(
        unit_four, inv_four, gain_four.astype(jnp.float32), grad_hidden
    )
    grad_pre = gelu_pull(grad_activ)[0].astype(jnp.bfloat16)
    expand_bias_grad = jnp.sum(grad_pre.astype(jnp.float32), axis=0)
    expand_weight_grad = jnp.einsum(
        "td,tf->df", second_low, grad_pre, preferred_element_type=jnp.float32
    )
    grad_second = jnp.einsum("tf,df->td", grad_pre, expand_full, preferred_element_type=jnp.float32)
    grad_mid_part, second_gain_grad, second_shift_grad = norm_back(
        unit_three, inv_three, gain_three.astype(jnp.float32), grad_second
    )
    grad_middle = grad_out + grad_mid_part
    order_a, order_b = hypercube_orders(group_size, shard_size)
    shrink_in = (
        shrink_weight_grad.reshape(shard_size, group_size, -1, model_width)
        .transpose(1, 0, 2, 3)
        .reshape(wide_width, model_width)
    )
    grad_branch = grad_middle.astype(jnp.bfloat16)
    proj_bias_grad = jnp.sum(grad_branch.astype(jnp.float32), axis=0)
    proj_weight_grad = jnp.einsum(
        "td,te->de", inner_low, grad_branch, preferred_element_type=jnp.float32
    )
    grad_inner = jnp.einsum("te,de->td", grad_branch, proj_full, preferred_element_type=jnp.float32)
    grad_attended, inner_gain_grad, inner_shift_grad = norm_back(
        unit_two, inv_two, gain_inner.astype(jnp.float32), grad_inner
    )
    ffn_small = (
        second_gain_grad,
        second_shift_grad,
        shrink_bias_grad,
        expand_bias_grad,
        hidden_gain_grad,
        hidden_shift_grad,
        inner_gain_grad,
        inner_shift_grad,
        proj_bias_grad,
    )
    ffn_small_widths = [p.shape[0] // model_width for p in ffn_small]
    ffn_pack = jnp.concatenate(
        [
            expand_weight_grad,
            proj_weight_grad,
            pack_columns(ffn_small, model_width),
        ],
        axis=1,
    ).astype(jnp.bfloat16)
    grad_att_low = grad_attended.astype(jnp.bfloat16)
    ffn_pack, shrink_in, grad_att_low = lax.optimization_barrier(
        (ffn_pack, shrink_in, grad_att_low)
    )
    ffn_part = grad_rows_reduce(ffn_pack, group_size, shard_size)
    grad_att_low = grad_att_low.astype(jnp.bfloat16)
    group_inputs = []
    for r in range(row_count):
        grad_heads = heads_major(grad_att_low[r * length : (r + 1) * length])
        for h in range(0, HEADS, HEAD_GROUP):
            group_inputs.append(
                tuple(x[h : h + HEAD_GROUP] for x in row_heads[r])
                + (grad_heads[h : h + HEAD_GROUP],)
            )
    shrink_part, tied = hypercube_reduce_scatter(
        shrink_in, order_a, group_size, shard_size, tuple(group_inputs[1:])
    )
    group_inputs = group_inputs[:1] + list(tied)
    grad_rows = []
    per_row = HEADS // HEAD_GROUP
    for r in range(row_count):
        pieces = [
            attention_backward(*group_inputs[r * per_row + j], segments[r], row_starts[r])
            for j in range(per_row)
        ]
        parts = [jnp.concatenate([p[j] for p in pieces], axis=0) for j in range(3)]
        grad_rows.append(jnp.concatenate([tokens_major(p) for p in parts], axis=1))
    grad_qkv = jnp.concatenate(grad_rows, axis=0).astype(jnp.bfloat16)
    grad_qkv_wide = grad_qkv.astype(jnp.float32)
    query_bias_grad = jnp.sum(grad_qkv_wide[:, :model_width], axis=0)
    value_bias_grad = jnp.sum(grad_qkv_wide[:, 2 * model_width :], axis=0)
    qkv_weight_grad = jnp.einsum(
        "td,te->de", normed_low, grad_qkv, preferred_element_type=jnp.float32
    )
    grad_normed = jnp.einsum("te,de->td", grad_qkv, qkv_full, preferred_element_type=jnp.float32)
    grad_in_part, first_gain_grad, first_shift_grad = norm_back(
        unit_one, inv_one, gain_one.astype(jnp.float32), grad_normed
    )
    input_grad = (grad_middle + grad_in_part).astype(jnp.bfloat16)
    attn_small = (
        first_gain_grad,
        first_shift_grad,
        query_bias_grad,
        value_bias_grad,
    )
    attn_pack = jnp.concatenate(
        [qkv_weight_grad, pack_columns(attn_small, model_width)], axis=1
    )
    attn_pack = (
        attn_pack.reshape(shard_size, group_size, n, -1)
        .transpose(1, 0, 2, 3)
        .reshape(model_width, -1)
    )
    ffn_part, shrink_part, attn_pack = lax.optimization_barrier(
        (ffn_part, shrink_part, attn_pack)
    )
    split = (attn_pack.shape[1] // 256) * 128
    attn_left, _ = hypercube_reduce_scatter(attn_pack[:, :split], order_a, group_size, shard_size)
    attn_right, _ = hypercube_reduce_scatter(attn_pack[:, split:], order_b, group_size, shard_size)
    ffn_both = lax.all_gather(
        jnp.concatenate(
            [ffn_part, shrink_part.astype(jnp.bfloat16).reshape(n, ratio * model_width)],
            axis=1,
        ),
        "group",
        axis=0,
        tiled=True,
    ).astype(jnp.float32)
    attn_back = lax.all_gather(
        jnp.concatenate(
            [attn_left.astype(jnp.bfloat16), attn_right.astype(jnp.bfloat16)], axis=1
        ),
        "group",
        axis=0,
        tiled=True,
    ).astype(jnp.float32)
    ffn_cols = ffn_pack.shape[1]
    ffn_back = ffn_both[:, :ffn_cols]
    shrink_back = ffn_both[:, ffn_cols:]
    half = ffn_both.shape[0]
    expand_out = ffn_back[:, :wide_width]
    proj_out = ffn_back[:, wide_width : wide_width + model_width]
    shrink_out = shrink_back.reshape(half * ratio, model_width)
    (
        second_gain_out,
        second_shift_out,
        sbias_out,
        ebias_out,
        gain_four_out,
        shift_four_out,
        gain_inner_out,
        shift_inner_out,
        pbias_out,
    ) = unpack_columns(ffn_back[:, wide_width + model_width :], ffn_small_widths)
    qkv_out = attn_back[:, :qkv_width]
    (
        gain_one_out,
        shift_one_out,
        qbias_out,
        vbias_out,
    ) = unpack_columns(attn_back[:, qkv_width:], [1] * 4)
    return (
        block_output,
        input_grad,
        gain_one_out,
        shift_one_out,
        qkv_out,
        qbias_out,
        vbias_out,
        gain_inner_out,
        shift_inner_out,
        proj_out,
        pbias_out,
        second_gain_out,
        second_shift_out,
        expand_out,
        ebias_out,
        gain_four_out,
        shift_four_out,
        shrink_out,
        sbias_out,
    )


def solution(mesh):
    in_specs = (
        P(("group", "shard"), None),
        P(("group", "shard"), None),
        P(("group", "shard")),
        P(("group", "shard")),
        P(("group", "shard"), None),
        P(("group", "shard")),
        P(("group", "shard")),
        P(("group", "shard")),
        P(("group", "shard")),
        P(("group", "shard"), None),
        P(("group", "shard")),
        P(("group", "shard")),
        P(("group", "shard")),
        P(("group", "shard"), None),
        P(("group", "shard")),
        P(("group", "shard")),
        P(("group", "shard")),
        P(("group", "shard"), None),
        P(("group", "shard")),
        P(("group", "shard"), None),
    )
    out_specs = (
        P(("group", "shard"), None),
        P(("group", "shard"), None),
        P("shard"),
        P("shard"),
        P("shard", None),
        P("shard"),
        P("shard"),
        P("shard"),
        P("shard"),
        P("shard", None),
        P("shard"),
        P("shard"),
        P("shard"),
        P("shard", None),
        P("shard"),
        P("shard"),
        P("shard"),
        P("shard", None),
        P("shard"),
    )

    return jax.shard_map(
        per_device, mesh=mesh, in_specs=in_specs, out_specs=out_specs, check_vma=False
    )
```

```python
import functools

import jax
import jax.numpy as jnp
from jax import lax
from jax.experimental import pallas as pl
from jax.experimental.pallas import tpu as pltpu
from jax.sharding import PartitionSpec as P


HEADS = 12
HEAD = 64
NSEG = 5


EPSILON = 1e-05


MASKED = -1000000000.0

CHUNK = 128
QBLOCK = 512


def _row_setup(segq_ref, i, tq):
    segq = segq_ref[...]
    own = jnp.broadcast_to(jnp.where(segq < NSEG - 1, segq, -1), (tq, CHUNK))
    rel = (i * tq + lax.broadcasted_iota(jnp.int32, (tq, CHUNK), 0)) - lax.broadcasted_iota(
        jnp.int32, (tq, CHUNK), 1
    )
    keep = (segq < NSEG - 1).astype(jnp.float32)
    return own, rel, keep


def _softmax_rows(q, kt_ref, own, rel, segk_ref, lo, hi, s_ref):
    tq = q.shape[0]

    def first(c, top):
        kc = kt_ref[0, :, pl.ds(c * CHUNK, CHUNK)]
        s = jnp.dot(q, kc, preferred_element_type=jnp.float32)
        allowed = (own == segk_ref[:, pl.ds(c * CHUNK, CHUNK)]) & (rel >= c * CHUNK)
        s = jnp.where(allowed, s, MASKED)
        s_ref[:, pl.ds(c * CHUNK, CHUNK)] = s
        return jnp.maximum(top, s)

    top = lax.fori_loop(lo, hi, first, jnp.full((tq, CHUNK), MASKED, jnp.float32))
    peak = jnp.broadcast_to(jnp.max(top, axis=1, keepdims=True), (tq, CHUNK))

    def second(c, acc):
        e = jnp.exp(s_ref[:, pl.ds(c * CHUNK, CHUNK)] - peak)
        s_ref[:, pl.ds(c * CHUNK, CHUNK)] = e
        return acc + e

    acc = lax.fori_loop(lo, hi, second, jnp.zeros((tq, CHUNK), jnp.float32))
    return jnp.sum(acc, axis=1, keepdims=True)


def _fwd_kernel(lo_ref, q_ref, kt_ref, v_ref, segq_ref, segk_ref, o_ref, s_ref):
    i = pl.program_id(1)
    tq = q_ref.shape[1]
    q = q_ref[0] * jnp.asarray(0.125, q_ref.dtype)
    own, rel, keep = _row_setup(segq_ref, i, tq)
    lo = lo_ref[i]
    hi = (i + 1) * (tq // CHUNK)
    total = _softmax_rows(q, kt_ref, own, rel, segk_ref, lo, hi, s_ref)
    scale = jnp.broadcast_to(keep / total, (tq, CHUNK))

    def third(c, acc):
        p = (s_ref[:, pl.ds(c * CHUNK, CHUNK)] * scale).astype(jnp.bfloat16)
        vc = v_ref[0, pl.ds(c * CHUNK, CHUNK), :]
        return acc + jnp.dot(p, vc, preferred_element_type=jnp.float32)

    o_ref[0] = lax.fori_loop(lo, hi, third, jnp.zeros((tq, q.shape[1]), jnp.float32))


def _bwd_kernel(lo_ref, q_ref, qt_ref, k_ref, kt_ref, vt_ref, do_ref, dot_ref, segq_ref, segk_ref,
                dq_ref, dkt_ref, dvt_ref, s_ref, dp_ref):
    i = pl.program_id(1)
    tq = q_ref.shape[1]

    @pl.when(i == 0)
    def _():
        dkt_ref[...] = jnp.zeros_like(dkt_ref)
        dvt_ref[...] = jnp.zeros_like(dvt_ref)

    eighth = jnp.asarray(0.125, q_ref.dtype)
    qs = q_ref[0] * eighth
    qts = qt_ref[0] * eighth
    do = do_ref[0]
    dot_ = dot_ref[0]
    own, rel, keep = _row_setup(segq_ref, i, tq)
    lo = lo_ref[i]
    hi = (i + 1) * (tq // CHUNK)
    total = _softmax_rows(qs, kt_ref, own, rel, segk_ref, lo, hi, s_ref)
    scale = jnp.broadcast_to(keep / total, (tq, CHUNK))

    def third(c, acc):
        p = s_ref[:, pl.ds(c * CHUNK, CHUNK)] * scale
        dp = jnp.dot(do, vt_ref[0, :, pl.ds(c * CHUNK, CHUNK)], preferred_element_type=jnp.float32)
        s_ref[:, pl.ds(c * CHUNK, CHUNK)] = p
        dp_ref[:, pl.ds(c * CHUNK, CHUNK)] = dp
        return acc + p * dp

    acc = lax.fori_loop(lo, hi, third, jnp.zeros((tq, CHUNK), jnp.float32))
    inner = jnp.broadcast_to(jnp.sum(acc, axis=1, keepdims=True), (tq, CHUNK))

    def fourth(c, dq):
        cols = pl.ds(c * CHUNK, CHUNK)
        p = s_ref[:, cols]
        ds = (p * (dp_ref[:, cols] - inner)).astype(jnp.bfloat16)
        dkt_ref[0, :, cols] += jnp.dot(qts, ds, preferred_element_type=jnp.float32)
        dvt_ref[0, :, cols] += jnp.dot(dot_, p.astype(jnp.bfloat16), preferred_element_type=jnp.float32)
        return dq + jnp.dot(ds, k_ref[0, cols, :], preferred_element_type=jnp.float32)

    dq = lax.fori_loop(lo, hi, fourth, jnp.zeros((tq, q_ref.shape[2]), jnp.float32))
    dq_ref[0] = dq * 0.125


def attention_forward(q, k, v, seg, lo):
    heads, length, head = q.shape
    tq = min(QBLOCK, length)
    rows = pl.BlockSpec((1, tq, head), lambda h, i, lo: (h, i, 0))
    whole = pl.BlockSpec((1, length, head), lambda h, i, lo: (h, 0, 0))
    wide = pl.BlockSpec((1, head, length), lambda h, i, lo: (h, 0, 0))
    segq = pl.BlockSpec((tq, 1), lambda h, i, lo: (i, 0))
    segk = pl.BlockSpec((1, length), lambda h, i, lo: (0, 0))
    return pl.pallas_call(
        _fwd_kernel,
        out_shape=jax.ShapeDtypeStruct((heads, length, head), jnp.float32),
        grid_spec=pltpu.PrefetchScalarGridSpec(
            num_scalar_prefetch=1,
            grid=(heads, length // tq),
            in_specs=[rows, wide, whole, segq, segk],
            out_specs=rows,
            scratch_shapes=[pltpu.VMEM((tq, length), jnp.float32)],
        ),
        compiler_params=pltpu.CompilerParams(dimension_semantics=("arbitrary", "arbitrary")),
        cost_estimate=pl.CostEstimate(
            flops=2 * heads * length * length * head,
            transcendentals=heads * length * length // 2,
            bytes_accessed=4 * heads * length * head * 2,
        ),
    )(lo, q, k.transpose(0, 2, 1), v, seg[:, None], seg[None, :])


def attention_backward(q, k, v, do, seg, lo):
    heads, length, head = q.shape
    tq = min(QBLOCK, length)
    rows = pl.BlockSpec((1, tq, head), lambda h, i, lo: (h, i, 0))
    rows_t = pl.BlockSpec((1, head, tq), lambda h, i, lo: (h, 0, i))
    whole = pl.BlockSpec((1, length, head), lambda h, i, lo: (h, 0, 0))
    wide = pl.BlockSpec((1, head, length), lambda h, i, lo: (h, 0, 0))
    segq = pl.BlockSpec((tq, 1), lambda h, i, lo: (i, 0))
    segk = pl.BlockSpec((1, length), lambda h, i, lo: (0, 0))
    dq, dkt, dvt = pl.pallas_call(
        _bwd_kernel,
        out_shape=(
            jax.ShapeDtypeStruct((heads, length, head), jnp.float32),
            jax.ShapeDtypeStruct((heads, head, length), jnp.float32),
            jax.ShapeDtypeStruct((heads, head, length), jnp.float32),
        ),
        grid_spec=pltpu.PrefetchScalarGridSpec(
            num_scalar_prefetch=1,
            grid=(heads, length // tq),
            in_specs=[rows, rows_t, whole, wide, wide, rows, rows_t, segq, segk],
            out_specs=(rows, wide, wide),
            scratch_shapes=[pltpu.VMEM((tq, length), jnp.float32), pltpu.VMEM((tq, length), jnp.float32)],
        ),
        compiler_params=pltpu.CompilerParams(dimension_semantics=("arbitrary", "arbitrary")),
        cost_estimate=pl.CostEstimate(
            flops=5 * heads * length * length * head,
            transcendentals=heads * length * length // 2,
            bytes_accessed=8 * heads * length * head * 2,
        ),
    )(lo, q, q.transpose(0, 2, 1), k, k.transpose(0, 2, 1), v.transpose(0, 2, 1), do, do.transpose(0, 2, 1), seg[:, None], seg[None, :])
    return dq, dkt.transpose(0, 2, 1), dvt.transpose(0, 2, 1)


def block_starts(seg, lengths, tq):
    ends = jnp.cumsum(lengths)
    starts = jnp.concatenate([jnp.zeros((1,), ends.dtype), ends[:-1]])
    first_seg = seg[::tq]
    return (starts[first_seg] // CHUNK).astype(jnp.int32)


def heads_major(block):
    return block.reshape(block.shape[0], HEADS, HEAD).transpose(1, 0, 2)


def tokens_major(block):
    return block.transpose(1, 0, 2).reshape(block.shape[1], HEADS * HEAD)


def norm_apply(values, gain, shift):
    average = jnp.mean(values, axis=-1, keepdims=True)
    centered = values - average
    inv_scale = lax.rsqrt(jnp.mean(centered * centered, axis=-1, keepdims=True) + EPSILON)
    unit = centered * inv_scale
    return (unit * gain + shift, unit, inv_scale)


def norm_back(unit, inv_scale, gain, grad):
    scaled = grad * gain
    back = inv_scale * (
        scaled
        - jnp.mean(scaled, axis=-1, keepdims=True)
        - unit * jnp.mean(scaled * unit, axis=-1, keepdims=True)
    )
    return (back, jnp.sum(grad * unit, axis=0), jnp.sum(grad, axis=0))


def gelu_exact(values):
    return jax.nn.gelu(values, approximate=False)


def segment_ids(lengths_row, length):
    ends = jnp.cumsum(lengths_row)
    places = jnp.arange(length, dtype=jnp.int32)
    return jnp.sum((places[:, None] >= ends[None, :]).astype(jnp.int32), axis=1)


def pack_columns(parts, rows):
    cols = [p.reshape(rows, -1) for p in parts]
    width = sum(c.shape[1] for c in cols)
    pad = (-width) % 128
    if pad:
        cols.append(jnp.zeros((rows, pad), cols[0].dtype))
    return jnp.concatenate(cols, axis=1)


def unpack_columns(block, widths):
    out = []
    offset = 0
    for w in widths:
        out.append(block[:, offset : offset + w].reshape(-1))
        offset += w
    return out


def grad_rows_reduce(packed, group_size, shard_size):
    rows, cols = packed.shape
    n = rows // (group_size * shard_size)
    permuted = (
        packed.reshape(shard_size, group_size, n, cols)
        .transpose(1, 0, 2, 3)
        .reshape(rows, cols)
    )
    return lax.psum_scatter(
        permuted, ("group", "shard"), scatter_dimension=0, tiled=True
    )


def hypercube_orders(group_size, shard_size):
    gbits = [("group", b) for b in range(group_size.bit_length() - 1)]
    sbits = [("shard", b) for b in range(shard_size.bit_length() - 1)]
    first = gbits[:-1] + sbits + gbits[-1:]
    second = list(first)
    if len(gbits) >= 3:
        second[1], second[2] = first[2], first[1]
    return first, second


def hypercube_reduce_scatter(x, order, group_size, shard_size):
    total = group_size * shard_size
    levels = total.bit_length() - 1
    rows, cols = x.shape
    n = rows // total
    sbits = shard_size.bit_length() - 1

    def k_bit(axis, b):
        return b if axis == "shard" else sbits + b

    axes = [levels - 1 - k_bit(axis, b) for axis, b in order]
    cur = (
        x.reshape([2] * levels + [n, cols])
        .transpose(axes + [levels, levels + 1])
        .reshape(rows, cols)
    )
    for axis, b in order:
        size = group_size if axis == "group" else shard_size
        half = cur.shape[0] // 2
        mine = (lax.axis_index(axis) >> b) & 1
        low, high = cur[:half], cur[half:]
        keep = jnp.where(mine == 1, high, low)
        send = jnp.where(mine == 1, low, high).astype(jnp.bfloat16)
        got = lax.ppermute(send, axis, [(j, j ^ (1 << b)) for j in range(size)])
        cur = keep + got.astype(jnp.float32)
    return cur


def per_device(
    tokens,
    doc_lengths,
    first_gain,
    first_shift,
    qkv_weight,
    query_bias,
    value_bias,
    inner_gain,
    inner_shift,
    proj_weight,
    proj_bias,
    second_gain,
    second_shift,
    expand_weight,
    expand_bias,
    hidden_gain,
    hidden_shift,
    shrink_weight,
    shrink_bias,
    out_cotangent,
):
    group_size = lax.axis_size("group")
    shard_size = lax.axis_size("shard")
    n = qkv_weight.shape[0]
    model_width = n * group_size * shard_size
    wide_width = expand_weight.shape[1]
    ratio = wide_width // model_width
    qkv_width = qkv_weight.shape[1]

    small_parts = (
        first_gain,
        first_shift,
        query_bias,
        value_bias,
        inner_gain,
        inner_shift,
        proj_bias,
        second_gain,
        second_shift,
        shrink_bias,
        expand_bias,
        hidden_gain,
        hidden_shift,
    )
    small_widths = [p.shape[0] // n for p in small_parts]
    first_pack = jnp.concatenate([qkv_weight, pack_columns(small_parts, n)], axis=1)
    first_full = lax.all_gather(first_pack, ("group", "shard"), axis=0, tiled=True)
    qkv_full = first_full[:, :qkv_width]
    (
        gain_one,
        shift_one,
        qbias_full,
        vbias_full,
        gain_inner,
        shift_inner,
        pbias_full,
        gain_three,
        shift_three,
        sbias_full,
        ebias_full,
        gain_four,
        shift_four,
    ) = unpack_columns(first_full[:, qkv_width:], small_widths)
    second_pack = jnp.concatenate([proj_weight, expand_weight], axis=1)
    second_full = lax.all_gather(second_pack, ("group", "shard"), axis=0, tiled=True)
    proj_full = second_full[:, :model_width]
    expand_full = second_full[:, model_width:]
    shrink_full = lax.all_gather(shrink_weight, ("group", "shard"), axis=0, tiled=True)

    row_count = doc_lengths.shape[0]
    length = tokens.shape[0] // row_count
    inputs = tokens.astype(jnp.float32)
    normed, unit_one, inv_one = norm_apply(
        inputs, gain_one.astype(jnp.float32), shift_one.astype(jnp.float32)
    )
    normed_low = normed.astype(jnp.bfloat16)
    bias_cat = jnp.concatenate([qbias_full, jnp.zeros_like(qbias_full), vbias_full]).astype(
        jnp.float32
    )
    qkv_low = (jnp.dot(normed_low, qkv_full, preferred_element_type=jnp.float32) + bias_cat).astype(
        jnp.bfloat16
    )
    segments = jax.vmap(functools.partial(segment_ids, length=length))(doc_lengths).astype(
        jnp.int32
    )
    tq = min(QBLOCK, length)
    row_heads = []
    row_starts = []
    attended_rows = []
    for r in range(row_count):
        piece = qkv_low[r * length : (r + 1) * length]
        heads = tuple(
            heads_major(piece[:, j * model_width : (j + 1) * model_width]) for j in range(3)
        )
        lo = block_starts(segments[r], doc_lengths[r], tq)
        row_heads.append(heads)
        row_starts.append(lo)
        attended_rows.append(tokens_major(attention_forward(*heads, segments[r], lo)))
    attended = jnp.concatenate(attended_rows, axis=0)
    inner, unit_two, inv_two = norm_apply(
        attended, gain_inner.astype(jnp.float32), shift_inner.astype(jnp.float32)
    )
    inner_low = inner.astype(jnp.bfloat16)
    middle = (
        inputs
        + jnp.dot(inner_low, proj_full, preferred_element_type=jnp.float32)
        + pbias_full.astype(jnp.float32)
    )
    second, unit_three, inv_three = norm_apply(
        middle, gain_three.astype(jnp.float32), shift_three.astype(jnp.float32)
    )
    second_low = second.astype(jnp.bfloat16)
    pre_act = jnp.dot(
        second_low, expand_full, preferred_element_type=jnp.float32
    ) + ebias_full.astype(jnp.float32)
    activ, gelu_pull = jax.vjp(gelu_exact, pre_act)
    hidden, unit_four, inv_four = norm_apply(
        activ, gain_four.astype(jnp.float32), shift_four.astype(jnp.float32)
    )
    hidden_low = hidden.astype(jnp.bfloat16)
    output = (
        middle
        + jnp.dot(hidden_low, shrink_full, preferred_element_type=jnp.float32)
        + sbias_full.astype(jnp.float32)
    )
    block_output = output.astype(jnp.bfloat16)
    grad_out = out_cotangent.astype(jnp.float32)
    shrink_weight_grad = jnp.einsum(
        "tf,td->fd", hidden_low, out_cotangent, preferred_element_type=jnp.float32
    )
    shrink_bias_grad = jnp.sum(grad_out, axis=0)
    grad_hidden = jnp.einsum(
        "td,fd->tf", out_cotangent, shrink_full, preferred_element_type=jnp.float32
    )
    grad_activ, hidden_gain_grad, hidden_shift_grad = norm_back(
        unit_four, inv_four, gain_four.astype(jnp.float32), grad_hidden
    )
    grad_pre = gelu_pull(grad_activ)[0].astype(jnp.bfloat16)
    expand_bias_grad = jnp.sum(grad_pre.astype(jnp.float32), axis=0)
    expand_weight_grad = jnp.einsum(
        "td,tf->df", second_low, grad_pre, preferred_element_type=jnp.float32
    )
    grad_second = jnp.einsum("tf,df->td", grad_pre, expand_full, preferred_element_type=jnp.float32)
    grad_mid_part, second_gain_grad, second_shift_grad = norm_back(
        unit_three, inv_three, gain_three.astype(jnp.float32), grad_second
    )
    grad_middle = grad_out + grad_mid_part
    order_a, order_b = hypercube_orders(group_size, shard_size)
    grad_branch = grad_middle.astype(jnp.bfloat16)
    proj_bias_grad = jnp.sum(grad_branch.astype(jnp.float32), axis=0)
    proj_weight_grad = jnp.einsum(
        "td,te->de", inner_low, grad_branch, preferred_element_type=jnp.float32
    )
    grad_inner = jnp.einsum("te,de->td", grad_branch, proj_full, preferred_element_type=jnp.float32)
    grad_attended, inner_gain_grad, inner_shift_grad = norm_back(
        unit_two, inv_two, gain_inner.astype(jnp.float32), grad_inner
    )
    ffn_small = (
        second_gain_grad,
        second_shift_grad,
        shrink_bias_grad,
        expand_bias_grad,
        hidden_gain_grad,
        hidden_shift_grad,
        inner_gain_grad,
        inner_shift_grad,
        proj_bias_grad,
    )
    ffn_small_widths = [p.shape[0] // model_width for p in ffn_small]
    ffn_pack = jnp.concatenate(
        [
            expand_weight_grad,
            shrink_weight_grad.reshape(model_width, ratio * model_width),
            proj_weight_grad,
            pack_columns(ffn_small, model_width),
        ],
        axis=1,
    ).astype(jnp.bfloat16)
    grad_att_low = grad_attended.astype(jnp.bfloat16)
    ffn_pack, grad_att_low = lax.optimization_barrier((ffn_pack, grad_att_low))
    ffn_part = grad_rows_reduce(ffn_pack, group_size, shard_size)
    grad_rows = []
    for r in range(row_count):
        parts = attention_backward(
            *row_heads[r],
            heads_major(grad_att_low[r * length : (r + 1) * length]),
            segments[r],
            row_starts[r],
        )
        grad_rows.append(jnp.concatenate([tokens_major(p) for p in parts], axis=1))
    grad_qkv = jnp.concatenate(grad_rows, axis=0).astype(jnp.bfloat16)
    grad_qkv_wide = grad_qkv.astype(jnp.float32)
    query_bias_grad = jnp.sum(grad_qkv_wide[:, :model_width], axis=0)
    value_bias_grad = jnp.sum(grad_qkv_wide[:, 2 * model_width :], axis=0)
    qkv_weight_grad = jnp.einsum(
        "td,te->de", normed_low, grad_qkv, preferred_element_type=jnp.float32
    )
    grad_normed = jnp.einsum("te,de->td", grad_qkv, qkv_full, preferred_element_type=jnp.float32)
    grad_in_part, first_gain_grad, first_shift_grad = norm_back(
        unit_one, inv_one, gain_one.astype(jnp.float32), grad_normed
    )
    input_grad = (grad_middle + grad_in_part).astype(jnp.bfloat16)
    attn_small = (
        first_gain_grad,
        first_shift_grad,
        query_bias_grad,
        value_bias_grad,
    )
    attn_pack = jnp.concatenate(
        [qkv_weight_grad, pack_columns(attn_small, model_width)], axis=1
    )
    attn_pack = (
        attn_pack.reshape(shard_size, group_size, n, -1)
        .transpose(1, 0, 2, 3)
        .reshape(model_width, -1)
    )
    ffn_part, attn_pack = lax.optimization_barrier((ffn_part, attn_pack))
    split = (attn_pack.shape[1] // 256) * 128
    attn_left = hypercube_reduce_scatter(
        attn_pack[:, :split], order_a, group_size, shard_size
    )
    attn_right = hypercube_reduce_scatter(
        attn_pack[:, split:], order_b, group_size, shard_size
    )
    both = lax.all_gather(
        jnp.concatenate(
            [
                ffn_part,
                attn_left.astype(jnp.bfloat16),
                attn_right.astype(jnp.bfloat16),
            ],
            axis=1,
        ),
        "group",
        axis=0,
        tiled=True,
    ).astype(jnp.float32)
    ffn_cols = ffn_pack.shape[1]
    ffn_back = both[:, :ffn_cols]
    attn_back = both[:, ffn_cols:]
    half = both.shape[0]
    expand_out = ffn_back[:, :wide_width]
    shrink_out = ffn_back[:, wide_width : 2 * wide_width].reshape(half * ratio, model_width)
    proj_out = ffn_back[:, 2 * wide_width : 2 * wide_width + model_width]
    (
        second_gain_out,
        second_shift_out,
        sbias_out,
        ebias_out,
        gain_four_out,
        shift_four_out,
        gain_inner_out,
        shift_inner_out,
        pbias_out,
    ) = unpack_columns(ffn_back[:, 2 * wide_width + model_width :], ffn_small_widths)
    qkv_out = attn_back[:, :qkv_width]
    (
        gain_one_out,
        shift_one_out,
        qbias_out,
        vbias_out,
    ) = unpack_columns(attn_back[:, qkv_width:], [1] * 4)
    return (
        block_output,
        input_grad,
        gain_one_out,
        shift_one_out,
        qkv_out,
        qbias_out,
        vbias_out,
        gain_inner_out,
        shift_inner_out,
        proj_out,
        pbias_out,
        second_gain_out,
        second_shift_out,
        expand_out,
        ebias_out,
        gain_four_out,
        shift_four_out,
        shrink_out,
        sbias_out,
    )


def solution(mesh):
    in_specs = (
        P(("group", "shard"), None),
        P(("group", "shard"), None),
        P(("group", "shard")),
        P(("group", "shard")),
        P(("group", "shard"), None),
        P(("group", "shard")),
        P(("group", "shard")),
        P(("group", "shard")),
        P(("group", "shard")),
        P(("group", "shard"), None),
        P(("group", "shard")),
        P(("group", "shard")),
        P(("group", "shard")),
        P(("group", "shard"), None),
        P(("group", "shard")),
        P(("group", "shard")),
        P(("group", "shard")),
        P(("group", "shard"), None),
        P(("group", "shard")),
        P(("group", "shard"), None),
    )
    out_specs = (
        P(("group", "shard"), None),
        P(("group", "shard"), None),
        P("shard"),
        P("shard"),
        P("shard", None),
        P("shard"),
        P("shard"),
        P("shard"),
        P("shard"),
        P("shard", None),
        P("shard"),
        P("shard"),
        P("shard"),
        P("shard", None),
        P("shard"),
        P("shard"),
        P("shard"),
        P("shard", None),
        P("shard"),
    )

    return jax.shard_map(
        per_device, mesh=mesh, in_specs=in_specs, out_specs=out_specs, check_vma=False
    )
```

```python
import functools

import jax
import jax.numpy as jnp
from jax import lax
from jax.experimental import pallas as pl
from jax.experimental.pallas import tpu as pltpu
from jax.sharding import PartitionSpec as P


HEADS = 12
HEAD = 64
NSEG = 5


EPSILON = 1e-05


MASKED = -1000000000.0

CHUNK = 128
QBLOCK = 512


def _row_setup(segq_ref, i, tq):
    segq = segq_ref[...]
    own = jnp.broadcast_to(jnp.where(segq < NSEG - 1, segq, -1), (tq, CHUNK))
    rel = (i * tq + lax.broadcasted_iota(jnp.int32, (tq, CHUNK), 0)) - lax.broadcasted_iota(
        jnp.int32, (tq, CHUNK), 1
    )
    keep = (segq < NSEG - 1).astype(jnp.float32)
    return own, rel, keep


def _softmax_rows(q, kt_ref, own, rel, segk_ref, lo, hi, s_ref):
    tq = q.shape[0]

    def first(c, top):
        kc = kt_ref[0, :, pl.ds(c * CHUNK, CHUNK)]
        s = jnp.dot(q, kc, preferred_element_type=jnp.float32)
        allowed = (own == segk_ref[:, pl.ds(c * CHUNK, CHUNK)]) & (rel >= c * CHUNK)
        s = jnp.where(allowed, s, MASKED)
        s_ref[:, pl.ds(c * CHUNK, CHUNK)] = s
        return jnp.maximum(top, s)

    top = lax.fori_loop(lo, hi, first, jnp.full((tq, CHUNK), MASKED, jnp.float32))
    peak = jnp.broadcast_to(jnp.max(top, axis=1, keepdims=True), (tq, CHUNK))

    def second(c, acc):
        e = jnp.exp(s_ref[:, pl.ds(c * CHUNK, CHUNK)] - peak)
        s_ref[:, pl.ds(c * CHUNK, CHUNK)] = e
        return acc + e

    acc = lax.fori_loop(lo, hi, second, jnp.zeros((tq, CHUNK), jnp.float32))
    return jnp.sum(acc, axis=1, keepdims=True)


def _fwd_kernel(lo_ref, q_ref, kt_ref, v_ref, segq_ref, segk_ref, o_ref, s_ref):
    i = pl.program_id(1)
    tq = q_ref.shape[1]
    q = q_ref[0] * jnp.asarray(0.125, q_ref.dtype)
    own, rel, keep = _row_setup(segq_ref, i, tq)
    lo = lo_ref[i]
    hi = (i + 1) * (tq // CHUNK)
    total = _softmax_rows(q, kt_ref, own, rel, segk_ref, lo, hi, s_ref)
    scale = jnp.broadcast_to(keep / total, (tq, CHUNK))

    def third(c, acc):
        p = (s_ref[:, pl.ds(c * CHUNK, CHUNK)] * scale).astype(jnp.bfloat16)
        vc = v_ref[0, pl.ds(c * CHUNK, CHUNK), :]
        return acc + jnp.dot(p, vc, preferred_element_type=jnp.float32)

    o_ref[0] = lax.fori_loop(lo, hi, third, jnp.zeros((tq, q.shape[1]), jnp.float32))


def _bwd_kernel(lo_ref, q_ref, qt_ref, k_ref, kt_ref, vt_ref, do_ref, dot_ref, segq_ref, segk_ref,
                dq_ref, dkt_ref, dvt_ref, s_ref, dp_ref):
    i = pl.program_id(1)
    tq = q_ref.shape[1]

    @pl.when(i == 0)
    def _():
        dkt_ref[...] = jnp.zeros_like(dkt_ref)
        dvt_ref[...] = jnp.zeros_like(dvt_ref)

    eighth = jnp.asarray(0.125, q_ref.dtype)
    qs = q_ref[0] * eighth
    qts = qt_ref[0] * eighth
    do = do_ref[0]
    dot_ = dot_ref[0]
    own, rel, keep = _row_setup(segq_ref, i, tq)
    lo = lo_ref[i]
    hi = (i + 1) * (tq // CHUNK)
    total = _softmax_rows(qs, kt_ref, own, rel, segk_ref, lo, hi, s_ref)
    scale = jnp.broadcast_to(keep / total, (tq, CHUNK))

    def third(c, acc):
        p = s_ref[:, pl.ds(c * CHUNK, CHUNK)] * scale
        dp = jnp.dot(do, vt_ref[0, :, pl.ds(c * CHUNK, CHUNK)], preferred_element_type=jnp.float32)
        s_ref[:, pl.ds(c * CHUNK, CHUNK)] = p
        dp_ref[:, pl.ds(c * CHUNK, CHUNK)] = dp
        return acc + p * dp

    acc = lax.fori_loop(lo, hi, third, jnp.zeros((tq, CHUNK), jnp.float32))
    inner = jnp.broadcast_to(jnp.sum(acc, axis=1, keepdims=True), (tq, CHUNK))

    def fourth(c, dq):
        cols = pl.ds(c * CHUNK, CHUNK)
        p = s_ref[:, cols]
        ds = (p * (dp_ref[:, cols] - inner)).astype(jnp.bfloat16)
        dkt_ref[0, :, cols] += jnp.dot(qts, ds, preferred_element_type=jnp.float32)
        dvt_ref[0, :, cols] += jnp.dot(dot_, p.astype(jnp.bfloat16), preferred_element_type=jnp.float32)
        return dq + jnp.dot(ds, k_ref[0, cols, :], preferred_element_type=jnp.float32)

    dq = lax.fori_loop(lo, hi, fourth, jnp.zeros((tq, q_ref.shape[2]), jnp.float32))
    dq_ref[0] = dq * 0.125


def attention_forward(q, k, v, seg, lo):
    heads, length, head = q.shape
    tq = min(QBLOCK, length)
    rows = pl.BlockSpec((1, tq, head), lambda h, i, lo: (h, i, 0))
    whole = pl.BlockSpec((1, length, head), lambda h, i, lo: (h, 0, 0))
    wide = pl.BlockSpec((1, head, length), lambda h, i, lo: (h, 0, 0))
    segq = pl.BlockSpec((tq, 1), lambda h, i, lo: (i, 0))
    segk = pl.BlockSpec((1, length), lambda h, i, lo: (0, 0))
    return pl.pallas_call(
        _fwd_kernel,
        out_shape=jax.ShapeDtypeStruct((heads, length, head), jnp.float32),
        grid_spec=pltpu.PrefetchScalarGridSpec(
            num_scalar_prefetch=1,
            grid=(heads, length // tq),
            in_specs=[rows, wide, whole, segq, segk],
            out_specs=rows,
            scratch_shapes=[pltpu.VMEM((tq, length), jnp.float32)],
        ),
        compiler_params=pltpu.CompilerParams(dimension_semantics=("arbitrary", "arbitrary")),
        cost_estimate=pl.CostEstimate(
            flops=2 * heads * length * length * head,
            transcendentals=heads * length * length // 2,
            bytes_accessed=4 * heads * length * head * 2,
        ),
    )(lo, q, k.transpose(0, 2, 1), v, seg[:, None], seg[None, :])


def attention_backward(q, k, v, do, seg, lo):
    heads, length, head = q.shape
    tq = min(QBLOCK, length)
    rows = pl.BlockSpec((1, tq, head), lambda h, i, lo: (h, i, 0))
    rows_t = pl.BlockSpec((1, head, tq), lambda h, i, lo: (h, 0, i))
    whole = pl.BlockSpec((1, length, head), lambda h, i, lo: (h, 0, 0))
    wide = pl.BlockSpec((1, head, length), lambda h, i, lo: (h, 0, 0))
    segq = pl.BlockSpec((tq, 1), lambda h, i, lo: (i, 0))
    segk = pl.BlockSpec((1, length), lambda h, i, lo: (0, 0))
    dq, dkt, dvt = pl.pallas_call(
        _bwd_kernel,
        out_shape=(
            jax.ShapeDtypeStruct((heads, length, head), jnp.float32),
            jax.ShapeDtypeStruct((heads, head, length), jnp.float32),
            jax.ShapeDtypeStruct((heads, head, length), jnp.float32),
        ),
        grid_spec=pltpu.PrefetchScalarGridSpec(
            num_scalar_prefetch=1,
            grid=(heads, length // tq),
            in_specs=[rows, rows_t, whole, wide, wide, rows, rows_t, segq, segk],
            out_specs=(rows, wide, wide),
            scratch_shapes=[pltpu.VMEM((tq, length), jnp.float32), pltpu.VMEM((tq, length), jnp.float32)],
        ),
        compiler_params=pltpu.CompilerParams(dimension_semantics=("arbitrary", "arbitrary")),
        cost_estimate=pl.CostEstimate(
            flops=5 * heads * length * length * head,
            transcendentals=heads * length * length // 2,
            bytes_accessed=8 * heads * length * head * 2,
        ),
    )(lo, q, q.transpose(0, 2, 1), k, k.transpose(0, 2, 1), v.transpose(0, 2, 1), do, do.transpose(0, 2, 1), seg[:, None], seg[None, :])
    return dq, dkt.transpose(0, 2, 1), dvt.transpose(0, 2, 1)


def block_starts(seg, lengths, tq):
    ends = jnp.cumsum(lengths)
    starts = jnp.concatenate([jnp.zeros((1,), ends.dtype), ends[:-1]])
    first_seg = seg[::tq]
    return (starts[first_seg] // CHUNK).astype(jnp.int32)


def heads_major(block):
    return block.reshape(block.shape[0], HEADS, HEAD).transpose(1, 0, 2)


def tokens_major(block):
    return block.transpose(1, 0, 2).reshape(block.shape[1], HEADS * HEAD)


def norm_apply(values, gain, shift):
    average = jnp.mean(values, axis=-1, keepdims=True)
    centered = values - average
    inv_scale = lax.rsqrt(jnp.mean(centered * centered, axis=-1, keepdims=True) + EPSILON)
    unit = centered * inv_scale
    return (unit * gain + shift, unit, inv_scale)


def norm_back(unit, inv_scale, gain, grad):
    scaled = grad * gain
    back = inv_scale * (
        scaled
        - jnp.mean(scaled, axis=-1, keepdims=True)
        - unit * jnp.mean(scaled * unit, axis=-1, keepdims=True)
    )
    return (back, jnp.sum(grad * unit, axis=0), jnp.sum(grad, axis=0))


def gelu_exact(values):
    return jax.nn.gelu(values, approximate=False)


def segment_ids(lengths_row, length):
    ends = jnp.cumsum(lengths_row)
    places = jnp.arange(length, dtype=jnp.int32)
    return jnp.sum((places[:, None] >= ends[None, :]).astype(jnp.int32), axis=1)


def pack_columns(parts, rows):
    cols = [p.reshape(rows, -1) for p in parts]
    width = sum(c.shape[1] for c in cols)
    pad = (-width) % 128
    if pad:
        cols.append(jnp.zeros((rows, pad), cols[0].dtype))
    return jnp.concatenate(cols, axis=1)


def unpack_columns(block, widths):
    out = []
    offset = 0
    for w in widths:
        out.append(block[:, offset : offset + w].reshape(-1))
        offset += w
    return out


def destination_order(x, group_size, shard_size, axis):
    shape = x.shape
    lead, size, rest = shape[:axis], shape[axis], shape[axis + 1 :]
    blocks = x.reshape(lead + (shard_size, group_size, size // (group_size * shard_size)) + rest)
    moved = jnp.swapaxes(blocks, len(lead), len(lead) + 1)
    return moved.reshape(shape)


def grad_rows_reduce(packed):
    return lax.psum_scatter(
        packed, ("group", "shard"), scatter_dimension=0, tiled=True
    )


def hypercube_orders(group_size, shard_size):
    gbits = [("group", b) for b in range(group_size.bit_length() - 1)]
    sbits = [("shard", b) for b in range(shard_size.bit_length() - 1)]
    first = gbits[:-1] + sbits + gbits[-1:]
    second = list(first)
    if len(gbits) >= 3:
        second[1], second[2] = first[2], first[1]
    return first, second


def hypercube_reduce_scatter(x, order, group_size, shard_size):
    total = group_size * shard_size
    levels = total.bit_length() - 1
    rows, cols = x.shape
    n = rows // total
    sbits = shard_size.bit_length() - 1

    def k_bit(axis, b):
        return b if axis == "shard" else sbits + b

    axes = [levels - 1 - k_bit(axis, b) for axis, b in order]
    cur = (
        x.reshape([2] * levels + [n, cols])
        .transpose(axes + [levels, levels + 1])
        .reshape(rows, cols)
    )
    for axis, b in order:
        size = group_size if axis == "group" else shard_size
        half = cur.shape[0] // 2
        mine = (lax.axis_index(axis) >> b) & 1
        low, high = cur[:half], cur[half:]
        keep = jnp.where(mine == 1, high, low)
        send = jnp.where(mine == 1, low, high).astype(jnp.bfloat16)
        got = lax.ppermute(send, axis, [(j, j ^ (1 << b)) for j in range(size)])
        cur = keep + got.astype(jnp.float32)
    return cur


def per_device(
    tokens,
    doc_lengths,
    first_gain,
    first_shift,
    qkv_weight,
    query_bias,
    value_bias,
    inner_gain,
    inner_shift,
    proj_weight,
    proj_bias,
    second_gain,
    second_shift,
    expand_weight,
    expand_bias,
    hidden_gain,
    hidden_shift,
    shrink_weight,
    shrink_bias,
    out_cotangent,
):
    group_size = lax.axis_size("group")
    shard_size = lax.axis_size("shard")
    n = qkv_weight.shape[0]
    model_width = n * group_size * shard_size
    wide_width = expand_weight.shape[1]
    ratio = wide_width // model_width
    qkv_width = qkv_weight.shape[1]

    small_parts = (
        first_gain,
        first_shift,
        query_bias,
        value_bias,
        inner_gain,
        inner_shift,
        proj_bias,
        second_gain,
        second_shift,
        shrink_bias,
        expand_bias,
        hidden_gain,
        hidden_shift,
    )
    small_widths = [p.shape[0] // n for p in small_parts]
    first_pack = jnp.concatenate([qkv_weight, pack_columns(small_parts, n)], axis=1)
    first_full = lax.all_gather(first_pack, ("group", "shard"), axis=0, tiled=True)
    qkv_full = first_full[:, :qkv_width]
    (
        gain_one,
        shift_one,
        qbias_full,
        vbias_full,
        gain_inner,
        shift_inner,
        pbias_full,
        gain_three,
        shift_three,
        sbias_full,
        ebias_full,
        gain_four,
        shift_four,
    ) = unpack_columns(first_full[:, qkv_width:], small_widths)
    second_pack = jnp.concatenate([proj_weight, expand_weight], axis=1)
    second_full = lax.all_gather(second_pack, ("group", "shard"), axis=0, tiled=True)
    proj_full = second_full[:, :model_width]
    expand_full = second_full[:, model_width:]
    shrink_full = lax.all_gather(shrink_weight, ("group", "shard"), axis=0, tiled=True)

    row_count = doc_lengths.shape[0]
    length = tokens.shape[0] // row_count
    inputs = tokens.astype(jnp.float32)
    normed, unit_one, inv_one = norm_apply(
        inputs, gain_one.astype(jnp.float32), shift_one.astype(jnp.float32)
    )
    normed_low = normed.astype(jnp.bfloat16)
    bias_cat = jnp.concatenate([qbias_full, jnp.zeros_like(qbias_full), vbias_full]).astype(
        jnp.float32
    )
    qkv_low = (jnp.dot(normed_low, qkv_full, preferred_element_type=jnp.float32) + bias_cat).astype(
        jnp.bfloat16
    )
    segments = jax.vmap(functools.partial(segment_ids, length=length))(doc_lengths).astype(
        jnp.int32
    )
    tq = min(QBLOCK, length)
    row_heads = []
    row_starts = []
    attended_rows = []
    for r in range(row_count):
        piece = qkv_low[r * length : (r + 1) * length]
        heads = tuple(
            heads_major(piece[:, j * model_width : (j + 1) * model_width]) for j in range(3)
        )
        lo = block_starts(segments[r], doc_lengths[r], tq)
        row_heads.append(heads)
        row_starts.append(lo)
        attended_rows.append(tokens_major(attention_forward(*heads, segments[r], lo)))
    attended = jnp.concatenate(attended_rows, axis=0)
    inner, unit_two, inv_two = norm_apply(
        attended, gain_inner.astype(jnp.float32), shift_inner.astype(jnp.float32)
    )
    inner_low = inner.astype(jnp.bfloat16)
    middle = (
        inputs
        + jnp.dot(inner_low, proj_full, preferred_element_type=jnp.float32)
        + pbias_full.astype(jnp.float32)
    )
    second, unit_three, inv_three = norm_apply(
        middle, gain_three.astype(jnp.float32), shift_three.astype(jnp.float32)
    )
    second_low = second.astype(jnp.bfloat16)
    pre_act = jnp.dot(
        second_low, expand_full, preferred_element_type=jnp.float32
    ) + ebias_full.astype(jnp.float32)
    activ, gelu_pull = jax.vjp(gelu_exact, pre_act)
    hidden, unit_four, inv_four = norm_apply(
        activ, gain_four.astype(jnp.float32), shift_four.astype(jnp.float32)
    )
    hidden_low = hidden.astype(jnp.bfloat16)
    output = (
        middle
        + jnp.dot(hidden_low, shrink_full, preferred_element_type=jnp.float32)
        + sbias_full.astype(jnp.float32)
    )
    block_output = output.astype(jnp.bfloat16)
    grad_out = out_cotangent.astype(jnp.float32)
    shrink_weight_grad = jnp.einsum(
        "tf,td->fd",
        destination_order(hidden_low, group_size, shard_size, 1),
        out_cotangent,
        preferred_element_type=jnp.float32,
    )
    shrink_bias_grad = jnp.sum(grad_out, axis=0)
    grad_hidden = jnp.einsum(
        "td,fd->tf", out_cotangent, shrink_full, preferred_element_type=jnp.float32
    )
    grad_activ, hidden_gain_grad, hidden_shift_grad = norm_back(
        unit_four, inv_four, gain_four.astype(jnp.float32), grad_hidden
    )
    grad_pre = gelu_pull(grad_activ)[0].astype(jnp.bfloat16)
    expand_bias_grad = jnp.sum(grad_pre.astype(jnp.float32), axis=0)
    expand_weight_grad = jnp.einsum(
        "td,tf->df",
        destination_order(second_low, group_size, shard_size, 1),
        grad_pre,
        preferred_element_type=jnp.float32,
    )
    grad_second = jnp.einsum("tf,df->td", grad_pre, expand_full, preferred_element_type=jnp.float32)
    grad_mid_part, second_gain_grad, second_shift_grad = norm_back(
        unit_three, inv_three, gain_three.astype(jnp.float32), grad_second
    )
    grad_middle = grad_out + grad_mid_part
    order_a, order_b = hypercube_orders(group_size, shard_size)
    grad_branch = grad_middle.astype(jnp.bfloat16)
    proj_bias_grad = jnp.sum(grad_branch.astype(jnp.float32), axis=0)
    proj_weight_grad = jnp.einsum(
        "td,te->de",
        destination_order(inner_low, group_size, shard_size, 1),
        grad_branch,
        preferred_element_type=jnp.float32,
    )
    grad_inner = jnp.einsum("te,de->td", grad_branch, proj_full, preferred_element_type=jnp.float32)
    grad_attended, inner_gain_grad, inner_shift_grad = norm_back(
        unit_two, inv_two, gain_inner.astype(jnp.float32), grad_inner
    )
    ffn_small = (
        second_gain_grad,
        second_shift_grad,
        shrink_bias_grad,
        expand_bias_grad,
        hidden_gain_grad,
        hidden_shift_grad,
        inner_gain_grad,
        inner_shift_grad,
        proj_bias_grad,
    )
    ffn_small_widths = [p.shape[0] // model_width for p in ffn_small]
    ffn_pack = jnp.concatenate(
        [
            expand_weight_grad,
            shrink_weight_grad.reshape(model_width, ratio * model_width),
            proj_weight_grad,
            destination_order(pack_columns(ffn_small, model_width), group_size, shard_size, 0),
        ],
        axis=1,
    ).astype(jnp.bfloat16)
    grad_att_low = grad_attended.astype(jnp.bfloat16)
    ffn_pack, grad_att_low = lax.optimization_barrier((ffn_pack, grad_att_low))
    ffn_part = grad_rows_reduce(ffn_pack)
    grad_rows = []
    for r in range(row_count):
        parts = attention_backward(
            *row_heads[r],
            heads_major(grad_att_low[r * length : (r + 1) * length]),
            segments[r],
            row_starts[r],
        )
        grad_rows.append(jnp.concatenate([tokens_major(p) for p in parts], axis=1))
    grad_qkv = jnp.concatenate(grad_rows, axis=0).astype(jnp.bfloat16)
    grad_qkv_wide = grad_qkv.astype(jnp.float32)
    query_bias_grad = jnp.sum(grad_qkv_wide[:, :model_width], axis=0)
    value_bias_grad = jnp.sum(grad_qkv_wide[:, 2 * model_width :], axis=0)
    qkv_weight_grad = jnp.einsum(
        "td,te->de",
        destination_order(normed_low, group_size, shard_size, 1),
        grad_qkv,
        preferred_element_type=jnp.float32,
    )
    grad_normed = jnp.einsum("te,de->td", grad_qkv, qkv_full, preferred_element_type=jnp.float32)
    grad_in_part, first_gain_grad, first_shift_grad = norm_back(
        unit_one, inv_one, gain_one.astype(jnp.float32), grad_normed
    )
    input_grad = (grad_middle + grad_in_part).astype(jnp.bfloat16)
    attn_small = (
        first_gain_grad,
        first_shift_grad,
        query_bias_grad,
        value_bias_grad,
    )
    attn_pack = jnp.concatenate(
        [
            qkv_weight_grad,
            destination_order(pack_columns(attn_small, model_width), group_size, shard_size, 0),
        ],
        axis=1,
    )
    ffn_part, attn_pack = lax.optimization_barrier((ffn_part, attn_pack))
    split = (attn_pack.shape[1] // 256) * 128
    attn_left = hypercube_reduce_scatter(
        attn_pack[:, :split], order_a, group_size, shard_size
    )
    attn_right = hypercube_reduce_scatter(
        attn_pack[:, split:], order_b, group_size, shard_size
    )
    both = lax.all_gather(
        jnp.concatenate(
            [
                ffn_part,
                attn_left.astype(jnp.bfloat16),
                attn_right.astype(jnp.bfloat16),
            ],
            axis=1,
        ),
        "group",
        axis=0,
        tiled=True,
    ).astype(jnp.float32)
    ffn_cols = ffn_pack.shape[1]
    ffn_back = both[:, :ffn_cols]
    attn_back = both[:, ffn_cols:]
    half = both.shape[0]
    expand_out = ffn_back[:, :wide_width]
    shrink_out = ffn_back[:, wide_width : 2 * wide_width].reshape(half * ratio, model_width)
    proj_out = ffn_back[:, 2 * wide_width : 2 * wide_width + model_width]
    (
        second_gain_out,
        second_shift_out,
        sbias_out,
        ebias_out,
        gain_four_out,
        shift_four_out,
        gain_inner_out,
        shift_inner_out,
        pbias_out,
    ) = unpack_columns(ffn_back[:, 2 * wide_width + model_width :], ffn_small_widths)
    qkv_out = attn_back[:, :qkv_width]
    (
        gain_one_out,
        shift_one_out,
        qbias_out,
        vbias_out,
    ) = unpack_columns(attn_back[:, qkv_width:], [1] * 4)
    return (
        block_output,
        input_grad,
        gain_one_out,
        shift_one_out,
        qkv_out,
        qbias_out,
        vbias_out,
        gain_inner_out,
        shift_inner_out,
        proj_out,
        pbias_out,
        second_gain_out,
        second_shift_out,
        expand_out,
        ebias_out,
        gain_four_out,
        shift_four_out,
        shrink_out,
        sbias_out,
    )


def solution(mesh):
    in_specs = (
        P(("group", "shard"), None),
        P(("group", "shard"), None),
        P(("group", "shard")),
        P(("group", "shard")),
        P(("group", "shard"), None),
        P(("group", "shard")),
        P(("group", "shard")),
        P(("group", "shard")),
        P(("group", "shard")),
        P(("group", "shard"), None),
        P(("group", "shard")),
        P(("group", "shard")),
        P(("group", "shard")),
        P(("group", "shard"), None),
        P(("group", "shard")),
        P(("group", "shard")),
        P(("group", "shard")),
        P(("group", "shard"), None),
        P(("group", "shard")),
        P(("group", "shard"), None),
    )
    out_specs = (
        P(("group", "shard"), None),
        P(("group", "shard"), None),
        P("shard"),
        P("shard"),
        P("shard", None),
        P("shard"),
        P("shard"),
        P("shard"),
        P("shard"),
        P("shard", None),
        P("shard"),
        P("shard"),
        P("shard"),
        P("shard", None),
        P("shard"),
        P("shard"),
        P("shard"),
        P("shard", None),
        P("shard"),
    )

    return jax.shard_map(
        per_device, mesh=mesh, in_specs=in_specs, out_specs=out_specs, check_vma=False
    )
```

```python
import functools

import jax
import jax.numpy as jnp
from jax import lax
from jax.experimental import pallas as pl
from jax.experimental.pallas import tpu as pltpu
from jax.sharding import PartitionSpec as P


HEADS = 12
HEAD = 64
NSEG = 5


EPSILON = 1e-05


MASKED = -1000000000.0

CHUNK = 128
QBLOCK = 512


def _row_setup(segq_ref, i, tq):
    segq = segq_ref[...]
    own = jnp.broadcast_to(jnp.where(segq < NSEG - 1, segq, -1), (tq, CHUNK))
    rel = (i * tq + lax.broadcasted_iota(jnp.int32, (tq, CHUNK), 0)) - lax.broadcasted_iota(
        jnp.int32, (tq, CHUNK), 1
    )
    keep = (segq < NSEG - 1).astype(jnp.float32)
    return own, rel, keep


def _softmax_rows(q, kt_ref, own, rel, segk_ref, lo, hi, s_ref):
    tq = q.shape[0]

    def first(c, top):
        kc = kt_ref[0, :, pl.ds(c * CHUNK, CHUNK)]
        s = jnp.dot(q, kc, preferred_element_type=jnp.float32)
        allowed = (own == segk_ref[:, pl.ds(c * CHUNK, CHUNK)]) & (rel >= c * CHUNK)
        s = jnp.where(allowed, s, MASKED)
        s_ref[:, pl.ds(c * CHUNK, CHUNK)] = s
        return jnp.maximum(top, s)

    top = lax.fori_loop(lo, hi, first, jnp.full((tq, CHUNK), MASKED, jnp.float32))
    peak = jnp.broadcast_to(jnp.max(top, axis=1, keepdims=True), (tq, CHUNK))

    def second(c, acc):
        e = jnp.exp(s_ref[:, pl.ds(c * CHUNK, CHUNK)] - peak)
        s_ref[:, pl.ds(c * CHUNK, CHUNK)] = e
        return acc + e

    acc = lax.fori_loop(lo, hi, second, jnp.zeros((tq, CHUNK), jnp.float32))
    return jnp.sum(acc, axis=1, keepdims=True)


def _fwd_kernel(lo_ref, q_ref, kt_ref, v_ref, segq_ref, segk_ref, o_ref, s_ref):
    i = pl.program_id(1)
    tq = q_ref.shape[1]
    q = q_ref[0] * jnp.asarray(0.125, q_ref.dtype)
    own, rel, keep = _row_setup(segq_ref, i, tq)
    lo = lo_ref[i]
    hi = (i + 1) * (tq // CHUNK)
    total = _softmax_rows(q, kt_ref, own, rel, segk_ref, lo, hi, s_ref)
    scale = jnp.broadcast_to(keep / total, (tq, CHUNK))

    def third(c, acc):
        p = (s_ref[:, pl.ds(c * CHUNK, CHUNK)] * scale).astype(jnp.bfloat16)
        vc = v_ref[0, pl.ds(c * CHUNK, CHUNK), :]
        return acc + jnp.dot(p, vc, preferred_element_type=jnp.float32)

    o_ref[0] = lax.fori_loop(lo, hi, third, jnp.zeros((tq, q.shape[1]), jnp.float32))


def _bwd_kernel(lo_ref, q_ref, qt_ref, k_ref, kt_ref, vt_ref, do_ref, dot_ref, segq_ref, segk_ref,
                dq_ref, dkt_ref, dvt_ref, s_ref, dp_ref):
    i = pl.program_id(1)
    tq = q_ref.shape[1]

    @pl.when(i == 0)
    def _():
        dkt_ref[...] = jnp.zeros_like(dkt_ref)
        dvt_ref[...] = jnp.zeros_like(dvt_ref)

    eighth = jnp.asarray(0.125, q_ref.dtype)
    qs = q_ref[0] * eighth
    qts = qt_ref[0] * eighth
    do = do_ref[0]
    dot_ = dot_ref[0]
    own, rel, keep = _row_setup(segq_ref, i, tq)
    lo = lo_ref[i]
    hi = (i + 1) * (tq // CHUNK)
    total = _softmax_rows(qs, kt_ref, own, rel, segk_ref, lo, hi, s_ref)
    scale = jnp.broadcast_to(keep / total, (tq, CHUNK))

    def third(c, acc):
        p = s_ref[:, pl.ds(c * CHUNK, CHUNK)] * scale
        dp = jnp.dot(do, vt_ref[0, :, pl.ds(c * CHUNK, CHUNK)], preferred_element_type=jnp.float32)
        s_ref[:, pl.ds(c * CHUNK, CHUNK)] = p
        dp_ref[:, pl.ds(c * CHUNK, CHUNK)] = dp
        return acc + p * dp

    acc = lax.fori_loop(lo, hi, third, jnp.zeros((tq, CHUNK), jnp.float32))
    inner = jnp.broadcast_to(jnp.sum(acc, axis=1, keepdims=True), (tq, CHUNK))

    def fourth(c, dq):
        cols = pl.ds(c * CHUNK, CHUNK)
        p = s_ref[:, cols]
        ds = (p * (dp_ref[:, cols] - inner)).astype(jnp.bfloat16)
        dkt_ref[0, :, cols] += jnp.dot(qts, ds, preferred_element_type=jnp.float32)
        dvt_ref[0, :, cols] += jnp.dot(dot_, p.astype(jnp.bfloat16), preferred_element_type=jnp.float32)
        return dq + jnp.dot(ds, k_ref[0, cols, :], preferred_element_type=jnp.float32)

    dq = lax.fori_loop(lo, hi, fourth, jnp.zeros((tq, q_ref.shape[2]), jnp.float32))
    dq_ref[0] = dq * 0.125


def attention_forward(q, k, v, seg, lo):
    heads, length, head = q.shape
    tq = min(QBLOCK, length)
    rows = pl.BlockSpec((1, tq, head), lambda h, i, lo: (h, i, 0))
    whole = pl.BlockSpec((1, length, head), lambda h, i, lo: (h, 0, 0))
    wide = pl.BlockSpec((1, head, length), lambda h, i, lo: (h, 0, 0))
    segq = pl.BlockSpec((tq, 1), lambda h, i, lo: (i, 0))
    segk = pl.BlockSpec((1, length), lambda h, i, lo: (0, 0))
    return pl.pallas_call(
        _fwd_kernel,
        out_shape=jax.ShapeDtypeStruct((heads, length, head), jnp.float32),
        grid_spec=pltpu.PrefetchScalarGridSpec(
            num_scalar_prefetch=1,
            grid=(heads, length // tq),
            in_specs=[rows, wide, whole, segq, segk],
            out_specs=rows,
            scratch_shapes=[pltpu.VMEM((tq, length), jnp.float32)],
        ),
        compiler_params=pltpu.CompilerParams(dimension_semantics=("arbitrary", "arbitrary")),
        cost_estimate=pl.CostEstimate(
            flops=2 * heads * length * length * head,
            transcendentals=heads * length * length // 2,
            bytes_accessed=4 * heads * length * head * 2,
        ),
    )(lo, q, k.transpose(0, 2, 1), v, seg[:, None], seg[None, :])


def attention_backward(q, k, v, do, seg, lo):
    heads, length, head = q.shape
    tq = min(QBLOCK, length)
    rows = pl.BlockSpec((1, tq, head), lambda h, i, lo: (h, i, 0))
    rows_t = pl.BlockSpec((1, head, tq), lambda h, i, lo: (h, 0, i))
    whole = pl.BlockSpec((1, length, head), lambda h, i, lo: (h, 0, 0))
    wide = pl.BlockSpec((1, head, length), lambda h, i, lo: (h, 0, 0))
    segq = pl.BlockSpec((tq, 1), lambda h, i, lo: (i, 0))
    segk = pl.BlockSpec((1, length), lambda h, i, lo: (0, 0))
    dq, dkt, dvt = pl.pallas_call(
        _bwd_kernel,
        out_shape=(
            jax.ShapeDtypeStruct((heads, length, head), jnp.float32),
            jax.ShapeDtypeStruct((heads, head, length), jnp.float32),
            jax.ShapeDtypeStruct((heads, head, length), jnp.float32),
        ),
        grid_spec=pltpu.PrefetchScalarGridSpec(
            num_scalar_prefetch=1,
            grid=(heads, length // tq),
            in_specs=[rows, rows_t, whole, wide, wide, rows, rows_t, segq, segk],
            out_specs=(rows, wide, wide),
            scratch_shapes=[pltpu.VMEM((tq, length), jnp.float32), pltpu.VMEM((tq, length), jnp.float32)],
        ),
        compiler_params=pltpu.CompilerParams(dimension_semantics=("arbitrary", "arbitrary")),
        cost_estimate=pl.CostEstimate(
            flops=5 * heads * length * length * head,
            transcendentals=heads * length * length // 2,
            bytes_accessed=8 * heads * length * head * 2,
        ),
    )(lo, q, q.transpose(0, 2, 1), k, k.transpose(0, 2, 1), v.transpose(0, 2, 1), do, do.transpose(0, 2, 1), seg[:, None], seg[None, :])
    return dq, dkt.transpose(0, 2, 1), dvt.transpose(0, 2, 1)


def block_starts(seg, lengths, tq):
    ends = jnp.cumsum(lengths)
    starts = jnp.concatenate([jnp.zeros((1,), ends.dtype), ends[:-1]])
    first_seg = seg[::tq]
    return (starts[first_seg] // CHUNK).astype(jnp.int32)


def heads_major(block):
    return block.reshape(block.shape[0], HEADS, HEAD).transpose(1, 0, 2)


def tokens_major(block):
    return block.transpose(1, 0, 2).reshape(block.shape[1], HEADS * HEAD)


def norm_apply(values, gain, shift):
    average = jnp.mean(values, axis=-1, keepdims=True)
    centered = values - average
    inv_scale = lax.rsqrt(jnp.mean(centered * centered, axis=-1, keepdims=True) + EPSILON)
    unit = centered * inv_scale
    return (unit * gain + shift, unit, inv_scale)


def norm_back(unit, inv_scale, gain, grad):
    scaled = grad * gain
    back = inv_scale * (
        scaled
        - jnp.mean(scaled, axis=-1, keepdims=True)
        - unit * jnp.mean(scaled * unit, axis=-1, keepdims=True)
    )
    return (back, jnp.sum(grad * unit, axis=0), jnp.sum(grad, axis=0))


def gelu_exact(values):
    return jax.nn.gelu(values, approximate=False)


def segment_ids(lengths_row, length):
    ends = jnp.cumsum(lengths_row)
    places = jnp.arange(length, dtype=jnp.int32)
    return jnp.sum((places[:, None] >= ends[None, :]).astype(jnp.int32), axis=1)


def pack_columns(parts, rows):
    cols = [p.reshape(rows, -1) for p in parts]
    width = sum(c.shape[1] for c in cols)
    pad = (-width) % 128
    if pad:
        cols.append(jnp.zeros((rows, pad), cols[0].dtype))
    return jnp.concatenate(cols, axis=1)


def unpack_columns(block, widths):
    out = []
    offset = 0
    for w in widths:
        out.append(block[:, offset : offset + w].reshape(-1))
        offset += w
    return out


def grad_rows_reduce(packed, group_size, shard_size):
    rows, cols = packed.shape
    n = rows // (group_size * shard_size)
    permuted = (
        packed.reshape(shard_size, group_size, n, cols)
        .transpose(1, 0, 2, 3)
        .reshape(rows, cols)
    )
    return lax.psum_scatter(
        permuted, ("group", "shard"), scatter_dimension=0, tiled=True
    )


def hypercube_orders(group_size, shard_size):
    gbits = [("group", b) for b in range(group_size.bit_length() - 1)]
    sbits = [("shard", b) for b in range(shard_size.bit_length() - 1)]
    first = gbits[:-1] + sbits + gbits[-1:]
    second = list(first)
    if len(gbits) >= 3:
        second[1], second[2] = first[2], first[1]
    return first, second


def hypercube_reduce_scatter(x, order, group_size, shard_size):
    total = group_size * shard_size
    levels = total.bit_length() - 1
    rows, cols = x.shape
    n = rows // total
    sbits = shard_size.bit_length() - 1

    def k_bit(axis, b):
        return b if axis == "shard" else sbits + b

    axes = [levels - 1 - k_bit(axis, b) for axis, b in order]
    cur = (
        x.reshape([2] * levels + [n, cols])
        .transpose(axes + [levels, levels + 1])
        .reshape(rows, cols)
    )
    for axis, b in order:
        size = group_size if axis == "group" else shard_size
        half = cur.shape[0] // 2
        mine = (lax.axis_index(axis) >> b) & 1
        low, high = cur[:half], cur[half:]
        keep = jnp.where(mine == 1, high, low)
        send = jnp.where(mine == 1, low, high).astype(jnp.bfloat16)
        got = lax.ppermute(send, axis, [(j, j ^ (1 << b)) for j in range(size)])
        cur = keep + got.astype(jnp.float32)
    return cur


def per_device(
    tokens,
    doc_lengths,
    first_gain,
    first_shift,
    qkv_weight,
    query_bias,
    value_bias,
    inner_gain,
    inner_shift,
    proj_weight,
    proj_bias,
    second_gain,
    second_shift,
    expand_weight,
    expand_bias,
    hidden_gain,
    hidden_shift,
    shrink_weight,
    shrink_bias,
    out_cotangent,
):
    group_size = lax.axis_size("group")
    shard_size = lax.axis_size("shard")
    n = qkv_weight.shape[0]
    model_width = n * group_size * shard_size
    wide_width = expand_weight.shape[1]
    ratio = wide_width // model_width
    qkv_width = qkv_weight.shape[1]

    small_parts = (
        first_gain,
        first_shift,
        query_bias,
        value_bias,
        inner_gain,
        inner_shift,
        proj_bias,
        second_gain,
        second_shift,
        shrink_bias,
        expand_bias,
        hidden_gain,
        hidden_shift,
    )
    small_widths = [p.shape[0] // n for p in small_parts]
    first_pack = jnp.concatenate([qkv_weight, pack_columns(small_parts, n)], axis=1)
    first_full = lax.all_gather(first_pack, ("group", "shard"), axis=0, tiled=True)
    qkv_full = first_full[:, :qkv_width]
    (
        gain_one,
        shift_one,
        qbias_full,
        vbias_full,
        gain_inner,
        shift_inner,
        pbias_full,
        gain_three,
        shift_three,
        sbias_full,
        ebias_full,
        gain_four,
        shift_four,
    ) = unpack_columns(first_full[:, qkv_width:], small_widths)
    second_pack = jnp.concatenate([proj_weight, expand_weight], axis=1)
    second_full = lax.all_gather(second_pack, ("group", "shard"), axis=0, tiled=True)
    proj_full = second_full[:, :model_width]
    expand_full = second_full[:, model_width:]
    shrink_full = lax.all_gather(shrink_weight, ("group", "shard"), axis=0, tiled=True)

    row_count = doc_lengths.shape[0]
    length = tokens.shape[0] // row_count
    inputs = tokens.astype(jnp.float32)
    normed, unit_one, inv_one = norm_apply(
        inputs, gain_one.astype(jnp.float32), shift_one.astype(jnp.float32)
    )
    normed_low = normed.astype(jnp.bfloat16)
    bias_cat = jnp.concatenate([qbias_full, jnp.zeros_like(qbias_full), vbias_full]).astype(
        jnp.float32
    )
    qkv_low = (jnp.dot(normed_low, qkv_full, preferred_element_type=jnp.float32) + bias_cat).astype(
        jnp.bfloat16
    )
    segments = jax.vmap(functools.partial(segment_ids, length=length))(doc_lengths).astype(
        jnp.int32
    )
    tq = min(QBLOCK, length)
    row_heads = []
    row_starts = []
    attended_rows = []
    for r in range(row_count):
        piece = qkv_low[r * length : (r + 1) * length]
        heads = tuple(
            heads_major(piece[:, j * model_width : (j + 1) * model_width]) for j in range(3)
        )
        lo = block_starts(segments[r], doc_lengths[r], tq)
        row_heads.append(heads)
        row_starts.append(lo)
        attended_rows.append(tokens_major(attention_forward(*heads, segments[r], lo)))
    attended = jnp.concatenate(attended_rows, axis=0)
    inner, unit_two, inv_two = norm_apply(
        attended, gain_inner.astype(jnp.float32), shift_inner.astype(jnp.float32)
    )
    inner_low = inner.astype(jnp.bfloat16)
    middle = (
        inputs
        + jnp.dot(inner_low, proj_full, preferred_element_type=jnp.float32)
        + pbias_full.astype(jnp.float32)
    )
    second, unit_three, inv_three = norm_apply(
        middle, gain_three.astype(jnp.float32), shift_three.astype(jnp.float32)
    )
    second_low = second.astype(jnp.bfloat16)
    pre_act = jnp.dot(
        second_low, expand_full, preferred_element_type=jnp.float32
    ) + ebias_full.astype(jnp.float32)
    activ, gelu_pull = jax.vjp(gelu_exact, pre_act)
    hidden, unit_four, inv_four = norm_apply(
        activ, gain_four.astype(jnp.float32), shift_four.astype(jnp.float32)
    )
    hidden_low = hidden.astype(jnp.bfloat16)
    output = (
        middle
        + jnp.dot(hidden_low, shrink_full, preferred_element_type=jnp.float32)
        + sbias_full.astype(jnp.float32)
    )
    block_output = output.astype(jnp.bfloat16)
    grad_out = out_cotangent.astype(jnp.float32)
    shrink_weight_grad = jnp.einsum(
        "tf,td->fd", hidden_low, out_cotangent, preferred_element_type=jnp.float32
    )
    shrink_bias_grad = jnp.sum(grad_out, axis=0)
    grad_hidden = jnp.einsum(
        "td,fd->tf", out_cotangent, shrink_full, preferred_element_type=jnp.float32
    )
    grad_activ, hidden_gain_grad, hidden_shift_grad = norm_back(
        unit_four, inv_four, gain_four.astype(jnp.float32), grad_hidden
    )
    grad_pre = gelu_pull(grad_activ)[0].astype(jnp.bfloat16)
    expand_bias_grad = jnp.sum(grad_pre.astype(jnp.float32), axis=0)
    expand_weight_grad = jnp.einsum(
        "td,tf->df", second_low, grad_pre, preferred_element_type=jnp.float32
    )
    grad_second = jnp.einsum("tf,df->td", grad_pre, expand_full, preferred_element_type=jnp.float32)
    grad_mid_part, second_gain_grad, second_shift_grad = norm_back(
        unit_three, inv_three, gain_three.astype(jnp.float32), grad_second
    )
    grad_middle = grad_out + grad_mid_part
    order_a, order_b = hypercube_orders(group_size, shard_size)
    grad_branch = grad_middle.astype(jnp.bfloat16)
    proj_bias_grad = jnp.sum(grad_branch.astype(jnp.float32), axis=0)
    proj_weight_grad = jnp.einsum(
        "td,te->de", inner_low, grad_branch, preferred_element_type=jnp.float32
    )
    grad_inner = jnp.einsum("te,de->td", grad_branch, proj_full, preferred_element_type=jnp.float32)
    grad_attended, inner_gain_grad, inner_shift_grad = norm_back(
        unit_two, inv_two, gain_inner.astype(jnp.float32), grad_inner
    )
    ffn_small = (
        second_gain_grad,
        second_shift_grad,
        shrink_bias_grad,
        expand_bias_grad,
        hidden_gain_grad,
        hidden_shift_grad,
        inner_gain_grad,
        inner_shift_grad,
        proj_bias_grad,
    )
    ffn_small_widths = [p.shape[0] // model_width for p in ffn_small]
    ffn_pack = jnp.concatenate(
        [
            expand_weight_grad,
            shrink_weight_grad.reshape(model_width, ratio * model_width),
            proj_weight_grad,
            pack_columns(ffn_small, model_width),
        ],
        axis=1,
    ).astype(jnp.bfloat16)
    grad_att_low = grad_attended.astype(jnp.bfloat16)
    ffn_pack, grad_att_low = lax.optimization_barrier((ffn_pack, grad_att_low))
    ffn_part = grad_rows_reduce(ffn_pack, group_size, shard_size)
    grad_rows = []
    for r in range(row_count):
        parts = attention_backward(
            *row_heads[r],
            heads_major(grad_att_low[r * length : (r + 1) * length]),
            segments[r],
            row_starts[r],
        )
        grad_rows.append(jnp.concatenate([tokens_major(p) for p in parts], axis=1))
    grad_qkv = jnp.concatenate(grad_rows, axis=0).astype(jnp.bfloat16)
    grad_qkv_wide = grad_qkv.astype(jnp.float32)
    query_bias_grad = jnp.sum(grad_qkv_wide[:, :model_width], axis=0)
    value_bias_grad = jnp.sum(grad_qkv_wide[:, 2 * model_width :], axis=0)
    qkv_weight_grad = jnp.einsum(
        "td,te->de", normed_low, grad_qkv, preferred_element_type=jnp.float32
    )
    grad_normed = jnp.einsum("te,de->td", grad_qkv, qkv_full, preferred_element_type=jnp.float32)
    grad_in_part, first_gain_grad, first_shift_grad = norm_back(
        unit_one, inv_one, gain_one.astype(jnp.float32), grad_normed
    )
    input_grad = (grad_middle + grad_in_part).astype(jnp.bfloat16)
    attn_small = (
        first_gain_grad,
        first_shift_grad,
        query_bias_grad,
        value_bias_grad,
    )
    attn_pack = jnp.concatenate(
        [qkv_weight_grad, pack_columns(attn_small, model_width)], axis=1
    )
    attn_pack = (
        attn_pack.reshape(shard_size, group_size, n, -1)
        .transpose(1, 0, 2, 3)
        .reshape(model_width, -1)
    )
    ffn_part, attn_pack = lax.optimization_barrier((ffn_part, attn_pack))
    split = (attn_pack.shape[1] // 256) * 128
    attn_left = hypercube_reduce_scatter(
        attn_pack[:, :split], order_a, group_size, shard_size
    )
    attn_right = hypercube_reduce_scatter(
        attn_pack[:, split:], order_b, group_size, shard_size
    )
    both = lax.all_gather(
        jnp.concatenate(
            [
                ffn_part,
                attn_left.astype(jnp.bfloat16),
                attn_right.astype(jnp.bfloat16),
            ],
            axis=1,
        ),
        "group",
        axis=0,
        tiled=True,
    )
    ffn_cols = ffn_pack.shape[1]
    ffn_back = both[:, :ffn_cols]
    attn_back = both[:, ffn_cols:]
    half = both.shape[0]
    expand_out = ffn_back[:, :wide_width].astype(jnp.float32)
    shrink_out = (
        ffn_back[:, wide_width : 2 * wide_width]
        .reshape(half * ratio, model_width)
        .astype(jnp.float32)
    )
    proj_out = ffn_back[:, 2 * wide_width : 2 * wide_width + model_width].astype(jnp.float32)
    (
        second_gain_out,
        second_shift_out,
        sbias_out,
        ebias_out,
        gain_four_out,
        shift_four_out,
        gain_inner_out,
        shift_inner_out,
        pbias_out,
    ) = unpack_columns(
        ffn_back[:, 2 * wide_width + model_width :].astype(jnp.float32), ffn_small_widths
    )
    qkv_out = attn_back[:, :qkv_width].astype(jnp.float32)
    (
        gain_one_out,
        shift_one_out,
        qbias_out,
        vbias_out,
    ) = unpack_columns(attn_back[:, qkv_width:].astype(jnp.float32), [1] * 4)
    return (
        block_output,
        input_grad,
        gain_one_out,
        shift_one_out,
        qkv_out,
        qbias_out,
        vbias_out,
        gain_inner_out,
        shift_inner_out,
        proj_out,
        pbias_out,
        second_gain_out,
        second_shift_out,
        expand_out,
        ebias_out,
        gain_four_out,
        shift_four_out,
        shrink_out,
        sbias_out,
    )


def solution(mesh):
    in_specs = (
        P(("group", "shard"), None),
        P(("group", "shard"), None),
        P(("group", "shard")),
        P(("group", "shard")),
        P(("group", "shard"), None),
        P(("group", "shard")),
        P(("group", "shard")),
        P(("group", "shard")),
        P(("group", "shard")),
        P(("group", "shard"), None),
        P(("group", "shard")),
        P(("group", "shard")),
        P(("group", "shard")),
        P(("group", "shard"), None),
        P(("group", "shard")),
        P(("group", "shard")),
        P(("group", "shard")),
        P(("group", "shard"), None),
        P(("group", "shard")),
        P(("group", "shard"), None),
    )
    out_specs = (
        P(("group", "shard"), None),
        P(("group", "shard"), None),
        P("shard"),
        P("shard"),
        P("shard", None),
        P("shard"),
        P("shard"),
        P("shard"),
        P("shard"),
        P("shard", None),
        P("shard"),
        P("shard"),
        P("shard"),
        P("shard", None),
        P("shard"),
        P("shard"),
        P("shard"),
        P("shard", None),
        P("shard"),
    )

    return jax.shard_map(
        per_device, mesh=mesh, in_specs=in_specs, out_specs=out_specs, check_vma=False
    )
```

```python
import functools

import jax
import jax.numpy as jnp
from jax import lax
from jax.experimental import pallas as pl
from jax.experimental.pallas import tpu as pltpu
from jax.sharding import PartitionSpec as P


HEADS = 12
HEAD = 64
NSEG = 5


EPSILON = 1e-05


MASKED = -1000000000.0

CHUNK = 128
QBLOCK = 512


def _row_setup(segq_ref, i, tq):
    segq = segq_ref[...]
    own = jnp.broadcast_to(jnp.where(segq < NSEG - 1, segq, -1), (tq, CHUNK))
    rel = (i * tq + lax.broadcasted_iota(jnp.int32, (tq, CHUNK), 0)) - lax.broadcasted_iota(
        jnp.int32, (tq, CHUNK), 1
    )
    keep = (segq < NSEG - 1).astype(jnp.float32)
    return own, rel, keep


def _softmax_rows(q, kt_ref, own, rel, segk_ref, lo, hi, s_ref):
    tq = q.shape[0]

    def first(c, top):
        kc = kt_ref[0, :, pl.ds(c * CHUNK, CHUNK)]
        s = jnp.dot(q, kc, preferred_element_type=jnp.float32)
        allowed = (own == segk_ref[:, pl.ds(c * CHUNK, CHUNK)]) & (rel >= c * CHUNK)
        s = jnp.where(allowed, s, MASKED)
        s_ref[:, pl.ds(c * CHUNK, CHUNK)] = s
        return jnp.maximum(top, s)

    top = lax.fori_loop(lo, hi, first, jnp.full((tq, CHUNK), MASKED, jnp.float32))
    peak = jnp.broadcast_to(jnp.max(top, axis=1, keepdims=True), (tq, CHUNK))

    def second(c, acc):
        e = jnp.exp(s_ref[:, pl.ds(c * CHUNK, CHUNK)] - peak)
        s_ref[:, pl.ds(c * CHUNK, CHUNK)] = e
        return acc + e

    acc = lax.fori_loop(lo, hi, second, jnp.zeros((tq, CHUNK), jnp.float32))
    return jnp.sum(acc, axis=1, keepdims=True)


def _fwd_kernel(lo_ref, q_ref, kt_ref, v_ref, segq_ref, segk_ref, o_ref, s_ref):
    i = pl.program_id(1)
    tq = q_ref.shape[1]
    q = q_ref[0] * jnp.asarray(0.125, q_ref.dtype)
    own, rel, keep = _row_setup(segq_ref, i, tq)
    lo = lo_ref[i]
    hi = (i + 1) * (tq // CHUNK)
    total = _softmax_rows(q, kt_ref, own, rel, segk_ref, lo, hi, s_ref)
    scale = jnp.broadcast_to(keep / total, (tq, CHUNK))

    def third(c, acc):
        p = (s_ref[:, pl.ds(c * CHUNK, CHUNK)] * scale).astype(jnp.bfloat16)
        vc = v_ref[0, pl.ds(c * CHUNK, CHUNK), :]
        return acc + jnp.dot(p, vc, preferred_element_type=jnp.float32)

    o_ref[0] = lax.fori_loop(lo, hi, third, jnp.zeros((tq, q.shape[1]), jnp.float32))


def _bwd_kernel(lo_ref, q_ref, qt_ref, k_ref, kt_ref, vt_ref, do_ref, dot_ref, segq_ref, segk_ref,
                dq_ref, dkt_ref, dvt_ref, s_ref, dp_ref):
    i = pl.program_id(1)
    tq = q_ref.shape[1]

    @pl.when(i == 0)
    def _():
        dkt_ref[...] = jnp.zeros_like(dkt_ref)
        dvt_ref[...] = jnp.zeros_like(dvt_ref)

    eighth = jnp.asarray(0.125, q_ref.dtype)
    qs = q_ref[0] * eighth
    qts = qt_ref[0] * eighth
    do = do_ref[0]
    dot_ = dot_ref[0]
    own, rel, keep = _row_setup(segq_ref, i, tq)
    lo = lo_ref[i]
    hi = (i + 1) * (tq // CHUNK)
    total = _softmax_rows(qs, kt_ref, own, rel, segk_ref, lo, hi, s_ref)
    scale = jnp.broadcast_to(keep / total, (tq, CHUNK))

    def third(c, acc):
        p = s_ref[:, pl.ds(c * CHUNK, CHUNK)] * scale
        dp = jnp.dot(do, vt_ref[0, :, pl.ds(c * CHUNK, CHUNK)], preferred_element_type=jnp.float32)
        s_ref[:, pl.ds(c * CHUNK, CHUNK)] = p
        dp_ref[:, pl.ds(c * CHUNK, CHUNK)] = dp
        return acc + p * dp

    acc = lax.fori_loop(lo, hi, third, jnp.zeros((tq, CHUNK), jnp.float32))
    inner = jnp.broadcast_to(jnp.sum(acc, axis=1, keepdims=True), (tq, CHUNK))

    def fourth(c, dq):
        cols = pl.ds(c * CHUNK, CHUNK)
        p = s_ref[:, cols]
        ds = (p * (dp_ref[:, cols] - inner)).astype(jnp.bfloat16)
        dkt_ref[0, :, cols] += jnp.dot(qts, ds, preferred_element_type=jnp.float32)
        dvt_ref[0, :, cols] += jnp.dot(dot_, p.astype(jnp.bfloat16), preferred_element_type=jnp.float32)
        return dq + jnp.dot(ds, k_ref[0, cols, :], preferred_element_type=jnp.float32)

    dq = lax.fori_loop(lo, hi, fourth, jnp.zeros((tq, q_ref.shape[2]), jnp.float32))
    dq_ref[0] = dq * 0.125


def attention_forward(q, k, v, seg, lo):
    heads, length, head = q.shape
    tq = min(QBLOCK, length)
    rows = pl.BlockSpec((1, tq, head), lambda h, i, lo: (h, i, 0))
    whole = pl.BlockSpec((1, length, head), lambda h, i, lo: (h, 0, 0))
    wide = pl.BlockSpec((1, head, length), lambda h, i, lo: (h, 0, 0))
    segq = pl.BlockSpec((tq, 1), lambda h, i, lo: (i, 0))
    segk = pl.BlockSpec((1, length), lambda h, i, lo: (0, 0))
    return pl.pallas_call(
        _fwd_kernel,
        out_shape=jax.ShapeDtypeStruct((heads, length, head), jnp.float32),
        grid_spec=pltpu.PrefetchScalarGridSpec(
            num_scalar_prefetch=1,
            grid=(heads, length // tq),
            in_specs=[rows, wide, whole, segq, segk],
            out_specs=rows,
            scratch_shapes=[pltpu.VMEM((tq, length), jnp.float32)],
        ),
        compiler_params=pltpu.CompilerParams(dimension_semantics=("arbitrary", "arbitrary")),
        cost_estimate=pl.CostEstimate(
            flops=2 * heads * length * length * head,
            transcendentals=heads * length * length // 2,
            bytes_accessed=4 * heads * length * head * 2,
        ),
    )(lo, q, k.transpose(0, 2, 1), v, seg[:, None], seg[None, :])


def attention_backward(q, k, v, do, seg, lo):
    heads, length, head = q.shape
    tq = min(QBLOCK, length)
    rows = pl.BlockSpec((1, tq, head), lambda h, i, lo: (h, i, 0))
    rows_t = pl.BlockSpec((1, head, tq), lambda h, i, lo: (h, 0, i))
    whole = pl.BlockSpec((1, length, head), lambda h, i, lo: (h, 0, 0))
    wide = pl.BlockSpec((1, head, length), lambda h, i, lo: (h, 0, 0))
    segq = pl.BlockSpec((tq, 1), lambda h, i, lo: (i, 0))
    segk = pl.BlockSpec((1, length), lambda h, i, lo: (0, 0))
    dq, dkt, dvt = pl.pallas_call(
        _bwd_kernel,
        out_shape=(
            jax.ShapeDtypeStruct((heads, length, head), jnp.float32),
            jax.ShapeDtypeStruct((heads, head, length), jnp.float32),
            jax.ShapeDtypeStruct((heads, head, length), jnp.float32),
        ),
        grid_spec=pltpu.PrefetchScalarGridSpec(
            num_scalar_prefetch=1,
            grid=(heads, length // tq),
            in_specs=[rows, rows_t, whole, wide, wide, rows, rows_t, segq, segk],
            out_specs=(rows, wide, wide),
            scratch_shapes=[pltpu.VMEM((tq, length), jnp.float32), pltpu.VMEM((tq, length), jnp.float32)],
        ),
        compiler_params=pltpu.CompilerParams(dimension_semantics=("arbitrary", "arbitrary")),
        cost_estimate=pl.CostEstimate(
            flops=5 * heads * length * length * head,
            transcendentals=heads * length * length // 2,
            bytes_accessed=8 * heads * length * head * 2,
        ),
    )(lo, q, q.transpose(0, 2, 1), k, k.transpose(0, 2, 1), v.transpose(0, 2, 1), do, do.transpose(0, 2, 1), seg[:, None], seg[None, :])
    return dq, dkt.transpose(0, 2, 1), dvt.transpose(0, 2, 1)


def block_starts(seg, lengths, tq):
    ends = jnp.cumsum(lengths)
    starts = jnp.concatenate([jnp.zeros((1,), ends.dtype), ends[:-1]])
    first_seg = seg[::tq]
    return (starts[first_seg] // CHUNK).astype(jnp.int32)


def heads_major(block):
    return block.reshape(block.shape[0], HEADS, HEAD).transpose(1, 0, 2)


def tokens_major(block):
    return block.transpose(1, 0, 2).reshape(block.shape[1], HEADS * HEAD)


def norm_apply(values, gain, shift):
    average = jnp.mean(values, axis=-1, keepdims=True)
    centered = values - average
    inv_scale = lax.rsqrt(jnp.mean(centered * centered, axis=-1, keepdims=True) + EPSILON)
    unit = centered * inv_scale
    return (unit * gain + shift, unit, inv_scale)


def norm_back(unit, inv_scale, gain, grad):
    scaled = grad * gain
    back = inv_scale * (
        scaled
        - jnp.mean(scaled, axis=-1, keepdims=True)
        - unit * jnp.mean(scaled * unit, axis=-1, keepdims=True)
    )
    return (back, jnp.sum(grad * unit, axis=0), jnp.sum(grad, axis=0))


def gelu_exact(values):
    return jax.nn.gelu(values, approximate=False)


def segment_ids(lengths_row, length):
    ends = jnp.cumsum(lengths_row)
    places = jnp.arange(length, dtype=jnp.int32)
    return jnp.sum((places[:, None] >= ends[None, :]).astype(jnp.int32), axis=1)


def pack_columns(parts, rows):
    cols = [p.reshape(rows, -1) for p in parts]
    width = sum(c.shape[1] for c in cols)
    pad = (-width) % 128
    if pad:
        cols.append(jnp.zeros((rows, pad), cols[0].dtype))
    return jnp.concatenate(cols, axis=1)


def unpack_columns(block, widths):
    out = []
    offset = 0
    for w in widths:
        out.append(block[:, offset : offset + w].reshape(-1))
        offset += w
    return out


def grad_rows_reduce(packed, group_size, shard_size):
    rows, cols = packed.shape
    n = rows // (group_size * shard_size)
    permuted = (
        packed.reshape(shard_size, group_size, n, cols)
        .transpose(1, 0, 2, 3)
        .reshape(rows, cols)
    )
    return lax.psum_scatter(
        permuted, ("group", "shard"), scatter_dimension=0, tiled=True
    )


def hypercube_orders(group_size, shard_size):
    gbits = [("group", b) for b in range(group_size.bit_length() - 1)]
    sbits = [("shard", b) for b in range(shard_size.bit_length() - 1)]
    first = gbits[:-1] + sbits + gbits[-1:]
    second = list(first)
    if len(gbits) >= 3:
        second[1], second[2] = first[2], first[1]
    return first, second


def hypercube_reduce_scatter(x, order, group_size, shard_size):
    total = group_size * shard_size
    levels = total.bit_length() - 1
    rows, cols = x.shape
    n = rows // total
    sbits = shard_size.bit_length() - 1

    def k_bit(axis, b):
        return b if axis == "shard" else sbits + b

    axes = [levels - 1 - k_bit(axis, b) for axis, b in order]
    cur = (
        x.reshape([2] * levels + [n, cols])
        .transpose(axes + [levels, levels + 1])
        .reshape(rows, cols)
    )
    for axis, b in order:
        size = group_size if axis == "group" else shard_size
        half = cur.shape[0] // 2
        mine = (lax.axis_index(axis) >> b) & 1
        low, high = cur[:half], cur[half:]
        keep = jnp.where(mine == 1, high, low)
        send = jnp.where(mine == 1, low, high).astype(jnp.bfloat16)
        got = lax.ppermute(send, axis, [(j, j ^ (1 << b)) for j in range(size)])
        cur = keep + got.astype(jnp.float32)
    return cur


def per_device(
    tokens,
    doc_lengths,
    first_gain,
    first_shift,
    qkv_weight,
    query_bias,
    value_bias,
    inner_gain,
    inner_shift,
    proj_weight,
    proj_bias,
    second_gain,
    second_shift,
    expand_weight,
    expand_bias,
    hidden_gain,
    hidden_shift,
    shrink_weight,
    shrink_bias,
    out_cotangent,
):
    group_size = lax.axis_size("group")
    shard_size = lax.axis_size("shard")
    n = qkv_weight.shape[0]
    model_width = n * group_size * shard_size
    wide_width = expand_weight.shape[1]
    ratio = wide_width // model_width
    qkv_width = qkv_weight.shape[1]

    small_parts = (
        first_gain,
        first_shift,
        query_bias,
        value_bias,
        inner_gain,
        inner_shift,
        proj_bias,
        second_gain,
        second_shift,
        shrink_bias,
        expand_bias,
        hidden_gain,
        hidden_shift,
    )
    small_widths = [p.shape[0] // n for p in small_parts]
    first_pack = jnp.concatenate([qkv_weight, pack_columns(small_parts, n)], axis=1)
    first_full = lax.all_gather(first_pack, ("group", "shard"), axis=0, tiled=True)
    qkv_full = first_full[:, :qkv_width]
    (
        gain_one,
        shift_one,
        qbias_full,
        vbias_full,
        gain_inner,
        shift_inner,
        pbias_full,
        gain_three,
        shift_three,
        sbias_full,
        ebias_full,
        gain_four,
        shift_four,
    ) = unpack_columns(first_full[:, qkv_width:], small_widths)
    second_pack = jnp.concatenate([proj_weight, expand_weight], axis=1)
    second_full = lax.all_gather(second_pack, ("group", "shard"), axis=0, tiled=True)
    proj_full = second_full[:, :model_width]
    expand_full = second_full[:, model_width:]
    shrink_full = lax.all_gather(shrink_weight, ("group", "shard"), axis=0, tiled=True)

    row_count = doc_lengths.shape[0]
    length = tokens.shape[0] // row_count
    inputs = tokens.astype(jnp.float32)
    normed, unit_one, inv_one = norm_apply(
        inputs, gain_one.astype(jnp.float32), shift_one.astype(jnp.float32)
    )
    normed_low = normed.astype(jnp.bfloat16)
    bias_cat = jnp.concatenate([qbias_full, jnp.zeros_like(qbias_full), vbias_full]).astype(
        jnp.float32
    )
    qkv_low = (jnp.dot(normed_low, qkv_full, preferred_element_type=jnp.float32) + bias_cat).astype(
        jnp.bfloat16
    )
    segments = jax.vmap(functools.partial(segment_ids, length=length))(doc_lengths).astype(
        jnp.int32
    )
    tq = min(QBLOCK, length)
    row_heads = []
    row_starts = []
    attended_rows = []
    for r in range(row_count):
        piece = qkv_low[r * length : (r + 1) * length]
        heads = tuple(
            heads_major(piece[:, j * model_width : (j + 1) * model_width]) for j in range(3)
        )
        lo = block_starts(segments[r], doc_lengths[r], tq)
        row_heads.append(heads)
        row_starts.append(lo)
        attended_rows.append(tokens_major(attention_forward(*heads, segments[r], lo)))
    attended = jnp.concatenate(attended_rows, axis=0)
    inner, unit_two, inv_two = norm_apply(
        attended, gain_inner.astype(jnp.float32), shift_inner.astype(jnp.float32)
    )
    inner_low = inner.astype(jnp.bfloat16)
    middle = (
        inputs
        + jnp.dot(inner_low, proj_full, preferred_element_type=jnp.float32)
        + pbias_full.astype(jnp.float32)
    )
    second, unit_three, inv_three = norm_apply(
        middle, gain_three.astype(jnp.float32), shift_three.astype(jnp.float32)
    )
    second_low = second.astype(jnp.bfloat16)
    pre_act = jnp.dot(
        second_low, expand_full, preferred_element_type=jnp.float32
    ) + ebias_full.astype(jnp.float32)
    activ, gelu_pull = jax.vjp(gelu_exact, pre_act)
    hidden, unit_four, inv_four = norm_apply(
        activ, gain_four.astype(jnp.float32), shift_four.astype(jnp.float32)
    )
    hidden_low = hidden.astype(jnp.bfloat16)
    output = (
        middle
        + jnp.dot(hidden_low, shrink_full, preferred_element_type=jnp.float32)
        + sbias_full.astype(jnp.float32)
    )
    block_output = output.astype(jnp.bfloat16)
    grad_out = out_cotangent.astype(jnp.float32)
    shrink_weight_grad = jnp.einsum(
        "tf,td->fd", hidden_low, out_cotangent, preferred_element_type=jnp.float32
    )
    shrink_bias_grad = jnp.sum(grad_out, axis=0)
    grad_hidden = jnp.einsum(
        "td,fd->tf", out_cotangent, shrink_full, preferred_element_type=jnp.float32
    )
    grad_activ, hidden_gain_grad, hidden_shift_grad = norm_back(
        unit_four, inv_four, gain_four.astype(jnp.float32), grad_hidden
    )
    grad_pre = gelu_pull(grad_activ)[0].astype(jnp.bfloat16)
    expand_bias_grad = jnp.sum(grad_pre.astype(jnp.float32), axis=0)
    expand_weight_grad = jnp.einsum(
        "td,tf->df", second_low, grad_pre, preferred_element_type=jnp.float32
    )
    grad_second = jnp.einsum("tf,df->td", grad_pre, expand_full, preferred_element_type=jnp.float32)
    grad_mid_part, second_gain_grad, second_shift_grad = norm_back(
        unit_three, inv_three, gain_three.astype(jnp.float32), grad_second
    )
    grad_middle = grad_out + grad_mid_part
    order_a, order_b = hypercube_orders(group_size, shard_size)
    grad_branch = grad_middle.astype(jnp.bfloat16)
    proj_bias_grad = jnp.sum(grad_branch.astype(jnp.float32), axis=0)
    proj_weight_grad = jnp.einsum(
        "td,te->de", inner_low, grad_branch, preferred_element_type=jnp.float32
    )
    grad_inner = jnp.einsum("te,de->td", grad_branch, proj_full, preferred_element_type=jnp.float32)
    grad_attended, inner_gain_grad, inner_shift_grad = norm_back(
        unit_two, inv_two, gain_inner.astype(jnp.float32), grad_inner
    )
    ffn_small = (
        second_gain_grad,
        second_shift_grad,
        shrink_bias_grad,
        expand_bias_grad,
        hidden_gain_grad,
        hidden_shift_grad,
        inner_gain_grad,
        inner_shift_grad,
        proj_bias_grad,
    )
    ffn_small_widths = [p.shape[0] // model_width for p in ffn_small]
    ffn_pack = jnp.concatenate(
        [
            expand_weight_grad,
            shrink_weight_grad.reshape(model_width, ratio * model_width),
            proj_weight_grad,
            pack_columns(ffn_small, model_width),
        ],
        axis=1,
    ).astype(jnp.bfloat16)
    grad_att_low = grad_attended.astype(jnp.bfloat16)
    ffn_pack, grad_att_low = lax.optimization_barrier((ffn_pack, grad_att_low))
    ffn_part = grad_rows_reduce(ffn_pack, group_size, shard_size)
    grad_rows = []
    for r in range(row_count):
        parts = attention_backward(
            *row_heads[r],
            heads_major(grad_att_low[r * length : (r + 1) * length]),
            segments[r],
            row_starts[r],
        )
        grad_rows.append(jnp.concatenate([tokens_major(p) for p in parts], axis=1))
    grad_qkv = jnp.concatenate(grad_rows, axis=0).astype(jnp.bfloat16)
    grad_qkv_wide = grad_qkv.astype(jnp.float32)
    query_bias_grad = jnp.sum(grad_qkv_wide[:, :model_width], axis=0)
    value_bias_grad = jnp.sum(grad_qkv_wide[:, 2 * model_width :], axis=0)
    qkv_weight_grad = jnp.einsum(
        "td,te->de", normed_low, grad_qkv, preferred_element_type=jnp.float32
    )
    grad_normed = jnp.einsum("te,de->td", grad_qkv, qkv_full, preferred_element_type=jnp.float32)
    grad_in_part, first_gain_grad, first_shift_grad = norm_back(
        unit_one, inv_one, gain_one.astype(jnp.float32), grad_normed
    )
    attn_small = (
        first_gain_grad,
        first_shift_grad,
        query_bias_grad,
        value_bias_grad,
    )
    attn_pack = jnp.concatenate(
        [qkv_weight_grad, pack_columns(attn_small, model_width)], axis=1
    )
    attn_pack = (
        attn_pack.reshape(shard_size, group_size, n, -1)
        .transpose(1, 0, 2, 3)
        .reshape(model_width, -1)
    )
    ffn_part, attn_pack = lax.optimization_barrier((ffn_part, attn_pack))
    split = (attn_pack.shape[1] // 256) * 128
    attn_left = hypercube_reduce_scatter(
        attn_pack[:, :split], order_a, group_size, shard_size
    )
    attn_right = hypercube_reduce_scatter(
        attn_pack[:, split:], order_b, group_size, shard_size
    )
    gather_in = jnp.concatenate(
        [
            ffn_part,
            attn_left.astype(jnp.bfloat16),
            attn_right.astype(jnp.bfloat16),
        ],
        axis=1,
    )
    gather_in, grad_middle, grad_in_part = lax.optimization_barrier(
        (gather_in, grad_middle, grad_in_part)
    )
    input_grad = (grad_middle + grad_in_part).astype(jnp.bfloat16)
    both = lax.all_gather(
        gather_in,
        "group",
        axis=0,
        tiled=True,
    )
    ffn_cols = ffn_pack.shape[1]
    ffn_back = both[:, :ffn_cols]
    attn_back = both[:, ffn_cols:]
    half = both.shape[0]
    expand_out = ffn_back[:, :wide_width].astype(jnp.float32)
    shrink_out = (
        ffn_back[:, wide_width : 2 * wide_width]
        .reshape(half * ratio, model_width)
        .astype(jnp.float32)
    )
    proj_out = ffn_back[:, 2 * wide_width : 2 * wide_width + model_width].astype(jnp.float32)
    (
        second_gain_out,
        second_shift_out,
        sbias_out,
        ebias_out,
        gain_four_out,
        shift_four_out,
        gain_inner_out,
        shift_inner_out,
        pbias_out,
    ) = unpack_columns(
        ffn_back[:, 2 * wide_width + model_width :].astype(jnp.float32), ffn_small_widths
    )
    qkv_out = attn_back[:, :qkv_width].astype(jnp.float32)
    (
        gain_one_out,
        shift_one_out,
        qbias_out,
        vbias_out,
    ) = unpack_columns(attn_back[:, qkv_width:].astype(jnp.float32), [1] * 4)
    return (
        block_output,
        input_grad,
        gain_one_out,
        shift_one_out,
        qkv_out,
        qbias_out,
        vbias_out,
        gain_inner_out,
        shift_inner_out,
        proj_out,
        pbias_out,
        second_gain_out,
        second_shift_out,
        expand_out,
        ebias_out,
        gain_four_out,
        shift_four_out,
        shrink_out,
        sbias_out,
    )


def solution(mesh):
    in_specs = (
        P(("group", "shard"), None),
        P(("group", "shard"), None),
        P(("group", "shard")),
        P(("group", "shard")),
        P(("group", "shard"), None),
        P(("group", "shard")),
        P(("group", "shard")),
        P(("group", "shard")),
        P(("group", "shard")),
        P(("group", "shard"), None),
        P(("group", "shard")),
        P(("group", "shard")),
        P(("group", "shard")),
        P(("group", "shard"), None),
        P(("group", "shard")),
        P(("group", "shard")),
        P(("group", "shard")),
        P(("group", "shard"), None),
        P(("group", "shard")),
        P(("group", "shard"), None),
    )
    out_specs = (
        P(("group", "shard"), None),
        P(("group", "shard"), None),
        P("shard"),
        P("shard"),
        P("shard", None),
        P("shard"),
        P("shard"),
        P("shard"),
        P("shard"),
        P("shard", None),
        P("shard"),
        P("shard"),
        P("shard"),
        P("shard", None),
        P("shard"),
        P("shard"),
        P("shard"),
        P("shard", None),
        P("shard"),
    )

    return jax.shard_map(
        per_device, mesh=mesh, in_specs=in_specs, out_specs=out_specs, check_vma=False
    )
```

```python
import functools

import jax
import jax.numpy as jnp
from jax import lax
from jax.experimental import pallas as pl
from jax.experimental.pallas import tpu as pltpu
from jax.sharding import PartitionSpec as P


HEADS = 12
HEAD = 64
NSEG = 5


EPSILON = 1e-05


MASKED = -1000000000.0

CHUNK = 128
QBLOCK = 512


def _row_setup(segq_ref, i, tq):
    segq = segq_ref[...]
    own = jnp.broadcast_to(jnp.where(segq < NSEG - 1, segq, -1), (tq, CHUNK))
    rel = (i * tq + lax.broadcasted_iota(jnp.int32, (tq, CHUNK), 0)) - lax.broadcasted_iota(
        jnp.int32, (tq, CHUNK), 1
    )
    keep = (segq < NSEG - 1).astype(jnp.float32)
    return own, rel, keep


def _softmax_rows(q, kt_ref, own, rel, segk_ref, lo, hi, s_ref):
    tq = q.shape[0]

    def first(c, top):
        kc = kt_ref[0, :, pl.ds(c * CHUNK, CHUNK)]
        s = jnp.dot(q, kc, preferred_element_type=jnp.float32)
        allowed = (own == segk_ref[:, pl.ds(c * CHUNK, CHUNK)]) & (rel >= c * CHUNK)
        s = jnp.where(allowed, s, MASKED)
        s_ref[:, pl.ds(c * CHUNK, CHUNK)] = s
        return jnp.maximum(top, s)

    top = lax.fori_loop(lo, hi, first, jnp.full((tq, CHUNK), MASKED, jnp.float32))
    peak = jnp.broadcast_to(jnp.max(top, axis=1, keepdims=True), (tq, CHUNK))

    def second(c, acc):
        e = jnp.exp(s_ref[:, pl.ds(c * CHUNK, CHUNK)] - peak)
        s_ref[:, pl.ds(c * CHUNK, CHUNK)] = e
        return acc + e

    acc = lax.fori_loop(lo, hi, second, jnp.zeros((tq, CHUNK), jnp.float32))
    return jnp.sum(acc, axis=1, keepdims=True)


def _fwd_kernel(lo_ref, q_ref, kt_ref, v_ref, segq_ref, segk_ref, o_ref, s_ref):
    i = pl.program_id(1)
    tq = q_ref.shape[1]
    q = q_ref[0] * jnp.asarray(0.125, q_ref.dtype)
    own, rel, keep = _row_setup(segq_ref, i, tq)
    lo = lo_ref[i]
    hi = (i + 1) * (tq // CHUNK)
    total = _softmax_rows(q, kt_ref, own, rel, segk_ref, lo, hi, s_ref)
    scale = jnp.broadcast_to(keep / total, (tq, CHUNK))

    def third(c, acc):
        p = (s_ref[:, pl.ds(c * CHUNK, CHUNK)] * scale).astype(jnp.bfloat16)
        vc = v_ref[0, pl.ds(c * CHUNK, CHUNK), :]
        return acc + jnp.dot(p, vc, preferred_element_type=jnp.float32)

    o_ref[0] = lax.fori_loop(lo, hi, third, jnp.zeros((tq, q.shape[1]), jnp.float32))


def _bwd_kernel(lo_ref, q_ref, qt_ref, k_ref, kt_ref, vt_ref, do_ref, dot_ref, segq_ref, segk_ref,
                dq_ref, dkt_ref, dvt_ref, s_ref, dp_ref):
    i = pl.program_id(1)
    tq = q_ref.shape[1]

    @pl.when(i == 0)
    def _():
        dkt_ref[...] = jnp.zeros_like(dkt_ref)
        dvt_ref[...] = jnp.zeros_like(dvt_ref)

    eighth = jnp.asarray(0.125, q_ref.dtype)
    qs = q_ref[0] * eighth
    qts = qt_ref[0] * eighth
    do = do_ref[0]
    dot_ = dot_ref[0]
    own, rel, keep = _row_setup(segq_ref, i, tq)
    lo = lo_ref[i]
    hi = (i + 1) * (tq // CHUNK)
    total = _softmax_rows(qs, kt_ref, own, rel, segk_ref, lo, hi, s_ref)
    scale = jnp.broadcast_to(keep / total, (tq, CHUNK))

    def third(c, acc):
        p = s_ref[:, pl.ds(c * CHUNK, CHUNK)] * scale
        dp = jnp.dot(do, vt_ref[0, :, pl.ds(c * CHUNK, CHUNK)], preferred_element_type=jnp.float32)
        s_ref[:, pl.ds(c * CHUNK, CHUNK)] = p
        dp_ref[:, pl.ds(c * CHUNK, CHUNK)] = dp
        return acc + p * dp

    acc = lax.fori_loop(lo, hi, third, jnp.zeros((tq, CHUNK), jnp.float32))
    inner = jnp.broadcast_to(jnp.sum(acc, axis=1, keepdims=True), (tq, CHUNK))

    def fourth(c, dq):
        cols = pl.ds(c * CHUNK, CHUNK)
        p = s_ref[:, cols]
        ds = (p * (dp_ref[:, cols] - inner)).astype(jnp.bfloat16)
        dkt_ref[0, :, cols] += jnp.dot(qts, ds, preferred_element_type=jnp.float32)
        dvt_ref[0, :, cols] += jnp.dot(dot_, p.astype(jnp.bfloat16), preferred_element_type=jnp.float32)
        return dq + jnp.dot(ds, k_ref[0, cols, :], preferred_element_type=jnp.float32)

    dq = lax.fori_loop(lo, hi, fourth, jnp.zeros((tq, q_ref.shape[2]), jnp.float32))
    dq_ref[0] = dq * 0.125


def attention_forward(q, k, v, seg, lo):
    heads, length, head = q.shape
    tq = min(QBLOCK, length)
    rows = pl.BlockSpec((1, tq, head), lambda h, i, lo: (h, i, 0))
    whole = pl.BlockSpec((1, length, head), lambda h, i, lo: (h, 0, 0))
    wide = pl.BlockSpec((1, head, length), lambda h, i, lo: (h, 0, 0))
    segq = pl.BlockSpec((tq, 1), lambda h, i, lo: (i, 0))
    segk = pl.BlockSpec((1, length), lambda h, i, lo: (0, 0))
    return pl.pallas_call(
        _fwd_kernel,
        out_shape=jax.ShapeDtypeStruct((heads, length, head), jnp.float32),
        grid_spec=pltpu.PrefetchScalarGridSpec(
            num_scalar_prefetch=1,
            grid=(heads, length // tq),
            in_specs=[rows, wide, whole, segq, segk],
            out_specs=rows,
            scratch_shapes=[pltpu.VMEM((tq, length), jnp.float32)],
        ),
        compiler_params=pltpu.CompilerParams(dimension_semantics=("arbitrary", "arbitrary")),
        cost_estimate=pl.CostEstimate(
            flops=2 * heads * length * length * head,
            transcendentals=heads * length * length // 2,
            bytes_accessed=4 * heads * length * head * 2,
        ),
    )(lo, q, k.transpose(0, 2, 1), v, seg[:, None], seg[None, :])


def attention_backward(q, k, v, do, seg, lo):
    heads, length, head = q.shape
    tq = min(QBLOCK, length)
    rows = pl.BlockSpec((1, tq, head), lambda h, i, lo: (h, i, 0))
    rows_t = pl.BlockSpec((1, head, tq), lambda h, i, lo: (h, 0, i))
    whole = pl.BlockSpec((1, length, head), lambda h, i, lo: (h, 0, 0))
    wide = pl.BlockSpec((1, head, length), lambda h, i, lo: (h, 0, 0))
    segq = pl.BlockSpec((tq, 1), lambda h, i, lo: (i, 0))
    segk = pl.BlockSpec((1, length), lambda h, i, lo: (0, 0))
    dq, dkt, dvt = pl.pallas_call(
        _bwd_kernel,
        out_shape=(
            jax.ShapeDtypeStruct((heads, length, head), jnp.float32),
            jax.ShapeDtypeStruct((heads, head, length), jnp.float32),
            jax.ShapeDtypeStruct((heads, head, length), jnp.float32),
        ),
        grid_spec=pltpu.PrefetchScalarGridSpec(
            num_scalar_prefetch=1,
            grid=(heads, length // tq),
            in_specs=[rows, rows_t, whole, wide, wide, rows, rows_t, segq, segk],
            out_specs=(rows, wide, wide),
            scratch_shapes=[pltpu.VMEM((tq, length), jnp.float32), pltpu.VMEM((tq, length), jnp.float32)],
        ),
        compiler_params=pltpu.CompilerParams(dimension_semantics=("arbitrary", "arbitrary")),
        cost_estimate=pl.CostEstimate(
            flops=5 * heads * length * length * head,
            transcendentals=heads * length * length // 2,
            bytes_accessed=8 * heads * length * head * 2,
        ),
    )(lo, q, q.transpose(0, 2, 1), k, k.transpose(0, 2, 1), v.transpose(0, 2, 1), do, do.transpose(0, 2, 1), seg[:, None], seg[None, :])
    return dq, dkt.transpose(0, 2, 1), dvt.transpose(0, 2, 1)


def block_starts(seg, lengths, tq):
    ends = jnp.cumsum(lengths)
    starts = jnp.concatenate([jnp.zeros((1,), ends.dtype), ends[:-1]])
    first_seg = seg[::tq]
    return (starts[first_seg] // CHUNK).astype(jnp.int32)


def heads_major(block):
    return block.reshape(block.shape[0], HEADS, HEAD).transpose(1, 0, 2)


def tokens_major(block):
    return block.transpose(1, 0, 2).reshape(block.shape[1], HEADS * HEAD)


def norm_apply(values, gain, shift):
    average = jnp.mean(values, axis=-1, keepdims=True)
    centered = values - average
    inv_scale = lax.rsqrt(jnp.mean(centered * centered, axis=-1, keepdims=True) + EPSILON)
    unit = centered * inv_scale
    return (unit * gain + shift, unit, inv_scale)


def norm_back(unit, inv_scale, gain, grad):
    scaled = grad * gain
    back = inv_scale * (
        scaled
        - jnp.mean(scaled, axis=-1, keepdims=True)
        - unit * jnp.mean(scaled * unit, axis=-1, keepdims=True)
    )
    return (back, jnp.sum(grad * unit, axis=0), jnp.sum(grad, axis=0))


def gelu_exact(values):
    return jax.nn.gelu(values, approximate=False)


def segment_ids(lengths_row, length):
    ends = jnp.cumsum(lengths_row)
    places = jnp.arange(length, dtype=jnp.int32)
    return jnp.sum((places[:, None] >= ends[None, :]).astype(jnp.int32), axis=1)


def pack_columns(parts, rows):
    cols = [p.reshape(rows, -1) for p in parts]
    width = sum(c.shape[1] for c in cols)
    pad = (-width) % 128
    if pad:
        cols.append(jnp.zeros((rows, pad), cols[0].dtype))
    return jnp.concatenate(cols, axis=1)


def unpack_columns(block, widths):
    out = []
    offset = 0
    for w in widths:
        out.append(block[:, offset : offset + w].reshape(-1))
        offset += w
    return out


def destination_order(x, group_size, shard_size, axis):
    shape = x.shape
    lead, size, rest = shape[:axis], shape[axis], shape[axis + 1 :]
    blocks = x.reshape(lead + (shard_size, group_size, size // (group_size * shard_size)) + rest)
    moved = jnp.swapaxes(blocks, len(lead), len(lead) + 1)
    return moved.reshape(shape)


def grad_rows_reduce(packed, group_size, shard_size):
    rows, cols = packed.shape
    n = rows // (group_size * shard_size)
    permuted = (
        packed.reshape(shard_size, group_size, n, cols)
        .transpose(1, 0, 2, 3)
        .reshape(rows, cols)
    )
    return lax.psum_scatter(
        permuted, ("group", "shard"), scatter_dimension=0, tiled=True
    )


def hypercube_orders(group_size, shard_size):
    gbits = [("group", b) for b in range(group_size.bit_length() - 1)]
    sbits = [("shard", b) for b in range(shard_size.bit_length() - 1)]
    first = gbits[:-1] + sbits + gbits[-1:]
    second = list(first)
    if len(gbits) >= 3:
        second[1], second[2] = first[2], first[1]
    return first, second


def hypercube_reduce_scatter(x, order, group_size, shard_size):
    total = group_size * shard_size
    levels = total.bit_length() - 1
    rows, cols = x.shape
    n = rows // total
    sbits = shard_size.bit_length() - 1

    def k_bit(axis, b):
        return b if axis == "shard" else sbits + b

    axes = [levels - 1 - k_bit(axis, b) for axis, b in order]
    cur = (
        x.reshape([2] * levels + [n, cols])
        .transpose(axes + [levels, levels + 1])
        .reshape(rows, cols)
    )
    for axis, b in order:
        size = group_size if axis == "group" else shard_size
        half = cur.shape[0] // 2
        mine = (lax.axis_index(axis) >> b) & 1
        low, high = cur[:half], cur[half:]
        keep = jnp.where(mine == 1, high, low)
        send = jnp.where(mine == 1, low, high).astype(jnp.bfloat16)
        got = lax.ppermute(send, axis, [(j, j ^ (1 << b)) for j in range(size)])
        cur = keep + got.astype(jnp.float32)
    return cur


def per_device(
    tokens,
    doc_lengths,
    first_gain,
    first_shift,
    qkv_weight,
    query_bias,
    value_bias,
    inner_gain,
    inner_shift,
    proj_weight,
    proj_bias,
    second_gain,
    second_shift,
    expand_weight,
    expand_bias,
    hidden_gain,
    hidden_shift,
    shrink_weight,
    shrink_bias,
    out_cotangent,
):
    group_size = lax.axis_size("group")
    shard_size = lax.axis_size("shard")
    n = qkv_weight.shape[0]
    model_width = n * group_size * shard_size
    wide_width = expand_weight.shape[1]
    ratio = wide_width // model_width
    qkv_width = qkv_weight.shape[1]

    small_parts = (
        first_gain,
        first_shift,
        query_bias,
        value_bias,
        inner_gain,
        inner_shift,
        proj_bias,
        second_gain,
        second_shift,
        shrink_bias,
        expand_bias,
        hidden_gain,
        hidden_shift,
    )
    small_widths = [p.shape[0] // n for p in small_parts]
    first_pack = jnp.concatenate([qkv_weight, pack_columns(small_parts, n)], axis=1)
    first_full = lax.all_gather(first_pack, ("group", "shard"), axis=0, tiled=True)
    qkv_full = first_full[:, :qkv_width]
    (
        gain_one,
        shift_one,
        qbias_full,
        vbias_full,
        gain_inner,
        shift_inner,
        pbias_full,
        gain_three,
        shift_three,
        sbias_full,
        ebias_full,
        gain_four,
        shift_four,
    ) = unpack_columns(first_full[:, qkv_width:], small_widths)
    second_pack = jnp.concatenate([proj_weight, expand_weight], axis=1)
    second_full = lax.all_gather(second_pack, ("group", "shard"), axis=0, tiled=True)
    proj_full = second_full[:, :model_width]
    expand_full = second_full[:, model_width:]
    shrink_full = lax.all_gather(shrink_weight, ("group", "shard"), axis=0, tiled=True)

    row_count = doc_lengths.shape[0]
    length = tokens.shape[0] // row_count
    inputs = tokens.astype(jnp.float32)
    normed, unit_one, inv_one = norm_apply(
        inputs, gain_one.astype(jnp.float32), shift_one.astype(jnp.float32)
    )
    normed_low = normed.astype(jnp.bfloat16)
    bias_cat = jnp.concatenate([qbias_full, jnp.zeros_like(qbias_full), vbias_full]).astype(
        jnp.float32
    )
    qkv_low = (jnp.dot(normed_low, qkv_full, preferred_element_type=jnp.float32) + bias_cat).astype(
        jnp.bfloat16
    )
    segments = jax.vmap(functools.partial(segment_ids, length=length))(doc_lengths).astype(
        jnp.int32
    )
    tq = min(QBLOCK, length)
    row_heads = []
    row_starts = []
    attended_rows = []
    for r in range(row_count):
        piece = qkv_low[r * length : (r + 1) * length]
        heads = tuple(
            heads_major(piece[:, j * model_width : (j + 1) * model_width]) for j in range(3)
        )
        lo = block_starts(segments[r], doc_lengths[r], tq)
        row_heads.append(heads)
        row_starts.append(lo)
        attended_rows.append(tokens_major(attention_forward(*heads, segments[r], lo)))
    attended = jnp.concatenate(attended_rows, axis=0)
    inner, unit_two, inv_two = norm_apply(
        attended, gain_inner.astype(jnp.float32), shift_inner.astype(jnp.float32)
    )
    inner_low = inner.astype(jnp.bfloat16)
    middle = (
        inputs
        + jnp.dot(inner_low, proj_full, preferred_element_type=jnp.float32)
        + pbias_full.astype(jnp.float32)
    )
    second, unit_three, inv_three = norm_apply(
        middle, gain_three.astype(jnp.float32), shift_three.astype(jnp.float32)
    )
    second_low = second.astype(jnp.bfloat16)
    pre_act = jnp.dot(
        second_low, expand_full, preferred_element_type=jnp.float32
    ) + ebias_full.astype(jnp.float32)
    activ, gelu_pull = jax.vjp(gelu_exact, pre_act)
    hidden, unit_four, inv_four = norm_apply(
        activ, gain_four.astype(jnp.float32), shift_four.astype(jnp.float32)
    )
    hidden_low = hidden.astype(jnp.bfloat16)
    output = (
        middle
        + jnp.dot(hidden_low, shrink_full, preferred_element_type=jnp.float32)
        + sbias_full.astype(jnp.float32)
    )
    block_output = output.astype(jnp.bfloat16)
    grad_out = out_cotangent.astype(jnp.float32)
    shrink_weight_grad = jnp.einsum(
        "tf,td->fd", hidden_low, out_cotangent, preferred_element_type=jnp.float32
    )
    shrink_bias_grad = jnp.sum(grad_out, axis=0)
    grad_hidden = jnp.einsum(
        "td,fd->tf", out_cotangent, shrink_full, preferred_element_type=jnp.float32
    )
    grad_activ, hidden_gain_grad, hidden_shift_grad = norm_back(
        unit_four, inv_four, gain_four.astype(jnp.float32), grad_hidden
    )
    grad_pre = gelu_pull(grad_activ)[0].astype(jnp.bfloat16)
    expand_bias_grad = jnp.sum(grad_pre.astype(jnp.float32), axis=0)
    expand_weight_grad = jnp.einsum(
        "td,tf->df", second_low, grad_pre, preferred_element_type=jnp.float32
    )
    grad_second = jnp.einsum("tf,df->td", grad_pre, expand_full, preferred_element_type=jnp.float32)
    grad_mid_part, second_gain_grad, second_shift_grad = norm_back(
        unit_three, inv_three, gain_three.astype(jnp.float32), grad_second
    )
    grad_middle = grad_out + grad_mid_part
    order_a, order_b = hypercube_orders(group_size, shard_size)
    grad_branch = grad_middle.astype(jnp.bfloat16)
    proj_bias_grad = jnp.sum(grad_branch.astype(jnp.float32), axis=0)
    proj_weight_grad = jnp.einsum(
        "td,te->de", inner_low, grad_branch, preferred_element_type=jnp.float32
    )
    grad_inner = jnp.einsum("te,de->td", grad_branch, proj_full, preferred_element_type=jnp.float32)
    grad_attended, inner_gain_grad, inner_shift_grad = norm_back(
        unit_two, inv_two, gain_inner.astype(jnp.float32), grad_inner
    )
    ffn_small = (
        second_gain_grad,
        second_shift_grad,
        shrink_bias_grad,
        expand_bias_grad,
        hidden_gain_grad,
        hidden_shift_grad,
        inner_gain_grad,
        inner_shift_grad,
        proj_bias_grad,
    )
    ffn_small_widths = [p.shape[0] // model_width for p in ffn_small]
    ffn_pack = jnp.concatenate(
        [
            expand_weight_grad,
            shrink_weight_grad.reshape(model_width, ratio * model_width),
            proj_weight_grad,
            pack_columns(ffn_small, model_width),
        ],
        axis=1,
    ).astype(jnp.bfloat16)
    grad_att_low = grad_attended.astype(jnp.bfloat16)
    ffn_pack, grad_att_low = lax.optimization_barrier((ffn_pack, grad_att_low))
    ffn_part = grad_rows_reduce(ffn_pack, group_size, shard_size)
    grad_rows = []
    for r in range(row_count):
        parts = attention_backward(
            *row_heads[r],
            heads_major(grad_att_low[r * length : (r + 1) * length]),
            segments[r],
            row_starts[r],
        )
        grad_rows.append(jnp.concatenate([tokens_major(p) for p in parts], axis=1))
    grad_qkv = jnp.concatenate(grad_rows, axis=0).astype(jnp.bfloat16)
    grad_qkv_wide = grad_qkv.astype(jnp.float32)
    query_bias_grad = jnp.sum(grad_qkv_wide[:, :model_width], axis=0)
    value_bias_grad = jnp.sum(grad_qkv_wide[:, 2 * model_width :], axis=0)
    split = ((qkv_width + 128) // 256) * 128
    left_grad = jnp.einsum(
        "td,te->de", normed_low, grad_qkv[:, :split], preferred_element_type=jnp.float32
    )
    grad_normed = jnp.einsum("te,de->td", grad_qkv, qkv_full, preferred_element_type=jnp.float32)
    grad_in_part, first_gain_grad, first_shift_grad = norm_back(
        unit_one, inv_one, gain_one.astype(jnp.float32), grad_normed
    )
    input_grad = (grad_middle + grad_in_part).astype(jnp.bfloat16)
    attn_small = (
        first_gain_grad,
        first_shift_grad,
        query_bias_grad,
        value_bias_grad,
    )
    right_grad = jnp.concatenate(
        [
            jnp.einsum(
                "td,te->de", normed_low, grad_qkv[:, split:], preferred_element_type=jnp.float32
            ),
            pack_columns(attn_small, model_width),
        ],
        axis=1,
    )
    left_grad = destination_order(left_grad, group_size, shard_size, 0)
    right_grad = destination_order(right_grad, group_size, shard_size, 0)
    ffn_part, left_grad = lax.optimization_barrier((ffn_part, left_grad))
    attn_left = hypercube_reduce_scatter(left_grad, order_a, group_size, shard_size)
    attn_right = hypercube_reduce_scatter(right_grad, order_b, group_size, shard_size)
    both = lax.all_gather(
        jnp.concatenate(
            [
                ffn_part,
                attn_left.astype(jnp.bfloat16),
                attn_right.astype(jnp.bfloat16),
            ],
            axis=1,
        ),
        "group",
        axis=0,
        tiled=True,
    )
    ffn_cols = ffn_pack.shape[1]
    ffn_back = both[:, :ffn_cols]
    attn_back = both[:, ffn_cols:]
    half = both.shape[0]
    expand_out = ffn_back[:, :wide_width].astype(jnp.float32)
    shrink_out = (
        ffn_back[:, wide_width : 2 * wide_width]
        .reshape(half * ratio, model_width)
        .astype(jnp.float32)
    )
    proj_out = ffn_back[:, 2 * wide_width : 2 * wide_width + model_width].astype(jnp.float32)
    (
        second_gain_out,
        second_shift_out,
        sbias_out,
        ebias_out,
        gain_four_out,
        shift_four_out,
        gain_inner_out,
        shift_inner_out,
        pbias_out,
    ) = unpack_columns(
        ffn_back[:, 2 * wide_width + model_width :].astype(jnp.float32), ffn_small_widths
    )
    qkv_out = attn_back[:, :qkv_width].astype(jnp.float32)
    (
        gain_one_out,
        shift_one_out,
        qbias_out,
        vbias_out,
    ) = unpack_columns(attn_back[:, qkv_width:].astype(jnp.float32), [1] * 4)
    return (
        block_output,
        input_grad,
        gain_one_out,
        shift_one_out,
        qkv_out,
        qbias_out,
        vbias_out,
        gain_inner_out,
        shift_inner_out,
        proj_out,
        pbias_out,
        second_gain_out,
        second_shift_out,
        expand_out,
        ebias_out,
        gain_four_out,
        shift_four_out,
        shrink_out,
        sbias_out,
    )


def solution(mesh):
    in_specs = (
        P(("group", "shard"), None),
        P(("group", "shard"), None),
        P(("group", "shard")),
        P(("group", "shard")),
        P(("group", "shard"), None),
        P(("group", "shard")),
        P(("group", "shard")),
        P(("group", "shard")),
        P(("group", "shard")),
        P(("group", "shard"), None),
        P(("group", "shard")),
        P(("group", "shard")),
        P(("group", "shard")),
        P(("group", "shard"), None),
        P(("group", "shard")),
        P(("group", "shard")),
        P(("group", "shard")),
        P(("group", "shard"), None),
        P(("group", "shard")),
        P(("group", "shard"), None),
    )
    out_specs = (
        P(("group", "shard"), None),
        P(("group", "shard"), None),
        P("shard"),
        P("shard"),
        P("shard", None),
        P("shard"),
        P("shard"),
        P("shard"),
        P("shard"),
        P("shard", None),
        P("shard"),
        P("shard"),
        P("shard"),
        P("shard", None),
        P("shard"),
        P("shard"),
        P("shard"),
        P("shard", None),
        P("shard"),
    )

    return jax.shard_map(
        per_device, mesh=mesh, in_specs=in_specs, out_specs=out_specs, check_vma=False
    )
```

```python
import functools

import jax
import jax.numpy as jnp
from jax import lax
from jax.experimental import pallas as pl
from jax.experimental.pallas import tpu as pltpu
from jax.sharding import PartitionSpec as P


HEADS = 12
HEAD = 64
NSEG = 5


EPSILON = 1e-05


MASKED = -1000000000.0

CHUNK = 128
QBLOCK = 512


def _row_setup(segq_ref, i, tq):
    segq = segq_ref[...]
    own = jnp.broadcast_to(jnp.where(segq < NSEG - 1, segq, -1), (tq, CHUNK))
    rel = (i * tq + lax.broadcasted_iota(jnp.int32, (tq, CHUNK), 0)) - lax.broadcasted_iota(
        jnp.int32, (tq, CHUNK), 1
    )
    keep = (segq < NSEG - 1).astype(jnp.float32)
    return own, rel, keep


def _softmax_rows(q, kt_ref, own, rel, segk_ref, lo, hi, s_ref):
    tq = q.shape[0]

    def first(c, top):
        kc = kt_ref[0, :, pl.ds(c * CHUNK, CHUNK)]
        s = jnp.dot(q, kc, preferred_element_type=jnp.float32)
        allowed = (own == segk_ref[:, pl.ds(c * CHUNK, CHUNK)]) & (rel >= c * CHUNK)
        s = jnp.where(allowed, s, MASKED)
        s_ref[:, pl.ds(c * CHUNK, CHUNK)] = s
        return jnp.maximum(top, s)

    top = lax.fori_loop(lo, hi, first, jnp.full((tq, CHUNK), MASKED, jnp.float32))
    peak = jnp.broadcast_to(jnp.max(top, axis=1, keepdims=True), (tq, CHUNK))

    def second(c, acc):
        e = jnp.exp(s_ref[:, pl.ds(c * CHUNK, CHUNK)] - peak)
        s_ref[:, pl.ds(c * CHUNK, CHUNK)] = e
        return acc + e

    acc = lax.fori_loop(lo, hi, second, jnp.zeros((tq, CHUNK), jnp.float32))
    return jnp.sum(acc, axis=1, keepdims=True)


def _fwd_kernel(lo_ref, q_ref, kt_ref, v_ref, segq_ref, segk_ref, o_ref, s_ref):
    i = pl.program_id(1)
    tq = q_ref.shape[1]
    q = q_ref[0] * jnp.asarray(0.125, q_ref.dtype)
    own, rel, keep = _row_setup(segq_ref, i, tq)
    lo = lo_ref[i]
    hi = (i + 1) * (tq // CHUNK)
    total = _softmax_rows(q, kt_ref, own, rel, segk_ref, lo, hi, s_ref)
    scale = jnp.broadcast_to(keep / total, (tq, CHUNK))

    def third(c, acc):
        p = (s_ref[:, pl.ds(c * CHUNK, CHUNK)] * scale).astype(jnp.bfloat16)
        vc = v_ref[0, pl.ds(c * CHUNK, CHUNK), :]
        return acc + jnp.dot(p, vc, preferred_element_type=jnp.float32)

    o_ref[0] = lax.fori_loop(lo, hi, third, jnp.zeros((tq, q.shape[1]), jnp.float32))


def _bwd_kernel(lo_ref, q_ref, qt_ref, k_ref, kt_ref, vt_ref, do_ref, dot_ref, segq_ref, segk_ref,
                dq_ref, dkt_ref, dvt_ref, s_ref, dp_ref):
    i = pl.program_id(1)
    tq = q_ref.shape[1]

    @pl.when(i == 0)
    def _():
        dkt_ref[...] = jnp.zeros_like(dkt_ref)
        dvt_ref[...] = jnp.zeros_like(dvt_ref)

    eighth = jnp.asarray(0.125, q_ref.dtype)
    qs = q_ref[0] * eighth
    qts = qt_ref[0] * eighth
    do = do_ref[0]
    dot_ = dot_ref[0]
    own, rel, keep = _row_setup(segq_ref, i, tq)
    lo = lo_ref[i]
    hi = (i + 1) * (tq // CHUNK)
    total = _softmax_rows(qs, kt_ref, own, rel, segk_ref, lo, hi, s_ref)
    scale = jnp.broadcast_to(keep / total, (tq, CHUNK))

    def third(c, acc):
        p = s_ref[:, pl.ds(c * CHUNK, CHUNK)] * scale
        dp = jnp.dot(do, vt_ref[0, :, pl.ds(c * CHUNK, CHUNK)], preferred_element_type=jnp.float32)
        s_ref[:, pl.ds(c * CHUNK, CHUNK)] = p
        dp_ref[:, pl.ds(c * CHUNK, CHUNK)] = dp
        return acc + p * dp

    acc = lax.fori_loop(lo, hi, third, jnp.zeros((tq, CHUNK), jnp.float32))
    inner = jnp.broadcast_to(jnp.sum(acc, axis=1, keepdims=True), (tq, CHUNK))

    def fourth(c, dq):
        cols = pl.ds(c * CHUNK, CHUNK)
        p = s_ref[:, cols]
        ds = (p * (dp_ref[:, cols] - inner)).astype(jnp.bfloat16)
        dkt_ref[0, :, cols] += jnp.dot(qts, ds, preferred_element_type=jnp.float32)
        dvt_ref[0, :, cols] += jnp.dot(dot_, p.astype(jnp.bfloat16), preferred_element_type=jnp.float32)
        return dq + jnp.dot(ds, k_ref[0, cols, :], preferred_element_type=jnp.float32)

    dq = lax.fori_loop(lo, hi, fourth, jnp.zeros((tq, q_ref.shape[2]), jnp.float32))
    dq_ref[0] = dq * 0.125


def attention_forward(q, k, v, seg, lo):
    heads, length, head = q.shape
    tq = min(QBLOCK, length)
    rows = pl.BlockSpec((1, tq, head), lambda h, i, lo: (h, i, 0))
    whole = pl.BlockSpec((1, length, head), lambda h, i, lo: (h, 0, 0))
    wide = pl.BlockSpec((1, head, length), lambda h, i, lo: (h, 0, 0))
    segq = pl.BlockSpec((tq, 1), lambda h, i, lo: (i, 0))
    segk = pl.BlockSpec((1, length), lambda h, i, lo: (0, 0))
    return pl.pallas_call(
        _fwd_kernel,
        out_shape=jax.ShapeDtypeStruct((heads, length, head), jnp.float32),
        grid_spec=pltpu.PrefetchScalarGridSpec(
            num_scalar_prefetch=1,
            grid=(heads, length // tq),
            in_specs=[rows, wide, whole, segq, segk],
            out_specs=rows,
            scratch_shapes=[pltpu.VMEM((tq, length), jnp.float32)],
        ),
        compiler_params=pltpu.CompilerParams(dimension_semantics=("arbitrary", "arbitrary")),
        cost_estimate=pl.CostEstimate(
            flops=2 * heads * length * length * head,
            transcendentals=heads * length * length // 2,
            bytes_accessed=4 * heads * length * head * 2,
        ),
    )(lo, q, k.transpose(0, 2, 1), v, seg[:, None], seg[None, :])


def attention_backward(q, k, v, do, seg, lo):
    heads, length, head = q.shape
    tq = min(QBLOCK, length)
    rows = pl.BlockSpec((1, tq, head), lambda h, i, lo: (h, i, 0))
    rows_t = pl.BlockSpec((1, head, tq), lambda h, i, lo: (h, 0, i))
    whole = pl.BlockSpec((1, length, head), lambda h, i, lo: (h, 0, 0))
    wide = pl.BlockSpec((1, head, length), lambda h, i, lo: (h, 0, 0))
    segq = pl.BlockSpec((tq, 1), lambda h, i, lo: (i, 0))
    segk = pl.BlockSpec((1, length), lambda h, i, lo: (0, 0))
    dq, dkt, dvt = pl.pallas_call(
        _bwd_kernel,
        out_shape=(
            jax.ShapeDtypeStruct((heads, length, head), jnp.float32),
            jax.ShapeDtypeStruct((heads, head, length), jnp.float32),
            jax.ShapeDtypeStruct((heads, head, length), jnp.float32),
        ),
        grid_spec=pltpu.PrefetchScalarGridSpec(
            num_scalar_prefetch=1,
            grid=(heads, length // tq),
            in_specs=[rows, rows_t, whole, wide, wide, rows, rows_t, segq, segk],
            out_specs=(rows, wide, wide),
            scratch_shapes=[pltpu.VMEM((tq, length), jnp.float32), pltpu.VMEM((tq, length), jnp.float32)],
        ),
        compiler_params=pltpu.CompilerParams(dimension_semantics=("arbitrary", "arbitrary")),
        cost_estimate=pl.CostEstimate(
            flops=5 * heads * length * length * head,
            transcendentals=heads * length * length // 2,
            bytes_accessed=8 * heads * length * head * 2,
        ),
    )(lo, q, q.transpose(0, 2, 1), k, k.transpose(0, 2, 1), v.transpose(0, 2, 1), do, do.transpose(0, 2, 1), seg[:, None], seg[None, :])
    return dq, dkt.transpose(0, 2, 1), dvt.transpose(0, 2, 1)


def block_starts(seg, lengths, tq):
    ends = jnp.cumsum(lengths)
    starts = jnp.concatenate([jnp.zeros((1,), ends.dtype), ends[:-1]])
    first_seg = seg[::tq]
    return (starts[first_seg] // CHUNK).astype(jnp.int32)


def heads_major(block):
    return block.reshape(block.shape[0], HEADS, HEAD).transpose(1, 0, 2)


def tokens_major(block):
    return block.transpose(1, 0, 2).reshape(block.shape[1], HEADS * HEAD)


def norm_apply(values, gain, shift):
    average = jnp.mean(values, axis=-1, keepdims=True)
    centered = values - average
    inv_scale = lax.rsqrt(jnp.mean(centered * centered, axis=-1, keepdims=True) + EPSILON)
    unit = centered * inv_scale
    return (unit * gain + shift, unit, inv_scale)


def norm_back(unit, inv_scale, gain, grad):
    scaled = grad * gain
    back = inv_scale * (
        scaled
        - jnp.mean(scaled, axis=-1, keepdims=True)
        - unit * jnp.mean(scaled * unit, axis=-1, keepdims=True)
    )
    return (back, jnp.sum(grad * unit, axis=0), jnp.sum(grad, axis=0))


def gelu_exact(values):
    return jax.nn.gelu(values, approximate=False)


def segment_ids(lengths_row, length):
    ends = jnp.cumsum(lengths_row)
    places = jnp.arange(length, dtype=jnp.int32)
    return jnp.sum((places[:, None] >= ends[None, :]).astype(jnp.int32), axis=1)


def pack_columns(parts, rows):
    cols = [p.reshape(rows, -1) for p in parts]
    width = sum(c.shape[1] for c in cols)
    pad = (-width) % 128
    if pad:
        cols.append(jnp.zeros((rows, pad), cols[0].dtype))
    return jnp.concatenate(cols, axis=1)


def unpack_columns(block, widths):
    out = []
    offset = 0
    for w in widths:
        out.append(block[:, offset : offset + w].reshape(-1))
        offset += w
    return out


def grad_rows_reduce(packed, group_size, shard_size):
    rows, cols = packed.shape
    n = rows // (group_size * shard_size)
    permuted = (
        packed.reshape(shard_size, group_size, n, cols)
        .transpose(1, 0, 2, 3)
        .reshape(rows, cols)
    )
    return lax.psum_scatter(
        permuted, ("group", "shard"), scatter_dimension=0, tiled=True
    )


def hypercube_orders(group_size, shard_size):
    gbits = [("group", b) for b in range(group_size.bit_length() - 1)]
    sbits = [("shard", b) for b in range(shard_size.bit_length() - 1)]
    first = gbits[:-1] + sbits + gbits[-1:]
    second = list(first)
    if len(gbits) >= 3:
        second[1], second[2] = first[2], first[1]
    return first, second


def hypercube_reduce_scatter(x, order, group_size, shard_size):
    total = group_size * shard_size
    levels = total.bit_length() - 1
    rows, cols = x.shape
    n = rows // total
    sbits = shard_size.bit_length() - 1

    def k_bit(axis, b):
        return b if axis == "shard" else sbits + b

    axes = [levels - 1 - k_bit(axis, b) for axis, b in order]
    cur = (
        x.reshape([2] * levels + [n, cols])
        .transpose(axes + [levels, levels + 1])
        .reshape(rows, cols)
    )
    for axis, b in order:
        size = group_size if axis == "group" else shard_size
        half = cur.shape[0] // 2
        mine = (lax.axis_index(axis) >> b) & 1
        low, high = cur[:half], cur[half:]
        keep = jnp.where(mine == 1, high, low)
        send = jnp.where(mine == 1, low, high).astype(jnp.bfloat16)
        got = lax.ppermute(send, axis, [(j, j ^ (1 << b)) for j in range(size)])
        cur = keep + got.astype(jnp.float32)
    return cur


def hypercube_all_gather(x, order, group_size, shard_size):
    total = group_size * shard_size
    levels = total.bit_length() - 1
    n, cols = x.shape
    sbits = shard_size.bit_length() - 1
    cur = x
    for axis, b in order:
        size = group_size if axis == "group" else shard_size
        got = lax.ppermute(cur, axis, [(j, j ^ (1 << b)) for j in range(size)])
        mine = (lax.axis_index(axis) >> b) & 1
        low = jnp.where(mine == 1, got, cur)
        high = jnp.where(mine == 1, cur, got)
        cur = jnp.concatenate([low, high], axis=0)
    kbits = [b if axis == "shard" else sbits + b for axis, b in order]
    perm = [levels - 1 - kbits.index(levels - 1 - a) for a in range(levels)]
    return (
        cur.reshape([2] * levels + [n, cols])
        .transpose(perm + [levels, levels + 1])
        .reshape(total * n, cols)
    )


def per_device(
    tokens,
    doc_lengths,
    first_gain,
    first_shift,
    qkv_weight,
    query_bias,
    value_bias,
    inner_gain,
    inner_shift,
    proj_weight,
    proj_bias,
    second_gain,
    second_shift,
    expand_weight,
    expand_bias,
    hidden_gain,
    hidden_shift,
    shrink_weight,
    shrink_bias,
    out_cotangent,
):
    group_size = lax.axis_size("group")
    shard_size = lax.axis_size("shard")
    n = qkv_weight.shape[0]
    model_width = n * group_size * shard_size
    wide_width = expand_weight.shape[1]
    ratio = wide_width // model_width
    qkv_width = qkv_weight.shape[1]

    small_parts = (
        first_gain,
        first_shift,
        query_bias,
        value_bias,
        inner_gain,
        inner_shift,
        proj_bias,
        second_gain,
        second_shift,
        shrink_bias,
        expand_bias,
        hidden_gain,
        hidden_shift,
    )
    small_widths = [p.shape[0] // n for p in small_parts]
    first_pack = jnp.concatenate([qkv_weight, pack_columns(small_parts, n)], axis=1)
    gather_a, gather_b = hypercube_orders(group_size, shard_size)
    cut = (first_pack.shape[1] // 256) * 128
    first_full = jnp.concatenate(
        [
            hypercube_all_gather(
                first_pack[:, :cut], gather_a[::-1], group_size, shard_size
            ),
            hypercube_all_gather(
                first_pack[:, cut:], gather_b[::-1], group_size, shard_size
            ),
        ],
        axis=1,
    )
    qkv_full = first_full[:, :qkv_width]
    (
        gain_one,
        shift_one,
        qbias_full,
        vbias_full,
        gain_inner,
        shift_inner,
        pbias_full,
        gain_three,
        shift_three,
        sbias_full,
        ebias_full,
        gain_four,
        shift_four,
    ) = unpack_columns(first_full[:, qkv_width:], small_widths)
    second_pack = jnp.concatenate([proj_weight, expand_weight], axis=1)
    second_full = lax.all_gather(second_pack, ("group", "shard"), axis=0, tiled=True)
    proj_full = second_full[:, :model_width]
    expand_full = second_full[:, model_width:]
    shrink_full = lax.all_gather(shrink_weight, ("group", "shard"), axis=0, tiled=True)

    row_count = doc_lengths.shape[0]
    length = tokens.shape[0] // row_count
    inputs = tokens.astype(jnp.float32)
    normed, unit_one, inv_one = norm_apply(
        inputs, gain_one.astype(jnp.float32), shift_one.astype(jnp.float32)
    )
    normed_low = normed.astype(jnp.bfloat16)
    bias_cat = jnp.concatenate([qbias_full, jnp.zeros_like(qbias_full), vbias_full]).astype(
        jnp.float32
    )
    qkv_low = (jnp.dot(normed_low, qkv_full, preferred_element_type=jnp.float32) + bias_cat).astype(
        jnp.bfloat16
    )
    segments = jax.vmap(functools.partial(segment_ids, length=length))(doc_lengths).astype(
        jnp.int32
    )
    tq = min(QBLOCK, length)
    row_heads = []
    row_starts = []
    attended_rows = []
    for r in range(row_count):
        piece = qkv_low[r * length : (r + 1) * length]
        heads = tuple(
            heads_major(piece[:, j * model_width : (j + 1) * model_width]) for j in range(3)
        )
        lo = block_starts(segments[r], doc_lengths[r], tq)
        row_heads.append(heads)
        row_starts.append(lo)
        attended_rows.append(tokens_major(attention_forward(*heads, segments[r], lo)))
    attended = jnp.concatenate(attended_rows, axis=0)
    inner, unit_two, inv_two = norm_apply(
        attended, gain_inner.astype(jnp.float32), shift_inner.astype(jnp.float32)
    )
    inner_low = inner.astype(jnp.bfloat16)
    middle = (
        inputs
        + jnp.dot(inner_low, proj_full, preferred_element_type=jnp.float32)
        + pbias_full.astype(jnp.float32)
    )
    second, unit_three, inv_three = norm_apply(
        middle, gain_three.astype(jnp.float32), shift_three.astype(jnp.float32)
    )
    second_low = second.astype(jnp.bfloat16)
    pre_act = jnp.dot(
        second_low, expand_full, preferred_element_type=jnp.float32
    ) + ebias_full.astype(jnp.float32)
    activ, gelu_pull = jax.vjp(gelu_exact, pre_act)
    hidden, unit_four, inv_four = norm_apply(
        activ, gain_four.astype(jnp.float32), shift_four.astype(jnp.float32)
    )
    hidden_low = hidden.astype(jnp.bfloat16)
    output = (
        middle
        + jnp.dot(hidden_low, shrink_full, preferred_element_type=jnp.float32)
        + sbias_full.astype(jnp.float32)
    )
    block_output = output.astype(jnp.bfloat16)
    grad_out = out_cotangent.astype(jnp.float32)
    shrink_weight_grad = jnp.einsum(
        "tf,td->fd", hidden_low, out_cotangent, preferred_element_type=jnp.float32
    )
    shrink_bias_grad = jnp.sum(grad_out, axis=0)
    grad_hidden = jnp.einsum(
        "td,fd->tf", out_cotangent, shrink_full, preferred_element_type=jnp.float32
    )
    grad_activ, hidden_gain_grad, hidden_shift_grad = norm_back(
        unit_four, inv_four, gain_four.astype(jnp.float32), grad_hidden
    )
    grad_pre = gelu_pull(grad_activ)[0].astype(jnp.bfloat16)
    expand_bias_grad = jnp.sum(grad_pre.astype(jnp.float32), axis=0)
    expand_weight_grad = jnp.einsum(
        "td,tf->df", second_low, grad_pre, preferred_element_type=jnp.float32
    )
    grad_second = jnp.einsum("tf,df->td", grad_pre, expand_full, preferred_element_type=jnp.float32)
    grad_mid_part, second_gain_grad, second_shift_grad = norm_back(
        unit_three, inv_three, gain_three.astype(jnp.float32), grad_second
    )
    grad_middle = grad_out + grad_mid_part
    order_a, order_b = hypercube_orders(group_size, shard_size)
    grad_branch = grad_middle.astype(jnp.bfloat16)
    proj_bias_grad = jnp.sum(grad_branch.astype(jnp.float32), axis=0)
    proj_weight_grad = jnp.einsum(
        "td,te->de", inner_low, grad_branch, preferred_element_type=jnp.float32
    )
    grad_inner = jnp.einsum("te,de->td", grad_branch, proj_full, preferred_element_type=jnp.float32)
    grad_attended, inner_gain_grad, inner_shift_grad = norm_back(
        unit_two, inv_two, gain_inner.astype(jnp.float32), grad_inner
    )
    ffn_small = (
        second_gain_grad,
        second_shift_grad,
        shrink_bias_grad,
        expand_bias_grad,
        hidden_gain_grad,
        hidden_shift_grad,
        inner_gain_grad,
        inner_shift_grad,
        proj_bias_grad,
    )
    ffn_small_widths = [p.shape[0] // model_width for p in ffn_small]
    ffn_pack = jnp.concatenate(
        [
            expand_weight_grad,
            shrink_weight_grad.reshape(model_width, ratio * model_width),
            proj_weight_grad,
            pack_columns(ffn_small, model_width),
        ],
        axis=1,
    ).astype(jnp.bfloat16)
    grad_att_low = grad_attended.astype(jnp.bfloat16)
    ffn_pack, grad_att_low = lax.optimization_barrier((ffn_pack, grad_att_low))
    ffn_part = grad_rows_reduce(ffn_pack, group_size, shard_size)
    grad_rows = []
    for r in range(row_count):
        parts = attention_backward(
            *row_heads[r],
            heads_major(grad_att_low[r * length : (r + 1) * length]),
            segments[r],
            row_starts[r],
        )
        grad_rows.append(jnp.concatenate([tokens_major(p) for p in parts], axis=1))
    grad_qkv = jnp.concatenate(grad_rows, axis=0).astype(jnp.bfloat16)
    grad_qkv_wide = grad_qkv.astype(jnp.float32)
    query_bias_grad = jnp.sum(grad_qkv_wide[:, :model_width], axis=0)
    value_bias_grad = jnp.sum(grad_qkv_wide[:, 2 * model_width :], axis=0)
    qkv_weight_grad = jnp.einsum(
        "td,te->de", normed_low, grad_qkv, preferred_element_type=jnp.float32
    )
    grad_normed = jnp.einsum("te,de->td", grad_qkv, qkv_full, preferred_element_type=jnp.float32)
    grad_in_part, first_gain_grad, first_shift_grad = norm_back(
        unit_one, inv_one, gain_one.astype(jnp.float32), grad_normed
    )
    input_grad = (grad_middle + grad_in_part).astype(jnp.bfloat16)
    attn_small = (
        first_gain_grad,
        first_shift_grad,
        query_bias_grad,
        value_bias_grad,
    )
    attn_pack = jnp.concatenate(
        [qkv_weight_grad, pack_columns(attn_small, model_width)], axis=1
    )
    attn_pack = (
        attn_pack.reshape(shard_size, group_size, n, -1)
        .transpose(1, 0, 2, 3)
        .reshape(model_width, -1)
    )
    ffn_part, attn_pack = lax.optimization_barrier((ffn_part, attn_pack))
    split = (attn_pack.shape[1] // 256) * 128
    attn_left = hypercube_reduce_scatter(
        attn_pack[:, :split], order_a, group_size, shard_size
    )
    attn_right = hypercube_reduce_scatter(
        attn_pack[:, split:], order_b, group_size, shard_size
    )
    both = lax.all_gather(
        jnp.concatenate(
            [
                ffn_part,
                attn_left.astype(jnp.bfloat16),
                attn_right.astype(jnp.bfloat16),
            ],
            axis=1,
        ),
        "group",
        axis=0,
        tiled=True,
    )
    ffn_cols = ffn_pack.shape[1]
    ffn_back = both[:, :ffn_cols]
    attn_back = both[:, ffn_cols:]
    half = both.shape[0]
    expand_out = ffn_back[:, :wide_width].astype(jnp.float32)
    shrink_out = (
        ffn_back[:, wide_width : 2 * wide_width]
        .reshape(half * ratio, model_width)
        .astype(jnp.float32)
    )
    proj_out = ffn_back[:, 2 * wide_width : 2 * wide_width + model_width].astype(jnp.float32)
    (
        second_gain_out,
        second_shift_out,
        sbias_out,
        ebias_out,
        gain_four_out,
        shift_four_out,
        gain_inner_out,
        shift_inner_out,
        pbias_out,
    ) = unpack_columns(
        ffn_back[:, 2 * wide_width + model_width :].astype(jnp.float32), ffn_small_widths
    )
    qkv_out = attn_back[:, :qkv_width].astype(jnp.float32)
    (
        gain_one_out,
        shift_one_out,
        qbias_out,
        vbias_out,
    ) = unpack_columns(attn_back[:, qkv_width:].astype(jnp.float32), [1] * 4)
    return (
        block_output,
        input_grad,
        gain_one_out,
        shift_one_out,
        qkv_out,
        qbias_out,
        vbias_out,
        gain_inner_out,
        shift_inner_out,
        proj_out,
        pbias_out,
        second_gain_out,
        second_shift_out,
        expand_out,
        ebias_out,
        gain_four_out,
        shift_four_out,
        shrink_out,
        sbias_out,
    )


def solution(mesh):
    in_specs = (
        P(("group", "shard"), None),
        P(("group", "shard"), None),
        P(("group", "shard")),
        P(("group", "shard")),
        P(("group", "shard"), None),
        P(("group", "shard")),
        P(("group", "shard")),
        P(("group", "shard")),
        P(("group", "shard")),
        P(("group", "shard"), None),
        P(("group", "shard")),
        P(("group", "shard")),
        P(("group", "shard")),
        P(("group", "shard"), None),
        P(("group", "shard")),
        P(("group", "shard")),
        P(("group", "shard")),
        P(("group", "shard"), None),
        P(("group", "shard")),
        P(("group", "shard"), None),
    )
    out_specs = (
        P(("group", "shard"), None),
        P(("group", "shard"), None),
        P("shard"),
        P("shard"),
        P("shard", None),
        P("shard"),
        P("shard"),
        P("shard"),
        P("shard"),
        P("shard", None),
        P("shard"),
        P("shard"),
        P("shard"),
        P("shard", None),
        P("shard"),
        P("shard"),
        P("shard"),
        P("shard", None),
        P("shard"),
    )

    return jax.shard_map(
        per_device, mesh=mesh, in_specs=in_specs, out_specs=out_specs, check_vma=False
    )
```

```python
import functools

import jax
import jax.numpy as jnp
from jax import lax
from jax.experimental import pallas as pl
from jax.experimental.pallas import tpu as pltpu
from jax.sharding import PartitionSpec as P


HEADS = 12
HEAD = 64
NSEG = 5


EPSILON = 1e-05


MASKED = -1000000000.0

CHUNK = 128
QBLOCK = 512


def _row_setup(segq_ref, i, tq):
    segq = segq_ref[...]
    own = jnp.broadcast_to(jnp.where(segq < NSEG - 1, segq, -1), (tq, CHUNK))
    rel = (i * tq + lax.broadcasted_iota(jnp.int32, (tq, CHUNK), 0)) - lax.broadcasted_iota(
        jnp.int32, (tq, CHUNK), 1
    )
    keep = (segq < NSEG - 1).astype(jnp.float32)
    return own, rel, keep


def _softmax_rows(q, kt_ref, own, rel, segk_ref, lo, hi, s_ref):
    tq = q.shape[0]

    def first(c, top):
        kc = kt_ref[0, :, pl.ds(c * CHUNK, CHUNK)]
        s = jnp.dot(q, kc, preferred_element_type=jnp.float32)
        allowed = (own == segk_ref[:, pl.ds(c * CHUNK, CHUNK)]) & (rel >= c * CHUNK)
        s = jnp.where(allowed, s, MASKED)
        s_ref[:, pl.ds(c * CHUNK, CHUNK)] = s
        return jnp.maximum(top, s)

    top = lax.fori_loop(lo, hi, first, jnp.full((tq, CHUNK), MASKED, jnp.float32))
    peak = jnp.broadcast_to(jnp.max(top, axis=1, keepdims=True), (tq, CHUNK))

    def second(c, acc):
        e = jnp.exp(s_ref[:, pl.ds(c * CHUNK, CHUNK)] - peak)
        s_ref[:, pl.ds(c * CHUNK, CHUNK)] = e
        return acc + e

    acc = lax.fori_loop(lo, hi, second, jnp.zeros((tq, CHUNK), jnp.float32))
    return jnp.sum(acc, axis=1, keepdims=True)


def _fwd_kernel(lo_ref, q_ref, kt_ref, v_ref, segq_ref, segk_ref, o_ref, s_ref):
    i = pl.program_id(1)
    tq = q_ref.shape[1]
    q = q_ref[0] * jnp.asarray(0.125, q_ref.dtype)
    own, rel, keep = _row_setup(segq_ref, i, tq)
    lo = lo_ref[i]
    hi = (i + 1) * (tq // CHUNK)
    total = _softmax_rows(q, kt_ref, own, rel, segk_ref, lo, hi, s_ref)
    scale = jnp.broadcast_to(keep / total, (tq, CHUNK))

    def third(c, acc):
        p = (s_ref[:, pl.ds(c * CHUNK, CHUNK)] * scale).astype(jnp.bfloat16)
        vc = v_ref[0, pl.ds(c * CHUNK, CHUNK), :]
        return acc + jnp.dot(p, vc, preferred_element_type=jnp.float32)

    o_ref[0] = lax.fori_loop(lo, hi, third, jnp.zeros((tq, q.shape[1]), jnp.float32))


def _bwd_kernel(lo_ref, q_ref, qt_ref, k_ref, kt_ref, vt_ref, do_ref, dot_ref, segq_ref, segk_ref,
                dq_ref, dkt_ref, dvt_ref, s_ref, dp_ref):
    i = pl.program_id(1)
    tq = q_ref.shape[1]

    @pl.when(i == 0)
    def _():
        dkt_ref[...] = jnp.zeros_like(dkt_ref)
        dvt_ref[...] = jnp.zeros_like(dvt_ref)

    eighth = jnp.asarray(0.125, q_ref.dtype)
    qs = q_ref[0] * eighth
    qts = qt_ref[0] * eighth
    do = do_ref[0]
    dot_ = dot_ref[0]
    own, rel, keep = _row_setup(segq_ref, i, tq)
    lo = lo_ref[i]
    hi = (i + 1) * (tq // CHUNK)
    total = _softmax_rows(qs, kt_ref, own, rel, segk_ref, lo, hi, s_ref)
    scale = jnp.broadcast_to(keep / total, (tq, CHUNK))

    def third(c, acc):
        p = s_ref[:, pl.ds(c * CHUNK, CHUNK)] * scale
        dp = jnp.dot(do, vt_ref[0, :, pl.ds(c * CHUNK, CHUNK)], preferred_element_type=jnp.float32)
        s_ref[:, pl.ds(c * CHUNK, CHUNK)] = p
        dp_ref[:, pl.ds(c * CHUNK, CHUNK)] = dp
        return acc + p * dp

    acc = lax.fori_loop(lo, hi, third, jnp.zeros((tq, CHUNK), jnp.float32))
    inner = jnp.broadcast_to(jnp.sum(acc, axis=1, keepdims=True), (tq, CHUNK))

    def fourth(c, dq):
        cols = pl.ds(c * CHUNK, CHUNK)
        p = s_ref[:, cols]
        ds = (p * (dp_ref[:, cols] - inner)).astype(jnp.bfloat16)
        dkt_ref[0, :, cols] += jnp.dot(qts, ds, preferred_element_type=jnp.float32)
        dvt_ref[0, :, cols] += jnp.dot(dot_, p.astype(jnp.bfloat16), preferred_element_type=jnp.float32)
        return dq + jnp.dot(ds, k_ref[0, cols, :], preferred_element_type=jnp.float32)

    dq = lax.fori_loop(lo, hi, fourth, jnp.zeros((tq, q_ref.shape[2]), jnp.float32))
    dq_ref[0] = dq * 0.125


def attention_forward(q, k, v, seg, lo):
    heads, length, head = q.shape
    tq = min(QBLOCK, length)
    rows = pl.BlockSpec((1, tq, head), lambda h, i, lo: (h, i, 0))
    whole = pl.BlockSpec((1, length, head), lambda h, i, lo: (h, 0, 0))
    wide = pl.BlockSpec((1, head, length), lambda h, i, lo: (h, 0, 0))
    segq = pl.BlockSpec((tq, 1), lambda h, i, lo: (i, 0))
    segk = pl.BlockSpec((1, length), lambda h, i, lo: (0, 0))
    return pl.pallas_call(
        _fwd_kernel,
        out_shape=jax.ShapeDtypeStruct((heads, length, head), jnp.float32),
        grid_spec=pltpu.PrefetchScalarGridSpec(
            num_scalar_prefetch=1,
            grid=(heads, length // tq),
            in_specs=[rows, wide, whole, segq, segk],
            out_specs=rows,
            scratch_shapes=[pltpu.VMEM((tq, length), jnp.float32)],
        ),
        compiler_params=pltpu.CompilerParams(dimension_semantics=("arbitrary", "arbitrary")),
        cost_estimate=pl.CostEstimate(
            flops=2 * heads * length * length * head,
            transcendentals=heads * length * length // 2,
            bytes_accessed=4 * heads * length * head * 2,
        ),
    )(lo, q, k.transpose(0, 2, 1), v, seg[:, None], seg[None, :])


def attention_backward(q, k, v, do, seg, lo):
    heads, length, head = q.shape
    tq = min(QBLOCK, length)
    rows = pl.BlockSpec((1, tq, head), lambda h, i, lo: (h, i, 0))
    rows_t = pl.BlockSpec((1, head, tq), lambda h, i, lo: (h, 0, i))
    whole = pl.BlockSpec((1, length, head), lambda h, i, lo: (h, 0, 0))
    wide = pl.BlockSpec((1, head, length), lambda h, i, lo: (h, 0, 0))
    segq = pl.BlockSpec((tq, 1), lambda h, i, lo: (i, 0))
    segk = pl.BlockSpec((1, length), lambda h, i, lo: (0, 0))
    dq, dkt, dvt = pl.pallas_call(
        _bwd_kernel,
        out_shape=(
            jax.ShapeDtypeStruct((heads, length, head), jnp.float32),
            jax.ShapeDtypeStruct((heads, head, length), jnp.float32),
            jax.ShapeDtypeStruct((heads, head, length), jnp.float32),
        ),
        grid_spec=pltpu.PrefetchScalarGridSpec(
            num_scalar_prefetch=1,
            grid=(heads, length // tq),
            in_specs=[rows, rows_t, whole, wide, wide, rows, rows_t, segq, segk],
            out_specs=(rows, wide, wide),
            scratch_shapes=[pltpu.VMEM((tq, length), jnp.float32), pltpu.VMEM((tq, length), jnp.float32)],
        ),
        compiler_params=pltpu.CompilerParams(dimension_semantics=("arbitrary", "arbitrary")),
        cost_estimate=pl.CostEstimate(
            flops=5 * heads * length * length * head,
            transcendentals=heads * length * length // 2,
            bytes_accessed=8 * heads * length * head * 2,
        ),
    )(lo, q, q.transpose(0, 2, 1), k, k.transpose(0, 2, 1), v.transpose(0, 2, 1), do, do.transpose(0, 2, 1), seg[:, None], seg[None, :])
    return dq, dkt.transpose(0, 2, 1), dvt.transpose(0, 2, 1)


def block_starts(seg, lengths, tq):
    ends = jnp.cumsum(lengths)
    starts = jnp.concatenate([jnp.zeros((1,), ends.dtype), ends[:-1]])
    first_seg = seg[::tq]
    return (starts[first_seg] // CHUNK).astype(jnp.int32)


def heads_major(block):
    return block.reshape(block.shape[0], HEADS, HEAD).transpose(1, 0, 2)


def tokens_major(block):
    return block.transpose(1, 0, 2).reshape(block.shape[1], HEADS * HEAD)


def norm_apply(values, gain, shift):
    average = jnp.mean(values, axis=-1, keepdims=True)
    centered = values - average
    inv_scale = lax.rsqrt(jnp.mean(centered * centered, axis=-1, keepdims=True) + EPSILON)
    unit = centered * inv_scale
    return (unit * gain + shift, unit, inv_scale)


def norm_back(unit, inv_scale, gain, grad):
    scaled = grad * gain
    back = inv_scale * (
        scaled
        - jnp.mean(scaled, axis=-1, keepdims=True)
        - unit * jnp.mean(scaled * unit, axis=-1, keepdims=True)
    )
    return (back, jnp.sum(grad * unit, axis=0), jnp.sum(grad, axis=0))


def gelu_exact(values):
    return jax.nn.gelu(values, approximate=False)


def segment_ids(lengths_row, length):
    ends = jnp.cumsum(lengths_row)
    places = jnp.arange(length, dtype=jnp.int32)
    return jnp.sum((places[:, None] >= ends[None, :]).astype(jnp.int32), axis=1)


def pack_columns(parts, rows):
    cols = [p.reshape(rows, -1) for p in parts]
    width = sum(c.shape[1] for c in cols)
    pad = (-width) % 128
    if pad:
        cols.append(jnp.zeros((rows, pad), cols[0].dtype))
    return jnp.concatenate(cols, axis=1)


def unpack_columns(block, widths):
    out = []
    offset = 0
    for w in widths:
        out.append(block[:, offset : offset + w].reshape(-1))
        offset += w
    return out


def grad_rows_reduce(packed, group_size, shard_size):
    rows, cols = packed.shape
    n = rows // (group_size * shard_size)
    permuted = (
        packed.reshape(shard_size, group_size, n, cols)
        .transpose(1, 0, 2, 3)
        .reshape(rows, cols)
    )
    return lax.psum_scatter(
        permuted, ("group", "shard"), scatter_dimension=0, tiled=True
    )


def hypercube_orders(group_size, shard_size):
    gbits = [("group", b) for b in range(group_size.bit_length() - 1)]
    sbits = [("shard", b) for b in range(shard_size.bit_length() - 1)]
    first = gbits[:-1] + sbits + gbits[-1:]
    second = list(first)
    if len(gbits) >= 3:
        second[1], second[2] = first[2], first[1]
    return first, second


def hypercube_reduce_scatter(x, order, group_size, shard_size):
    total = group_size * shard_size
    levels = total.bit_length() - 1
    rows, cols = x.shape
    n = rows // total
    sbits = shard_size.bit_length() - 1

    def k_bit(axis, b):
        return b if axis == "shard" else sbits + b

    axes = [levels - 1 - k_bit(axis, b) for axis, b in order]
    cur = (
        x.reshape([2] * levels + [n, cols])
        .transpose(axes + [levels, levels + 1])
        .reshape(rows, cols)
    )
    for axis, b in order:
        size = group_size if axis == "group" else shard_size
        half = cur.shape[0] // 2
        mine = (lax.axis_index(axis) >> b) & 1
        low, high = cur[:half], cur[half:]
        keep = jnp.where(mine == 1, high, low)
        send = jnp.where(mine == 1, low, high).astype(jnp.bfloat16)
        got = lax.ppermute(send, axis, [(j, j ^ (1 << b)) for j in range(size)])
        cur = keep + got.astype(jnp.float32)
    return cur


def hypercube_all_gather(x, order, group_size, shard_size):
    total = group_size * shard_size
    levels = total.bit_length() - 1
    n, cols = x.shape
    sbits = shard_size.bit_length() - 1
    cur = x
    for axis, b in order:
        size = group_size if axis == "group" else shard_size
        got = lax.ppermute(cur, axis, [(j, j ^ (1 << b)) for j in range(size)])
        mine = (lax.axis_index(axis) >> b) & 1
        low = jnp.where(mine == 1, got, cur)
        high = jnp.where(mine == 1, cur, got)
        cur = jnp.concatenate([low, high], axis=0)
    kbits = [b if axis == "shard" else sbits + b for axis, b in order]
    perm = [levels - 1 - kbits.index(levels - 1 - a) for a in range(levels)]
    return (
        cur.reshape([2] * levels + [n, cols])
        .transpose(perm + [levels, levels + 1])
        .reshape(total * n, cols)
    )


def per_device(
    tokens,
    doc_lengths,
    first_gain,
    first_shift,
    qkv_weight,
    query_bias,
    value_bias,
    inner_gain,
    inner_shift,
    proj_weight,
    proj_bias,
    second_gain,
    second_shift,
    expand_weight,
    expand_bias,
    hidden_gain,
    hidden_shift,
    shrink_weight,
    shrink_bias,
    out_cotangent,
):
    group_size = lax.axis_size("group")
    shard_size = lax.axis_size("shard")
    n = qkv_weight.shape[0]
    model_width = n * group_size * shard_size
    wide_width = expand_weight.shape[1]
    ratio = wide_width // model_width
    qkv_width = qkv_weight.shape[1]

    small_parts = (
        first_gain,
        first_shift,
        query_bias,
        value_bias,
        inner_gain,
        inner_shift,
        proj_bias,
        second_gain,
        second_shift,
        shrink_bias,
        expand_bias,
        hidden_gain,
        hidden_shift,
    )
    small_widths = [p.shape[0] // n for p in small_parts]
    first_pack = jnp.concatenate([qkv_weight, pack_columns(small_parts, n)], axis=1)
    gather_a, gather_b = hypercube_orders(group_size, shard_size)
    cut = (first_pack.shape[1] // 256) * 128
    first_full = jnp.concatenate(
        [
            hypercube_all_gather(
                first_pack[:, :cut], gather_a[::-1], group_size, shard_size
            ),
            hypercube_all_gather(
                first_pack[:, cut:],
                gather_b[::-1][1:2] + gather_b[::-1][:1] + gather_b[::-1][2:],
                group_size,
                shard_size,
            ),
        ],
        axis=1,
    )
    qkv_full = first_full[:, :qkv_width]
    (
        gain_one,
        shift_one,
        qbias_full,
        vbias_full,
        gain_inner,
        shift_inner,
        pbias_full,
        gain_three,
        shift_three,
        sbias_full,
        ebias_full,
        gain_four,
        shift_four,
    ) = unpack_columns(first_full[:, qkv_width:], small_widths)
    second_pack = jnp.concatenate([proj_weight, expand_weight], axis=1)
    second_full = lax.all_gather(second_pack, ("group", "shard"), axis=0, tiled=True)
    proj_full = second_full[:, :model_width]
    expand_full = second_full[:, model_width:]
    shrink_full = lax.all_gather(shrink_weight, ("group", "shard"), axis=0, tiled=True)

    row_count = doc_lengths.shape[0]
    length = tokens.shape[0] // row_count
    inputs = tokens.astype(jnp.float32)
    normed, unit_one, inv_one = norm_apply(
        inputs, gain_one.astype(jnp.float32), shift_one.astype(jnp.float32)
    )
    normed_low = normed.astype(jnp.bfloat16)
    bias_cat = jnp.concatenate([qbias_full, jnp.zeros_like(qbias_full), vbias_full]).astype(
        jnp.float32
    )
    qkv_low = (jnp.dot(normed_low, qkv_full, preferred_element_type=jnp.float32) + bias_cat).astype(
        jnp.bfloat16
    )
    segments = jax.vmap(functools.partial(segment_ids, length=length))(doc_lengths).astype(
        jnp.int32
    )
    tq = min(QBLOCK, length)
    row_heads = []
    row_starts = []
    attended_rows = []
    for r in range(row_count):
        piece = qkv_low[r * length : (r + 1) * length]
        heads = tuple(
            heads_major(piece[:, j * model_width : (j + 1) * model_width]) for j in range(3)
        )
        lo = block_starts(segments[r], doc_lengths[r], tq)
        row_heads.append(heads)
        row_starts.append(lo)
        attended_rows.append(tokens_major(attention_forward(*heads, segments[r], lo)))
    attended = jnp.concatenate(attended_rows, axis=0)
    inner, unit_two, inv_two = norm_apply(
        attended, gain_inner.astype(jnp.float32), shift_inner.astype(jnp.float32)
    )
    inner_low = inner.astype(jnp.bfloat16)
    middle = (
        inputs
        + jnp.dot(inner_low, proj_full, preferred_element_type=jnp.float32)
        + pbias_full.astype(jnp.float32)
    )
    second, unit_three, inv_three = norm_apply(
        middle, gain_three.astype(jnp.float32), shift_three.astype(jnp.float32)
    )
    second_low = second.astype(jnp.bfloat16)
    pre_act = jnp.dot(
        second_low, expand_full, preferred_element_type=jnp.float32
    ) + ebias_full.astype(jnp.float32)
    activ, gelu_pull = jax.vjp(gelu_exact, pre_act)
    hidden, unit_four, inv_four = norm_apply(
        activ, gain_four.astype(jnp.float32), shift_four.astype(jnp.float32)
    )
    hidden_low = hidden.astype(jnp.bfloat16)
    output = (
        middle
        + jnp.dot(hidden_low, shrink_full, preferred_element_type=jnp.float32)
        + sbias_full.astype(jnp.float32)
    )
    block_output = output.astype(jnp.bfloat16)
    grad_out = out_cotangent.astype(jnp.float32)
    shrink_weight_grad = jnp.einsum(
        "tf,td->fd", hidden_low, out_cotangent, preferred_element_type=jnp.float32
    )
    shrink_bias_grad = jnp.sum(grad_out, axis=0)
    grad_hidden = jnp.einsum(
        "td,fd->tf", out_cotangent, shrink_full, preferred_element_type=jnp.float32
    )
    grad_activ, hidden_gain_grad, hidden_shift_grad = norm_back(
        unit_four, inv_four, gain_four.astype(jnp.float32), grad_hidden
    )
    grad_pre = gelu_pull(grad_activ)[0].astype(jnp.bfloat16)
    expand_bias_grad = jnp.sum(grad_pre.astype(jnp.float32), axis=0)
    expand_weight_grad = jnp.einsum(
        "td,tf->df", second_low, grad_pre, preferred_element_type=jnp.float32
    )
    grad_second = jnp.einsum("tf,df->td", grad_pre, expand_full, preferred_element_type=jnp.float32)
    grad_mid_part, second_gain_grad, second_shift_grad = norm_back(
        unit_three, inv_three, gain_three.astype(jnp.float32), grad_second
    )
    grad_middle = grad_out + grad_mid_part
    order_a, order_b = hypercube_orders(group_size, shard_size)
    grad_branch = grad_middle.astype(jnp.bfloat16)
    proj_bias_grad = jnp.sum(grad_branch.astype(jnp.float32), axis=0)
    proj_weight_grad = jnp.einsum(
        "td,te->de", inner_low, grad_branch, preferred_element_type=jnp.float32
    )
    grad_inner = jnp.einsum("te,de->td", grad_branch, proj_full, preferred_element_type=jnp.float32)
    grad_attended, inner_gain_grad, inner_shift_grad = norm_back(
        unit_two, inv_two, gain_inner.astype(jnp.float32), grad_inner
    )
    ffn_small = (
        second_gain_grad,
        second_shift_grad,
        shrink_bias_grad,
        expand_bias_grad,
        hidden_gain_grad,
        hidden_shift_grad,
        inner_gain_grad,
        inner_shift_grad,
        proj_bias_grad,
    )
    ffn_small_widths = [p.shape[0] // model_width for p in ffn_small]
    ffn_pack = jnp.concatenate(
        [
            expand_weight_grad,
            shrink_weight_grad.reshape(model_width, ratio * model_width),
            proj_weight_grad,
            pack_columns(ffn_small, model_width),
        ],
        axis=1,
    ).astype(jnp.bfloat16)
    grad_att_low = grad_attended.astype(jnp.bfloat16)
    ffn_pack, grad_att_low = lax.optimization_barrier((ffn_pack, grad_att_low))
    ffn_part = grad_rows_reduce(ffn_pack, group_size, shard_size)
    grad_rows = []
    for r in range(row_count):
        parts = attention_backward(
            *row_heads[r],
            heads_major(grad_att_low[r * length : (r + 1) * length]),
            segments[r],
            row_starts[r],
        )
        grad_rows.append(jnp.concatenate([tokens_major(p) for p in parts], axis=1))
    grad_qkv = jnp.concatenate(grad_rows, axis=0).astype(jnp.bfloat16)
    grad_qkv_wide = grad_qkv.astype(jnp.float32)
    query_bias_grad = jnp.sum(grad_qkv_wide[:, :model_width], axis=0)
    value_bias_grad = jnp.sum(grad_qkv_wide[:, 2 * model_width :], axis=0)
    qkv_weight_grad = jnp.einsum(
        "td,te->de", normed_low, grad_qkv, preferred_element_type=jnp.float32
    )
    grad_normed = jnp.einsum("te,de->td", grad_qkv, qkv_full, preferred_element_type=jnp.float32)
    grad_in_part, first_gain_grad, first_shift_grad = norm_back(
        unit_one, inv_one, gain_one.astype(jnp.float32), grad_normed
    )
    input_grad = (grad_middle + grad_in_part).astype(jnp.bfloat16)
    attn_small = (
        first_gain_grad,
        first_shift_grad,
        query_bias_grad,
        value_bias_grad,
    )
    attn_pack = jnp.concatenate(
        [qkv_weight_grad, pack_columns(attn_small, model_width)], axis=1
    )
    attn_pack = (
        attn_pack.reshape(shard_size, group_size, n, -1)
        .transpose(1, 0, 2, 3)
        .reshape(model_width, -1)
    )
    ffn_part, attn_pack = lax.optimization_barrier((ffn_part, attn_pack))
    split = (attn_pack.shape[1] // 256) * 128
    attn_left = hypercube_reduce_scatter(
        attn_pack[:, :split], order_a, group_size, shard_size
    )
    attn_right = hypercube_reduce_scatter(
        attn_pack[:, split:], order_b, group_size, shard_size
    )
    both = lax.all_gather(
        jnp.concatenate(
            [
                ffn_part,
                attn_left.astype(jnp.bfloat16),
                attn_right.astype(jnp.bfloat16),
            ],
            axis=1,
        ),
        "group",
        axis=0,
        tiled=True,
    )
    ffn_cols = ffn_pack.shape[1]
    ffn_back = both[:, :ffn_cols]
    attn_back = both[:, ffn_cols:]
    half = both.shape[0]
    expand_out = ffn_back[:, :wide_width].astype(jnp.float32)
    shrink_out = (
        ffn_back[:, wide_width : 2 * wide_width]
        .reshape(half * ratio, model_width)
        .astype(jnp.float32)
    )
    proj_out = ffn_back[:, 2 * wide_width : 2 * wide_width + model_width].astype(jnp.float32)
    (
        second_gain_out,
        second_shift_out,
        sbias_out,
        ebias_out,
        gain_four_out,
        shift_four_out,
        gain_inner_out,
        shift_inner_out,
        pbias_out,
    ) = unpack_columns(
        ffn_back[:, 2 * wide_width + model_width :].astype(jnp.float32), ffn_small_widths
    )
    qkv_out = attn_back[:, :qkv_width].astype(jnp.float32)
    (
        gain_one_out,
        shift_one_out,
        qbias_out,
        vbias_out,
    ) = unpack_columns(attn_back[:, qkv_width:].astype(jnp.float32), [1] * 4)
    return (
        block_output,
        input_grad,
        gain_one_out,
        shift_one_out,
        qkv_out,
        qbias_out,
        vbias_out,
        gain_inner_out,
        shift_inner_out,
        proj_out,
        pbias_out,
        second_gain_out,
        second_shift_out,
        expand_out,
        ebias_out,
        gain_four_out,
        shift_four_out,
        shrink_out,
        sbias_out,
    )


def solution(mesh):
    in_specs = (
        P(("group", "shard"), None),
        P(("group", "shard"), None),
        P(("group", "shard")),
        P(("group", "shard")),
        P(("group", "shard"), None),
        P(("group", "shard")),
        P(("group", "shard")),
        P(("group", "shard")),
        P(("group", "shard")),
        P(("group", "shard"), None),
        P(("group", "shard")),
        P(("group", "shard")),
        P(("group", "shard")),
        P(("group", "shard"), None),
        P(("group", "shard")),
        P(("group", "shard")),
        P(("group", "shard")),
        P(("group", "shard"), None),
        P(("group", "shard")),
        P(("group", "shard"), None),
    )
    out_specs = (
        P(("group", "shard"), None),
        P(("group", "shard"), None),
        P("shard"),
        P("shard"),
        P("shard", None),
        P("shard"),
        P("shard"),
        P("shard"),
        P("shard"),
        P("shard", None),
        P("shard"),
        P("shard"),
        P("shard"),
        P("shard", None),
        P("shard"),
        P("shard"),
        P("shard"),
        P("shard", None),
        P("shard"),
    )

    return jax.shard_map(
        per_device, mesh=mesh, in_specs=in_specs, out_specs=out_specs, check_vma=False
    )
```
